32 devices in a mesh: stn: 16 (over z, x, core), chan: 2 (over y).
Axes of the slice: x: 2, y: 2, z: 4, core: 2. Of those that a mesh axis runs over, the one named last changes fastest.
Arguments:
- screen: float32 [32, 512, 512], P('stn'), may hold values from -6 to 6
- pierce_coords: float32 [2, 16, 2, 16, 1024], P(None, 'stn', 'chan'), may hold values from 0 to 1
- query_dest: int32 [16, 2, 16, 1024], P('stn', 'chan'), may hold values from 0 to 4096, as said below
- positions: float32 [3, 256], P(None, 'stn'), may hold values from -50 to 50
- directions: float32 [3, 512], replicated, may hold values from -0.7 to 0.7
- freq_ratio: float32 [64], P('chan'), may hold values from 0.7 to 1.4
- source_flux: float32 [512], replicated, may hold values from 0.2 to 5
- spectral_index: float32 [512], replicated, may hold values from -1.5 to 0.5
Outputs:
- visibilities: float32 [64, 2, 256, 256], P('chan', None, 'stn')
The draws below stay inside these ranges and needn't reach their ends.
Inputs may be any that keep to these rules, and one draw needn't show every extreme that they name: `query_dest`: in each block every number 0 to 4095 appears in exactly one slot and empty slots hold 4096; an owner's live slots come first in its row; one owner, the same for every block, has all 1024 of its slots live in every block.
All inputs are finite; a program needn't handle non-finite values.
Results may differ from the reference program's by a relative error of at most 0.008.
Values may be sent and summed in bfloat16 or wider, within the bound.
No kernel may reach another device: no remote copies, remote signals or barrier semaphores. Data moves between devices by JAX's collectives and lax.ppermute only.
A program may use at most 128 MiB of HBM per device.

```python
import math
import jax
import jax.numpy as jnp
from jax import lax

STN_DEV = 16
SRC = 512
TILE = 512
TILES_DEV = 2
STATIONS = 256
CHANNELS = 64
TILES = 32
SRCC = 256
QUERIES = 4096
CAP = 1024
N_STN = 16
N_CHAN = 2


def draw_screen(key, part):
    rough = jax.random.normal(jax.random.fold_in(key, 3), (TILES, TILE, TILE), jnp.float32)
    field = 1.5 * rough
    return jnp.clip(field, -6.0, 6.0)


def draw_query_dest(key, part):
    key_order, key_share, key_rank, key_query = jax.random.split(jax.random.fold_in(key, 7), 4)
    blocks = N_STN * N_CHAN
    hot_order = jax.random.permutation(key_order, N_STN).astype(jnp.int32)
    shares = jax.random.randint(key_share, (blocks, N_STN - 1), 1, 4).astype(jnp.int32)
    remain = QUERIES - CAP
    counts = remain * shares // jnp.sum(shares, axis=1, keepdims=True)
    leftover = remain - jnp.sum(counts, axis=1, keepdims=True)
    ranks = jnp.arange(N_STN - 1, dtype=jnp.int32)[None, :]
    counts = counts + (ranks < leftover).astype(jnp.int32)
    counts = jnp.concatenate([jnp.full((blocks, 1), CAP, jnp.int32), counts], axis=1)
    others = jax.vmap(lambda single: jax.random.permutation(single, N_STN - 1))(jax.random.split(key_rank, blocks))
    rank_slot = jnp.concatenate([jnp.zeros((blocks, 1), jnp.int32), others.astype(jnp.int32) + 1], axis=1)
    owner_of = hot_order[rank_slot]
    matches = (owner_of[:, :, None] == jnp.arange(N_STN, dtype=jnp.int32)[None, None, :]).astype(jnp.int32)
    per_owner = jnp.sum(counts[:, :, None] * matches, axis=1)
    starts = jnp.cumsum(per_owner, axis=1) - per_owner
    ordering = jax.vmap(lambda single: jax.random.permutation(single, QUERIES))(jax.random.split(key_query, blocks))
    padded = jnp.concatenate([ordering.astype(jnp.int32), jnp.full((blocks, 1), QUERIES, jnp.int32)], axis=1)
    slots = jnp.arange(CAP, dtype=jnp.int32)[None, None, :]
    live = slots < per_owner[:, :, None]
    positions_in = jnp.where(live, starts[:, :, None] + slots, QUERIES)
    picked = padded[jnp.arange(blocks, dtype=jnp.int32)[:, None, None], positions_in]
    return picked.reshape(N_STN, N_CHAN, N_STN, CAP)


def shard_levels(key, dims, pieces, smallest, high):
    def one(dim, blocks):
        draws = jax.random.uniform(jax.random.fold_in(jax.random.fold_in(key, 6), dim), (blocks,), jnp.float32, smallest / len(pieces), high / len(pieces))
        return jnp.repeat(jnp.exp(draws), dims[dim] // blocks).reshape((-1,) + (1,) * (len(dims) - dim - 1))

    level = one(*pieces[0])
    for cut in pieces[1:]:
        level = level * one(*cut)
    return level


def setup_inputs(seed: int = 0) -> dict:
    splits = jax.random.split(jax.random.key(seed), 9)
    return {
        "screen": draw_screen(jax.random.fold_in(splits[8], 71), 0),
        "pierce_coords": jnp.clip(1.0 * jax.random.uniform(splits[1], (2, N_STN, N_CHAN, N_STN, CAP), jnp.float32) ** shard_levels(splits[1], (2, N_STN, N_CHAN, N_STN, CAP), ((1, 16), (2, 2)), -0.2, 0.2), 0.0, 1.0),
        "query_dest": draw_query_dest(jax.random.fold_in(splits[8], 71), 0),
        "positions": jnp.clip(jax.random.uniform(splits[3], (3, STATIONS), jnp.float32, -50.0, 50.0) * shard_levels(splits[3], (3, STATIONS), ((1, 16),), -0.4, 0.0), -50.0, 50.0),
        "directions": jnp.clip(jax.random.uniform(splits[4], (3, SRC), jnp.float32, -0.7, 0.7), -0.7, 0.7),
        "freq_ratio": jnp.clip(jnp.exp(math.log(1.4) - 0.6931472 * jax.random.uniform(splits[5], (CHANNELS,), jnp.float32) ** shard_levels(splits[5], (CHANNELS,), ((0, 2),), -0.2, 0.2)), 0.7, 1.4),
        "source_flux": jnp.clip(jnp.exp(jax.random.uniform(splits[6], (SRC,), jnp.float32, math.log(0.2), math.log(5.0))), 0.2, 5.0),
        "spectral_index": jnp.clip(jax.random.uniform(splits[7], (SRC,), jnp.float32, -1.5, 0.5), -1.5, 0.5),
    }


TWO_PI = 2.0 * math.pi

def interpolate(values, coords, strip_rows, tile_cols, offsets):
    row_pos = coords[0] * (strip_rows - 1)
    col_pos = coords[1] * (tile_cols - 1)
    row_low = jnp.clip(jnp.floor(row_pos), 0.0, strip_rows - 2.0)
    col_low = jnp.clip(jnp.floor(col_pos), 0.0, tile_cols - 2.0)
    frac_y = row_pos - row_low
    frac_x = col_pos - col_low
    corner = offsets + row_low.astype(jnp.int32) * tile_cols + col_low.astype(jnp.int32)
    lower_pair = (1.0 - frac_x) * values[corner] + frac_x * values[corner + 1]
    upper_pair = (1.0 - frac_x) * values[corner + tile_cols] + frac_x * values[corner + tile_cols + 1]
    return (1.0 - frac_y) * lower_pair + frac_y * upper_pair

def make_phasors(station_rows, iono_rows, directions, freq_ratio):
    delays = station_rows[:, 0:1] * directions[0][None, :] + station_rows[:, 1:2] * directions[1][None, :]
    delays = delays + station_rows[:, 2:3] * directions[2][None, :]
    angles = (TWO_PI * freq_ratio)[None, :, None] * delays[:, None, :] + iono_rows[:, None, :] / freq_ratio[None, :, None]
    return jnp.concatenate([jnp.cos(angles), jnp.sin(angles)], axis=-1).astype(jnp.bfloat16)

def spectrum(source_flux, spectral_index, freq_ratio, count):
    return source_flux[None, :] * jnp.exp(spectral_index[None, :] * jnp.log(freq_ratio)[:, None]) / math.sqrt(count)

def weight_rows(phasors, intensity):
    sources = intensity.shape[1]
    real_part = (phasors[:, :, :sources].astype(jnp.float32) * intensity[None]).astype(jnp.bfloat16)
    imag_part = (phasors[:, :, sources:].astype(jnp.float32) * intensity[None]).astype(jnp.bfloat16)
    upper_rows = jnp.concatenate([real_part, imag_part], axis=-1)
    lower_rows = jnp.concatenate([imag_part, -real_part], axis=-1)
    return jnp.concatenate([upper_rows, lower_rows], axis=0)

def reference(screen, pierce_coords, query_dest, positions, directions, freq_ratio, source_flux, spectral_index):
    strip_rows = TILES_DEV * TILE
    values = screen.reshape(-1)
    owners = jnp.arange(N_STN, dtype=jnp.int32)[None, None, :, None] * (strip_rows * TILE)
    sampled = interpolate(values, pierce_coords, strip_rows, TILE, owners)
    blocks = N_STN * N_CHAN
    block_ids = jnp.broadcast_to(jnp.arange(blocks, dtype=jnp.int32).reshape(N_STN, N_CHAN, 1, 1), query_dest.shape)
    buffer = jnp.zeros((blocks, QUERIES + 1), jnp.float32).at[block_ids, query_dest].set(sampled.astype(jnp.float32))
    iono_phase = buffer[:, :QUERIES].reshape(N_STN, N_CHAN, STN_DEV, SRCC).transpose(0, 2, 1, 3).reshape(STATIONS, SRC)
    phasors = make_phasors(positions.T, iono_phase, directions, freq_ratio)
    intensity = spectrum(source_flux, spectral_index, freq_ratio, SRC)
    weighted = weight_rows(phasors, intensity)

    def per_channel(operands):
        return jnp.dot(operands[0], operands[1].T, preferred_element_type=jnp.float32)
    result = lax.map(per_channel, (weighted.transpose(1, 0, 2), phasors.transpose(1, 0, 2)))
    visible = result.reshape(CHANNELS, 2, STATIONS, STATIONS)
    cross_only = jnp.arange(STATIONS)[:, None] != jnp.arange(STATIONS)[None, :]
    return jnp.where(cross_only[None, None], visible, jnp.zeros_like(visible))
```

```python
import math

import jax
import jax.numpy as jnp
from jax import lax
from jax.experimental import pallas as pl
from jax.experimental.pallas import tpu as pltpu
from jax.sharding import PartitionSpec as P

TWO_PI = 2.0 * math.pi


def interpolate(values, coords, strip_rows, tile_cols):
    row_pos = coords[0] * (strip_rows - 1)
    col_pos = coords[1] * (tile_cols - 1)
    row_low = jnp.clip(jnp.floor(row_pos), 0.0, strip_rows - 2.0)
    col_low = jnp.clip(jnp.floor(col_pos), 0.0, tile_cols - 2.0)
    frac_y = row_pos - row_low
    frac_x = col_pos - col_low
    corner = row_low.astype(jnp.int32) * tile_cols + col_low.astype(jnp.int32)
    lower_pair = (1.0 - frac_x) * values[corner] + frac_x * values[corner + 1]
    upper_pair = (1.0 - frac_x) * values[corner + tile_cols] + frac_x * values[
        corner + tile_cols + 1
    ]
    return (1.0 - frac_y) * lower_pair + frac_y * upper_pair


UNROLL = 16


def _interp_kernel(r_ref, c_ref, s_ref, o_ref):
    rows = s_ref.shape[0]
    two_nb = s_ref.shape[1]
    nb = two_nb // 2
    cols = nb * 128
    chunk = o_ref.shape[0]
    base = pl.program_id(0) * chunk
    sub = lax.broadcasted_iota(jnp.int32, (two_nb, 128), 0)
    lane = lax.broadcasted_iota(jnp.int32, (two_nb, 128), 1)
    col = ((sub % nb) * 128 + lane).astype(jnp.float32)
    upper = sub >= nb
    rowid = lax.broadcasted_iota(jnp.int32, (8, 128), 0)

    def group(g, carry):
        for h in range(UNROLL // 8):
            acc = jnp.zeros((8, 128), jnp.float32)
            for u in range(8):
                j = base + g * UNROLL + h * 8 + u
                t = s_ref[r_ref[j]]
                y = jnp.full((two_nb, 128), c_ref[0, j], jnp.float32) * (rows - 1)
                x = jnp.full((two_nb, 128), c_ref[1, j], jnp.float32) * (cols - 1)
                ry = jnp.clip(jnp.floor(y), 0.0, rows - 2.0)
                kx = jnp.clip(jnp.floor(x), 0.0, cols - 2.0)
                fy = y - ry
                fx = x - kx
                wy = jnp.where(upper, fy, 1.0 - fy)
                wx = jnp.where(col == kx, 1.0 - fx, jnp.where(col == kx + 1.0, fx, 0.0))
                row = jnp.sum(t * (wy * wx), axis=0, keepdims=True)
                acc = jnp.where(rowid == u, row, acc)
            start = pl.multiple_of(g * UNROLL + h * 8, 8)
            o_ref[pl.ds(start, 8), :] = jnp.sum(acc, axis=1, keepdims=True)
        return carry

    lax.fori_loop(0, chunk // UNROLL, group, 0)


def interpolate_kernel(screen2d, coords):
    rows, cols = screen2d.shape
    nb = cols // 128
    q = coords.shape[1]
    chunk = min(2048, q)
    r = jnp.clip(jnp.floor(coords[0] * (rows - 1)), 0.0, rows - 2.0).astype(jnp.int32)
    pair = jnp.concatenate([screen2d, jnp.roll(screen2d, -1, axis=0)], axis=1)
    pair = pair.reshape(rows, 2 * nb, 128)
    out = pl.pallas_call(
        _interp_kernel,
        grid_spec=pltpu.PrefetchScalarGridSpec(
            num_scalar_prefetch=2,
            grid=(q // chunk,),
            in_specs=[pl.BlockSpec((rows, 2 * nb, 128), lambda i, rr, cc: (0, 0, 0))],
            out_specs=pl.BlockSpec((chunk, 1), lambda i, rr, cc: (i, 0)),
        ),
        out_shape=jax.ShapeDtypeStruct((q, 1), jnp.float32),
    )(r, coords, pair)
    return out[:, 0]


def make_phasors(station_rows, iono_rows, directions, freq_ratio):
    delays = (
        station_rows[:, 0:1] * directions[0][None, :]
        + station_rows[:, 1:2] * directions[1][None, :]
    )
    delays = delays + station_rows[:, 2:3] * directions[2][None, :]
    angles = (TWO_PI * freq_ratio)[None, :, None] * delays[:, None, :] + iono_rows[
        :, None, :
    ] / freq_ratio[None, :, None]
    return jnp.concatenate([jnp.cos(angles), jnp.sin(angles)], axis=-1).astype(jnp.bfloat16)


def spectrum(source_flux, spectral_index, freq_ratio, count):
    return (
        source_flux[None, :]
        * jnp.exp(spectral_index[None, :] * jnp.log(freq_ratio)[:, None])
        / math.sqrt(count)
    )


def weight_rows(phasors, intensity):
    sources = intensity.shape[1]
    real_part = (phasors[:, :, :sources].astype(jnp.float32) * intensity[None]).astype(jnp.bfloat16)
    imag_part = (phasors[:, :, sources:].astype(jnp.float32) * intensity[None]).astype(jnp.bfloat16)
    upper_rows = jnp.concatenate([real_part, imag_part], axis=-1)
    lower_rows = jnp.concatenate([imag_part, -real_part], axis=-1)
    return jnp.concatenate([upper_rows, lower_rows], axis=0)


def body(
    screen,
    pierce_coords,
    query_dest,
    positions,
    directions,
    freq_ratio,
    source_flux,
    spectral_index,
):
    groups = lax.axis_size("stn")
    tile_cols = screen.shape[2]
    strip_rows = screen.shape[0] * screen.shape[1]
    values = screen.reshape(-1)
    capacity = query_dest.shape[3]
    coords = pierce_coords.reshape(2, groups, capacity)
    received = lax.all_to_all(coords, "stn", split_axis=1, concat_axis=1, tiled=True)
    sampled = interpolate_kernel(
        values.reshape(strip_rows, tile_cols), received.reshape(2, groups * capacity)
    ).reshape(groups, capacity)
    returned = lax.all_to_all(sampled, "stn", split_axis=0, concat_axis=0, tiled=True)
    stations_local = positions.shape[1]
    local_sources = source_flux.shape[0] // lax.axis_size("chan")
    queries = stations_local * local_sources
    buffer = (
        jnp.zeros((queries + 1,), jnp.float32).at[query_dest.reshape(-1)].set(returned.reshape(-1))
    )
    own_iono = buffer[:queries].reshape(stations_local, local_sources)
    iono_phase = lax.all_gather(own_iono, "chan", axis=1, tiled=True)
    station_rows = positions.T
    own_phasors = make_phasors(station_rows, iono_phase, directions, freq_ratio)
    intensity = spectrum(source_flux, spectral_index, freq_ratio, source_flux.shape[0])
    weighted = weight_rows(own_phasors, intensity)
    total_stations = stations_local * groups
    channels = freq_ratio.shape[0]
    columns = jnp.einsum(
        "ack,nck->can",
        weighted,
        make_phasors(
            lax.all_gather(station_rows, "stn", axis=0, tiled=True),
            lax.all_gather(iono_phase, "stn", axis=0, tiled=True),
            directions,
            freq_ratio,
        ),
        preferred_element_type=jnp.float32,
    )
    visible = columns.reshape(channels, 2, stations_local, total_stations)
    first_row = lax.axis_index("stn") * stations_local
    rows_global = first_row + jnp.arange(stations_local, dtype=jnp.int32)
    cross_only = rows_global[:, None] != jnp.arange(total_stations, dtype=jnp.int32)[None, :]
    return jnp.where(cross_only[None, None], visible, jnp.zeros_like(visible))


def solution(mesh):
    in_specs = (
        P("stn", None, None),
        P(None, "stn", "chan", None, None),
        P("stn", "chan", None, None),
        P(None, "stn"),
        P(),
        P("chan"),
        P(),
        P(),
    )
    out_specs = P("chan", None, "stn", None)
    return jax.shard_map(body, mesh=mesh, in_specs=in_specs, out_specs=out_specs, check_vma=False)
```

```python
import math

import jax
import jax.numpy as jnp
from jax import lax
from jax.experimental import pallas as pl
from jax.experimental.pallas import tpu as pltpu
from jax.sharding import PartitionSpec as P

TWO_PI = 2.0 * math.pi


def interpolate(values, coords, strip_rows, tile_cols):
    row_pos = coords[0] * (strip_rows - 1)
    col_pos = coords[1] * (tile_cols - 1)
    row_low = jnp.clip(jnp.floor(row_pos), 0.0, strip_rows - 2.0)
    col_low = jnp.clip(jnp.floor(col_pos), 0.0, tile_cols - 2.0)
    frac_y = row_pos - row_low
    frac_x = col_pos - col_low
    corner = row_low.astype(jnp.int32) * tile_cols + col_low.astype(jnp.int32)
    lower_pair = (1.0 - frac_x) * values[corner] + frac_x * values[corner + 1]
    upper_pair = (1.0 - frac_x) * values[corner + tile_cols] + frac_x * values[
        corner + tile_cols + 1
    ]
    return (1.0 - frac_y) * lower_pair + frac_y * upper_pair


UNROLL = 16


def _interp_kernel(r_ref, c_ref, s_ref, o_ref):
    rows = s_ref.shape[0]
    two_nb = s_ref.shape[1]
    nb = two_nb // 2
    cols = nb * 128
    chunk = o_ref.shape[0]
    base = pl.program_id(0) * chunk
    sub = lax.broadcasted_iota(jnp.int32, (two_nb, 128), 0)
    lane = lax.broadcasted_iota(jnp.int32, (two_nb, 128), 1)
    col = ((sub % nb) * 128 + lane).astype(jnp.float32)
    upper = sub >= nb
    rowid = lax.broadcasted_iota(jnp.int32, (8, 128), 0)

    def group(g, carry):
        for h in range(UNROLL // 8):
            acc = jnp.zeros((8, 128), jnp.float32)
            for u in range(8):
                j = base + g * UNROLL + h * 8 + u
                t = s_ref[r_ref[j]]
                y = jnp.full((two_nb, 128), c_ref[0, j], jnp.float32) * (rows - 1)
                x = jnp.full((two_nb, 128), c_ref[1, j], jnp.float32) * (cols - 1)
                ry = jnp.clip(jnp.floor(y), 0.0, rows - 2.0)
                kx = jnp.clip(jnp.floor(x), 0.0, cols - 2.0)
                fy = y - ry
                fx = x - kx
                wy = jnp.where(upper, fy, 1.0 - fy)
                wx = jnp.where(col == kx, 1.0 - fx, jnp.where(col == kx + 1.0, fx, 0.0))
                row = jnp.sum(t * (wy * wx), axis=0, keepdims=True)
                acc = jnp.where(rowid == u, row, acc)
            start = pl.multiple_of(g * UNROLL + h * 8, 8)
            o_ref[pl.ds(start, 8), :] = jnp.sum(acc, axis=1, keepdims=True)
        return carry

    lax.fori_loop(0, chunk // UNROLL, group, 0)


def interpolate_kernel(screen2d, coords):
    rows, cols = screen2d.shape
    nb = cols // 128
    q = coords.shape[1]
    chunk = min(2048, q)
    r = jnp.clip(jnp.floor(coords[0] * (rows - 1)), 0.0, rows - 2.0).astype(jnp.int32)
    pair = jnp.concatenate([screen2d, jnp.roll(screen2d, -1, axis=0)], axis=1)
    pair = pair.reshape(rows, 2 * nb, 128)
    out = pl.pallas_call(
        _interp_kernel,
        grid_spec=pltpu.PrefetchScalarGridSpec(
            num_scalar_prefetch=2,
            grid=(q // chunk,),
            in_specs=[pl.BlockSpec((rows, 2 * nb, 128), lambda i, rr, cc: (0, 0, 0))],
            out_specs=pl.BlockSpec((chunk, 1), lambda i, rr, cc: (i, 0)),
        ),
        out_shape=jax.ShapeDtypeStruct((q, 1), jnp.float32),
    )(r, coords, pair)
    return out[:, 0]


def make_phasors(station_rows, iono_rows, directions, freq_ratio):
    delays = (
        station_rows[:, 0:1] * directions[0][None, :]
        + station_rows[:, 1:2] * directions[1][None, :]
    )
    delays = delays + station_rows[:, 2:3] * directions[2][None, :]
    angles = (TWO_PI * freq_ratio)[None, :, None] * delays[:, None, :] + iono_rows[
        :, None, :
    ] / freq_ratio[None, :, None]
    return jnp.concatenate([jnp.cos(angles), jnp.sin(angles)], axis=-1).astype(jnp.bfloat16)


def spectrum(source_flux, spectral_index, freq_ratio, count):
    return (
        source_flux[None, :]
        * jnp.exp(spectral_index[None, :] * jnp.log(freq_ratio)[:, None])
        / math.sqrt(count)
    )


def weight_rows(phasors, intensity):
    sources = intensity.shape[1]
    real_part = (phasors[:, :, :sources].astype(jnp.float32) * intensity[None]).astype(jnp.bfloat16)
    imag_part = (phasors[:, :, sources:].astype(jnp.float32) * intensity[None]).astype(jnp.bfloat16)
    upper_rows = jnp.concatenate([real_part, imag_part], axis=-1)
    lower_rows = jnp.concatenate([imag_part, -real_part], axis=-1)
    return jnp.concatenate([upper_rows, lower_rows], axis=0)


def body(
    screen,
    pierce_coords,
    query_dest,
    positions,
    directions,
    freq_ratio,
    source_flux,
    spectral_index,
):
    groups = lax.axis_size("stn")
    tile_cols = screen.shape[2]
    strip_rows = screen.shape[0] * screen.shape[1]
    values = screen.reshape(-1)
    capacity = query_dest.shape[3]
    coords = pierce_coords.reshape(2, groups, capacity)
    received = lax.all_to_all(coords, "stn", split_axis=1, concat_axis=1, tiled=True)
    sampled = interpolate_kernel(
        values.reshape(strip_rows, tile_cols), received.reshape(2, groups * capacity)
    ).reshape(groups, capacity)
    returned = lax.all_to_all(sampled, "stn", split_axis=0, concat_axis=0, tiled=True)
    stations_local = positions.shape[1]
    local_sources = source_flux.shape[0] // lax.axis_size("chan")
    queries = stations_local * local_sources
    buffer = (
        jnp.zeros((queries + 1,), jnp.float32).at[query_dest.reshape(-1)].set(returned.reshape(-1))
    )
    own_iono = buffer[:queries].reshape(stations_local, local_sources)
    station_rows = positions.T
    total_stations = stations_local * groups
    channels = freq_ratio.shape[0]
    n_chan = lax.axis_size("chan")
    if channels % groups:
        return _rows_path(own_iono, station_rows, directions, freq_ratio, source_flux, spectral_index)
    packed = jnp.concatenate([own_iono, station_rows], axis=1)
    gathered = lax.all_gather(packed, ("stn", "chan"), axis=0, tiled=False)
    gathered = gathered.reshape(groups, n_chan, stations_local, local_sources + 3)
    all_iono = (
        gathered[:, :, :, :local_sources]
        .transpose(0, 2, 1, 3)
        .reshape(total_stations, n_chan * local_sources)
    )
    all_rows = gathered[:, 0, :, local_sources:].reshape(total_stations, 3)
    per_dev = channels // groups
    my_freq = lax.dynamic_slice_in_dim(freq_ratio, lax.axis_index("stn") * per_dev, per_dev)
    phasors = make_phasors(all_rows, all_iono, directions, my_freq)
    intensity = spectrum(source_flux, spectral_index, my_freq, source_flux.shape[0])
    weighted = weight_rows(phasors, intensity)
    columns = jnp.einsum("ack,nck->can", weighted, phasors, preferred_element_type=jnp.float32)
    visible = columns.reshape(per_dev, 2, total_stations, total_stations)
    ids = jnp.arange(total_stations, dtype=jnp.int32)
    cross_only = ids[:, None] != ids[None, :]
    visible = jnp.where(cross_only[None, None], visible, jnp.zeros_like(visible))
    return lax.all_to_all(visible, "stn", split_axis=2, concat_axis=0, tiled=True)


def _rows_path(own_iono, station_rows, directions, freq_ratio, source_flux, spectral_index):
    groups = lax.axis_size("stn")
    stations_local = station_rows.shape[0]
    iono_phase = lax.all_gather(own_iono, "chan", axis=1, tiled=True)
    own_phasors = make_phasors(station_rows, iono_phase, directions, freq_ratio)
    intensity = spectrum(source_flux, spectral_index, freq_ratio, source_flux.shape[0])
    weighted = weight_rows(own_phasors, intensity)
    total_stations = stations_local * groups
    channels = freq_ratio.shape[0]
    columns = jnp.einsum(
        "ack,nck->can",
        weighted,
        make_phasors(
            lax.all_gather(station_rows, "stn", axis=0, tiled=True),
            lax.all_gather(iono_phase, "stn", axis=0, tiled=True),
            directions,
            freq_ratio,
        ),
        preferred_element_type=jnp.float32,
    )
    visible = columns.reshape(channels, 2, stations_local, total_stations)
    first_row = lax.axis_index("stn") * stations_local
    rows_global = first_row + jnp.arange(stations_local, dtype=jnp.int32)
    cross_only = rows_global[:, None] != jnp.arange(total_stations, dtype=jnp.int32)[None, :]
    return jnp.where(cross_only[None, None], visible, jnp.zeros_like(visible))


def solution(mesh):
    in_specs = (
        P("stn", None, None),
        P(None, "stn", "chan", None, None),
        P("stn", "chan", None, None),
        P(None, "stn"),
        P(),
        P("chan"),
        P(),
        P(),
    )
    out_specs = P("chan", None, "stn", None)
    return jax.shard_map(body, mesh=mesh, in_specs=in_specs, out_specs=out_specs, check_vma=False)
```

```python
import math

import jax
import jax.numpy as jnp
from jax import lax
from jax.experimental import pallas as pl
from jax.experimental.pallas import tpu as pltpu
from jax.sharding import PartitionSpec as P

TWO_PI = 2.0 * math.pi


def interpolate(values, coords, strip_rows, tile_cols):
    row_pos = coords[0] * (strip_rows - 1)
    col_pos = coords[1] * (tile_cols - 1)
    row_low = jnp.clip(jnp.floor(row_pos), 0.0, strip_rows - 2.0)
    col_low = jnp.clip(jnp.floor(col_pos), 0.0, tile_cols - 2.0)
    frac_y = row_pos - row_low
    frac_x = col_pos - col_low
    corner = row_low.astype(jnp.int32) * tile_cols + col_low.astype(jnp.int32)
    lower_pair = (1.0 - frac_x) * values[corner] + frac_x * values[corner + 1]
    upper_pair = (1.0 - frac_x) * values[corner + tile_cols] + frac_x * values[
        corner + tile_cols + 1
    ]
    return (1.0 - frac_y) * lower_pair + frac_y * upper_pair


UNROLL = 16


def _interp_kernel(r_ref, c_ref, s_ref, o_ref):
    rows = s_ref.shape[0]
    two_nb = s_ref.shape[1]
    nb = two_nb // 2
    cols = nb * 128
    chunk = o_ref.shape[0]
    base = pl.program_id(0) * chunk
    sub = lax.broadcasted_iota(jnp.int32, (two_nb, 128), 0)
    lane = lax.broadcasted_iota(jnp.int32, (two_nb, 128), 1)
    col = ((sub % nb) * 128 + lane).astype(jnp.float32)
    upper = sub >= nb
    rowid = lax.broadcasted_iota(jnp.int32, (8, 128), 0)

    def group(g, carry):
        for h in range(UNROLL // 8):
            acc = jnp.zeros((8, 128), jnp.float32)
            for u in range(8):
                j = base + g * UNROLL + h * 8 + u
                t = s_ref[r_ref[j]]
                y = jnp.full((two_nb, 128), c_ref[0, j], jnp.float32) * (rows - 1)
                x = jnp.full((two_nb, 128), c_ref[1, j], jnp.float32) * (cols - 1)
                ry = jnp.clip(jnp.floor(y), 0.0, rows - 2.0)
                kx = jnp.clip(jnp.floor(x), 0.0, cols - 2.0)
                fy = y - ry
                fx = x - kx
                wy = jnp.where(upper, fy, 1.0 - fy)
                wx = jnp.where(col == kx, 1.0 - fx, jnp.where(col == kx + 1.0, fx, 0.0))
                row = jnp.sum(t * (wy * wx), axis=0, keepdims=True)
                acc = jnp.where(rowid == u, row, acc)
            start = pl.multiple_of(g * UNROLL + h * 8, 8)
            o_ref[pl.ds(start, 8), :] = jnp.sum(acc, axis=1, keepdims=True)
        return carry

    lax.fori_loop(0, chunk // UNROLL, group, 0)


def interpolate_kernel(screen2d, coords):
    rows, cols = screen2d.shape
    nb = cols // 128
    q = coords.shape[1]
    chunk = min(2048, q)
    r = jnp.clip(jnp.floor(coords[0] * (rows - 1)), 0.0, rows - 2.0).astype(jnp.int32)
    pair = jnp.concatenate([screen2d, jnp.roll(screen2d, -1, axis=0)], axis=1)
    pair = pair.reshape(rows, 2 * nb, 128)
    out = pl.pallas_call(
        _interp_kernel,
        grid_spec=pltpu.PrefetchScalarGridSpec(
            num_scalar_prefetch=2,
            grid=(q // chunk,),
            in_specs=[pl.BlockSpec((rows, 2 * nb, 128), lambda i, rr, cc: (0, 0, 0))],
            out_specs=pl.BlockSpec((chunk, 1), lambda i, rr, cc: (i, 0)),
        ),
        out_shape=jax.ShapeDtypeStruct((q, 1), jnp.float32),
    )(r, coords, pair)
    return out[:, 0]


def make_phasors(station_rows, iono_rows, directions, freq_ratio):
    delays = (
        station_rows[:, 0:1] * directions[0][None, :]
        + station_rows[:, 1:2] * directions[1][None, :]
    )
    delays = delays + station_rows[:, 2:3] * directions[2][None, :]
    angles = (TWO_PI * freq_ratio)[None, :, None] * delays[:, None, :] + iono_rows[
        :, None, :
    ] / freq_ratio[None, :, None]
    return jnp.concatenate([jnp.cos(angles), jnp.sin(angles)], axis=-1).astype(jnp.bfloat16)


def spectrum(source_flux, spectral_index, freq_ratio, count):
    return (
        source_flux[None, :]
        * jnp.exp(spectral_index[None, :] * jnp.log(freq_ratio)[:, None])
        / math.sqrt(count)
    )


def weight_rows(phasors, intensity):
    sources = intensity.shape[1]
    real_part = (phasors[:, :, :sources].astype(jnp.float32) * intensity[None]).astype(jnp.bfloat16)
    imag_part = (phasors[:, :, sources:].astype(jnp.float32) * intensity[None]).astype(jnp.bfloat16)
    upper_rows = jnp.concatenate([real_part, imag_part], axis=-1)
    lower_rows = jnp.concatenate([imag_part, -real_part], axis=-1)
    return jnp.concatenate([upper_rows, lower_rows], axis=0)


def body(
    screen,
    pierce_coords,
    query_dest,
    positions,
    directions,
    freq_ratio,
    source_flux,
    spectral_index,
):
    groups = lax.axis_size("stn")
    tile_cols = screen.shape[2]
    strip_rows = screen.shape[0] * screen.shape[1]
    values = screen.reshape(-1)
    capacity = query_dest.shape[3]
    coords = pierce_coords.reshape(2, groups, capacity)
    received = lax.all_to_all(coords, "stn", split_axis=1, concat_axis=1, tiled=True)
    sampled = interpolate_kernel(
        values.reshape(strip_rows, tile_cols), received.reshape(2, groups * capacity)
    ).reshape(groups, capacity)
    returned = lax.all_to_all(sampled, "stn", split_axis=0, concat_axis=0, tiled=True)
    stations_local = positions.shape[1]
    local_sources = source_flux.shape[0] // lax.axis_size("chan")
    queries = stations_local * local_sources
    buffer = (
        jnp.zeros((queries + 1,), jnp.float32).at[query_dest.reshape(-1)].set(returned.reshape(-1))
    )
    own_iono = buffer[:queries].reshape(stations_local, local_sources)
    station_rows = positions.T
    total_stations = stations_local * groups
    channels = freq_ratio.shape[0]
    n_chan = lax.axis_size("chan")
    if channels % groups:
        return _rows_path(own_iono, station_rows, directions, freq_ratio, source_flux, spectral_index)
    iono_phase = lax.all_gather(own_iono, "chan", axis=1, tiled=True)
    packed = jnp.concatenate([iono_phase, station_rows], axis=1)
    gathered = lax.all_gather(packed, "stn", axis=0, tiled=True)
    all_iono = gathered[:, : n_chan * local_sources]
    all_rows = gathered[:, n_chan * local_sources :]
    per_dev = channels // groups
    my_freq = lax.dynamic_slice_in_dim(freq_ratio, lax.axis_index("stn") * per_dev, per_dev)
    phasors = make_phasors(all_rows, all_iono, directions, my_freq)
    intensity = spectrum(source_flux, spectral_index, my_freq, source_flux.shape[0])
    weighted = weight_rows(phasors, intensity)
    columns = jnp.einsum("ack,nck->can", weighted, phasors, preferred_element_type=jnp.float32)
    visible = columns.reshape(per_dev, 2, total_stations, total_stations)
    ids = jnp.arange(total_stations, dtype=jnp.int32)
    cross_only = ids[:, None] != ids[None, :]
    visible = jnp.where(cross_only[None, None], visible, jnp.zeros_like(visible))
    return lax.all_to_all(visible, "stn", split_axis=2, concat_axis=0, tiled=True)


def _rows_path(own_iono, station_rows, directions, freq_ratio, source_flux, spectral_index):
    groups = lax.axis_size("stn")
    stations_local = station_rows.shape[0]
    iono_phase = lax.all_gather(own_iono, "chan", axis=1, tiled=True)
    own_phasors = make_phasors(station_rows, iono_phase, directions, freq_ratio)
    intensity = spectrum(source_flux, spectral_index, freq_ratio, source_flux.shape[0])
    weighted = weight_rows(own_phasors, intensity)
    total_stations = stations_local * groups
    channels = freq_ratio.shape[0]
    columns = jnp.einsum(
        "ack,nck->can",
        weighted,
        make_phasors(
            lax.all_gather(station_rows, "stn", axis=0, tiled=True),
            lax.all_gather(iono_phase, "stn", axis=0, tiled=True),
            directions,
            freq_ratio,
        ),
        preferred_element_type=jnp.float32,
    )
    visible = columns.reshape(channels, 2, stations_local, total_stations)
    first_row = lax.axis_index("stn") * stations_local
    rows_global = first_row + jnp.arange(stations_local, dtype=jnp.int32)
    cross_only = rows_global[:, None] != jnp.arange(total_stations, dtype=jnp.int32)[None, :]
    return jnp.where(cross_only[None, None], visible, jnp.zeros_like(visible))


def solution(mesh):
    in_specs = (
        P("stn", None, None),
        P(None, "stn", "chan", None, None),
        P("stn", "chan", None, None),
        P(None, "stn"),
        P(),
        P("chan"),
        P(),
        P(),
    )
    out_specs = P("chan", None, "stn", None)
    return jax.shard_map(body, mesh=mesh, in_specs=in_specs, out_specs=out_specs, check_vma=False)
```

```python
import math

import jax
import jax.numpy as jnp
from jax import lax
from jax.experimental import pallas as pl
from jax.experimental.pallas import tpu as pltpu
from jax.sharding import PartitionSpec as P

TWO_PI = 2.0 * math.pi


def interpolate(values, coords, strip_rows, tile_cols):
    row_pos = coords[0] * (strip_rows - 1)
    col_pos = coords[1] * (tile_cols - 1)
    row_low = jnp.clip(jnp.floor(row_pos), 0.0, strip_rows - 2.0)
    col_low = jnp.clip(jnp.floor(col_pos), 0.0, tile_cols - 2.0)
    frac_y = row_pos - row_low
    frac_x = col_pos - col_low
    corner = row_low.astype(jnp.int32) * tile_cols + col_low.astype(jnp.int32)
    lower_pair = (1.0 - frac_x) * values[corner] + frac_x * values[corner + 1]
    upper_pair = (1.0 - frac_x) * values[corner + tile_cols] + frac_x * values[
        corner + tile_cols + 1
    ]
    return (1.0 - frac_y) * lower_pair + frac_y * upper_pair


UNROLL = 32


def _interp_kernel(r_ref, c_ref, s_ref, o_ref):
    rows = s_ref.shape[0]
    two_nb = s_ref.shape[1]
    nb = two_nb // 2
    cols = nb * 128
    chunk = o_ref.shape[0]
    base = pl.program_id(0) * chunk
    sub = lax.broadcasted_iota(jnp.int32, (two_nb, 128), 0)
    lane = lax.broadcasted_iota(jnp.int32, (two_nb, 128), 1)
    col = ((sub % nb) * 128 + lane).astype(jnp.float32)
    upper = sub >= nb
    rowid = lax.broadcasted_iota(jnp.int32, (8, 128), 0)

    def group(g, carry):
        for h in range(UNROLL // 8):
            acc = jnp.zeros((8, 128), jnp.float32)
            for u in range(8):
                j = base + g * UNROLL + h * 8 + u
                t = s_ref[r_ref[j]]
                y = jnp.full((two_nb, 128), c_ref[0, j], jnp.float32) * (rows - 1)
                x = jnp.full((two_nb, 128), c_ref[1, j], jnp.float32) * (cols - 1)
                ry = jnp.clip(jnp.floor(y), 0.0, rows - 2.0)
                kx = jnp.clip(jnp.floor(x), 0.0, cols - 2.0)
                fy = y - ry
                fx = x - kx
                wy = jnp.where(upper, fy, 1.0 - fy)
                wx = jnp.where(col == kx, 1.0 - fx, jnp.where(col == kx + 1.0, fx, 0.0))
                row = jnp.sum(t * (wy * wx), axis=0, keepdims=True)
                acc = jnp.where(rowid == u, row, acc)
            start = pl.multiple_of(g * UNROLL + h * 8, 8)
            o_ref[pl.ds(start, 8), :] = jnp.sum(acc, axis=1, keepdims=True)
        return carry

    lax.fori_loop(0, chunk // UNROLL, group, 0)


def interpolate_kernel(screen2d, coords):
    rows, cols = screen2d.shape
    nb = cols // 128
    q = coords.shape[1]
    chunk = min(2048, q)
    r = jnp.clip(jnp.floor(coords[0] * (rows - 1)), 0.0, rows - 2.0).astype(jnp.int32)
    pair = jnp.concatenate([screen2d, jnp.roll(screen2d, -1, axis=0)], axis=1)
    pair = pair.reshape(rows, 2 * nb, 128)
    out = pl.pallas_call(
        _interp_kernel,
        grid_spec=pltpu.PrefetchScalarGridSpec(
            num_scalar_prefetch=2,
            grid=(q // chunk,),
            in_specs=[pl.BlockSpec((rows, 2 * nb, 128), lambda i, rr, cc: (0, 0, 0))],
            out_specs=pl.BlockSpec((chunk, 1), lambda i, rr, cc: (i, 0)),
        ),
        out_shape=jax.ShapeDtypeStruct((q, 1), jnp.float32),
    )(r, coords, pair)
    return out[:, 0]


def _scatter_kernel(d_ref, v_ref, o_ref):
    def body(i, carry):
        o_ref[d_ref[i]] = v_ref[i]
        return carry

    lax.fori_loop(0, d_ref.shape[0], body, 0, unroll=16)


def scatter_kernel(dest, vals, size):
    return pl.pallas_call(
        _scatter_kernel,
        grid_spec=pltpu.PrefetchScalarGridSpec(
            num_scalar_prefetch=2,
            grid=(1,),
            in_specs=[],
            out_specs=pl.BlockSpec((size,), lambda i, d, v: (0,), memory_space=pltpu.SMEM),
        ),
        out_shape=jax.ShapeDtypeStruct((size,), jnp.float32),
    )(dest, vals)


def make_phasors(station_rows, iono_rows, directions, freq_ratio):
    delays = (
        station_rows[:, 0:1] * directions[0][None, :]
        + station_rows[:, 1:2] * directions[1][None, :]
    )
    delays = delays + station_rows[:, 2:3] * directions[2][None, :]
    angles = (TWO_PI * freq_ratio)[None, :, None] * delays[:, None, :] + iono_rows[
        :, None, :
    ] / freq_ratio[None, :, None]
    return jnp.concatenate([jnp.cos(angles), jnp.sin(angles)], axis=-1).astype(jnp.bfloat16)


def spectrum(source_flux, spectral_index, freq_ratio, count):
    return (
        source_flux[None, :]
        * jnp.exp(spectral_index[None, :] * jnp.log(freq_ratio)[:, None])
        / math.sqrt(count)
    )


def weight_rows(phasors, intensity):
    sources = intensity.shape[1]
    real_part = (phasors[:, :, :sources].astype(jnp.float32) * intensity[None]).astype(jnp.bfloat16)
    imag_part = (phasors[:, :, sources:].astype(jnp.float32) * intensity[None]).astype(jnp.bfloat16)
    upper_rows = jnp.concatenate([real_part, imag_part], axis=-1)
    lower_rows = jnp.concatenate([imag_part, -real_part], axis=-1)
    return jnp.concatenate([upper_rows, lower_rows], axis=0)


def body(
    screen,
    pierce_coords,
    query_dest,
    positions,
    directions,
    freq_ratio,
    source_flux,
    spectral_index,
):
    groups = lax.axis_size("stn")
    tile_cols = screen.shape[2]
    strip_rows = screen.shape[0] * screen.shape[1]
    values = screen.reshape(-1)
    capacity = query_dest.shape[3]
    coords = pierce_coords.reshape(2, groups, capacity)
    received = lax.all_to_all(coords, "stn", split_axis=1, concat_axis=1, tiled=True)
    sampled = interpolate_kernel(
        values.reshape(strip_rows, tile_cols), received.reshape(2, groups * capacity)
    ).reshape(groups, capacity)
    returned = lax.all_to_all(sampled, "stn", split_axis=0, concat_axis=0, tiled=True)
    stations_local = positions.shape[1]
    local_sources = source_flux.shape[0] // lax.axis_size("chan")
    queries = stations_local * local_sources
    buffer = scatter_kernel(query_dest.reshape(-1), returned.reshape(-1), queries + 1)
    own_iono = buffer[:queries].reshape(stations_local, local_sources)
    station_rows = positions.T
    total_stations = stations_local * groups
    channels = freq_ratio.shape[0]
    n_chan = lax.axis_size("chan")
    if channels % groups:
        return _rows_path(own_iono, station_rows, directions, freq_ratio, source_flux, spectral_index)
    iono_phase = lax.all_gather(own_iono, "chan", axis=1, tiled=True)
    packed = jnp.concatenate([iono_phase, station_rows], axis=1)
    gathered = lax.all_gather(packed, "stn", axis=0, tiled=True)
    all_iono = gathered[:, : n_chan * local_sources]
    all_rows = gathered[:, n_chan * local_sources :]
    per_dev = channels // groups
    my_freq = lax.dynamic_slice_in_dim(freq_ratio, lax.axis_index("stn") * per_dev, per_dev)
    phasors = make_phasors(all_rows, all_iono, directions, my_freq)
    intensity = spectrum(source_flux, spectral_index, my_freq, source_flux.shape[0])
    weighted = weight_rows(phasors, intensity)
    columns = jnp.einsum("ack,nck->can", weighted, phasors, preferred_element_type=jnp.float32)
    visible = columns.reshape(per_dev, 2, total_stations, total_stations)
    ids = jnp.arange(total_stations, dtype=jnp.int32)
    cross_only = ids[:, None] != ids[None, :]
    visible = jnp.where(cross_only[None, None], visible, jnp.zeros_like(visible))
    return lax.all_to_all(visible, "stn", split_axis=2, concat_axis=0, tiled=True)


def _rows_path(own_iono, station_rows, directions, freq_ratio, source_flux, spectral_index):
    groups = lax.axis_size("stn")
    stations_local = station_rows.shape[0]
    iono_phase = lax.all_gather(own_iono, "chan", axis=1, tiled=True)
    own_phasors = make_phasors(station_rows, iono_phase, directions, freq_ratio)
    intensity = spectrum(source_flux, spectral_index, freq_ratio, source_flux.shape[0])
    weighted = weight_rows(own_phasors, intensity)
    total_stations = stations_local * groups
    channels = freq_ratio.shape[0]
    columns = jnp.einsum(
        "ack,nck->can",
        weighted,
        make_phasors(
            lax.all_gather(station_rows, "stn", axis=0, tiled=True),
            lax.all_gather(iono_phase, "stn", axis=0, tiled=True),
            directions,
            freq_ratio,
        ),
        preferred_element_type=jnp.float32,
    )
    visible = columns.reshape(channels, 2, stations_local, total_stations)
    first_row = lax.axis_index("stn") * stations_local
    rows_global = first_row + jnp.arange(stations_local, dtype=jnp.int32)
    cross_only = rows_global[:, None] != jnp.arange(total_stations, dtype=jnp.int32)[None, :]
    return jnp.where(cross_only[None, None], visible, jnp.zeros_like(visible))


def solution(mesh):
    in_specs = (
        P("stn", None, None),
        P(None, "stn", "chan", None, None),
        P("stn", "chan", None, None),
        P(None, "stn"),
        P(),
        P("chan"),
        P(),
        P(),
    )
    out_specs = P("chan", None, "stn", None)
    return jax.shard_map(body, mesh=mesh, in_specs=in_specs, out_specs=out_specs, check_vma=False)
```

```python
import math

import jax
import jax.numpy as jnp
from jax import lax
from jax.experimental import pallas as pl
from jax.experimental.pallas import tpu as pltpu
from jax.sharding import PartitionSpec as P

TWO_PI = 2.0 * math.pi


def interpolate(values, coords, strip_rows, tile_cols):
    row_pos = coords[0] * (strip_rows - 1)
    col_pos = coords[1] * (tile_cols - 1)
    row_low = jnp.clip(jnp.floor(row_pos), 0.0, strip_rows - 2.0)
    col_low = jnp.clip(jnp.floor(col_pos), 0.0, tile_cols - 2.0)
    frac_y = row_pos - row_low
    frac_x = col_pos - col_low
    corner = row_low.astype(jnp.int32) * tile_cols + col_low.astype(jnp.int32)
    lower_pair = (1.0 - frac_x) * values[corner] + frac_x * values[corner + 1]
    upper_pair = (1.0 - frac_x) * values[corner + tile_cols] + frac_x * values[
        corner + tile_cols + 1
    ]
    return (1.0 - frac_y) * lower_pair + frac_y * upper_pair


UNROLL = 32


def _interp_kernel(r_ref, c_ref, s_ref, o_ref):
    rows = s_ref.shape[0]
    two_nb = s_ref.shape[1]
    nb = two_nb // 2
    cols = nb * 128
    chunk = o_ref.shape[0]
    base = pl.program_id(0) * chunk
    sub = lax.broadcasted_iota(jnp.int32, (two_nb, 128), 0)
    lane = lax.broadcasted_iota(jnp.int32, (two_nb, 128), 1)
    col = ((sub % nb) * 128 + lane).astype(jnp.float32)
    upper = sub >= nb
    rowid = lax.broadcasted_iota(jnp.int32, (8, 128), 0)

    def group(g, carry):
        for h in range(UNROLL // 8):
            acc = jnp.zeros((8, 128), jnp.float32)
            for u in range(8):
                j = base + g * UNROLL + h * 8 + u
                t = s_ref[r_ref[j]]
                y = jnp.full((two_nb, 128), c_ref[0, j], jnp.float32) * (rows - 1)
                x = jnp.full((two_nb, 128), c_ref[1, j], jnp.float32) * (cols - 1)
                ry = jnp.clip(jnp.floor(y), 0.0, rows - 2.0)
                kx = jnp.clip(jnp.floor(x), 0.0, cols - 2.0)
                fy = y - ry
                fx = x - kx
                wy = jnp.where(upper, fy, 1.0 - fy)
                wx = jnp.where(col == kx, 1.0 - fx, jnp.where(col == kx + 1.0, fx, 0.0))
                row = jnp.sum(t * (wy * wx), axis=0, keepdims=True)
                acc = jnp.where(rowid == u, row, acc)
            start = pl.multiple_of(g * UNROLL + h * 8, 8)
            o_ref[pl.ds(start, 8), :] = jnp.sum(acc, axis=1, keepdims=True)
        return carry

    lax.fori_loop(0, chunk // UNROLL, group, 0)


def interpolate_kernel(screen2d, coords):
    rows, cols = screen2d.shape
    nb = cols // 128
    q = coords.shape[1]
    chunk = min(2048, q)
    r = jnp.clip(jnp.floor(coords[0] * (rows - 1)), 0.0, rows - 2.0).astype(jnp.int32)
    pair = jnp.concatenate([screen2d, jnp.roll(screen2d, -1, axis=0)], axis=1)
    pair = pair.reshape(rows, 2 * nb, 128)
    out = pl.pallas_call(
        _interp_kernel,
        grid_spec=pltpu.PrefetchScalarGridSpec(
            num_scalar_prefetch=2,
            grid=(q // chunk,),
            in_specs=[pl.BlockSpec((rows, 2 * nb, 128), lambda i, rr, cc: (0, 0, 0))],
            out_specs=pl.BlockSpec((chunk, 1), lambda i, rr, cc: (i, 0)),
        ),
        out_shape=jax.ShapeDtypeStruct((q, 1), jnp.float32),
    )(r, coords, pair)
    return out[:, 0]


def _scatter_kernel(n_ref, d_ref, v_ref, o_ref):
    rows = n_ref.shape[0]
    width = d_ref.shape[0] // rows
    step = 8 if width % 8 == 0 else 1
    for row in range(rows):
        def body(i, carry, row=row):
            for u in range(step):
                slot = row * width + i * step + u
                o_ref[d_ref[slot]] = v_ref[slot]
            return carry

        lax.fori_loop(0, (n_ref[row] + step - 1) // step, body, 0)


def scatter_kernel(dest, vals, size):
    live = jnp.sum((dest < size - 1).astype(jnp.int32), axis=1)
    return pl.pallas_call(
        _scatter_kernel,
        grid_spec=pltpu.PrefetchScalarGridSpec(
            num_scalar_prefetch=3,
            grid=(1,),
            in_specs=[],
            out_specs=pl.BlockSpec((size,), lambda i, n, d, v: (0,), memory_space=pltpu.SMEM),
        ),
        out_shape=jax.ShapeDtypeStruct((size,), jnp.float32),
    )(live, dest.reshape(-1), vals.reshape(-1))


def make_phasors(station_rows, iono_rows, directions, freq_ratio):
    delays = (
        station_rows[:, 0:1] * directions[0][None, :]
        + station_rows[:, 1:2] * directions[1][None, :]
    )
    delays = delays + station_rows[:, 2:3] * directions[2][None, :]
    angles = (TWO_PI * freq_ratio)[None, :, None] * delays[:, None, :] + iono_rows[
        :, None, :
    ] / freq_ratio[None, :, None]
    return jnp.concatenate([jnp.cos(angles), jnp.sin(angles)], axis=-1).astype(jnp.bfloat16)


def spectrum(source_flux, spectral_index, freq_ratio, count):
    return (
        source_flux[None, :]
        * jnp.exp(spectral_index[None, :] * jnp.log(freq_ratio)[:, None])
        / math.sqrt(count)
    )


def weight_rows(phasors, intensity):
    sources = intensity.shape[1]
    real_part = (phasors[:, :, :sources].astype(jnp.float32) * intensity[None]).astype(jnp.bfloat16)
    imag_part = (phasors[:, :, sources:].astype(jnp.float32) * intensity[None]).astype(jnp.bfloat16)
    upper_rows = jnp.concatenate([real_part, imag_part], axis=-1)
    lower_rows = jnp.concatenate([imag_part, -real_part], axis=-1)
    return jnp.concatenate([upper_rows, lower_rows], axis=0)


def body(
    screen,
    pierce_coords,
    query_dest,
    positions,
    directions,
    freq_ratio,
    source_flux,
    spectral_index,
):
    groups = lax.axis_size("stn")
    tile_cols = screen.shape[2]
    strip_rows = screen.shape[0] * screen.shape[1]
    values = screen.reshape(-1)
    capacity = query_dest.shape[3]
    coords = pierce_coords.reshape(2, groups, capacity)
    received = lax.all_to_all(coords, "stn", split_axis=1, concat_axis=1, tiled=True)
    sampled = interpolate_kernel(
        values.reshape(strip_rows, tile_cols), received.reshape(2, groups * capacity)
    ).reshape(groups, capacity)
    returned = lax.all_to_all(sampled, "stn", split_axis=0, concat_axis=0, tiled=True)
    stations_local = positions.shape[1]
    local_sources = source_flux.shape[0] // lax.axis_size("chan")
    queries = stations_local * local_sources
    buffer = scatter_kernel(query_dest.reshape(groups, capacity), returned, queries + 1)
    own_iono = buffer[:queries].reshape(stations_local, local_sources)
    station_rows = positions.T
    total_stations = stations_local * groups
    channels = freq_ratio.shape[0]
    n_chan = lax.axis_size("chan")
    if channels % groups:
        return _rows_path(own_iono, station_rows, directions, freq_ratio, source_flux, spectral_index)
    iono_phase = lax.all_gather(own_iono, "chan", axis=1, tiled=True)
    packed = jnp.concatenate([iono_phase, station_rows], axis=1)
    gathered = lax.all_gather(packed, "stn", axis=0, tiled=True)
    all_iono = gathered[:, : n_chan * local_sources]
    all_rows = gathered[:, n_chan * local_sources :]
    per_dev = channels // groups
    my_freq = lax.dynamic_slice_in_dim(freq_ratio, lax.axis_index("stn") * per_dev, per_dev)
    phasors = make_phasors(all_rows, all_iono, directions, my_freq)
    intensity = spectrum(source_flux, spectral_index, my_freq, source_flux.shape[0])
    weighted = weight_rows(phasors, intensity)
    columns = jnp.einsum("ack,nck->can", weighted, phasors, preferred_element_type=jnp.float32)
    visible = columns.reshape(per_dev, 2, total_stations, total_stations)
    ids = jnp.arange(total_stations, dtype=jnp.int32)
    cross_only = ids[:, None] != ids[None, :]
    visible = jnp.where(cross_only[None, None], visible, jnp.zeros_like(visible))
    return lax.all_to_all(visible, "stn", split_axis=2, concat_axis=0, tiled=True)


def _rows_path(own_iono, station_rows, directions, freq_ratio, source_flux, spectral_index):
    groups = lax.axis_size("stn")
    stations_local = station_rows.shape[0]
    iono_phase = lax.all_gather(own_iono, "chan", axis=1, tiled=True)
    own_phasors = make_phasors(station_rows, iono_phase, directions, freq_ratio)
    intensity = spectrum(source_flux, spectral_index, freq_ratio, source_flux.shape[0])
    weighted = weight_rows(own_phasors, intensity)
    total_stations = stations_local * groups
    channels = freq_ratio.shape[0]
    columns = jnp.einsum(
        "ack,nck->can",
        weighted,
        make_phasors(
            lax.all_gather(station_rows, "stn", axis=0, tiled=True),
            lax.all_gather(iono_phase, "stn", axis=0, tiled=True),
            directions,
            freq_ratio,
        ),
        preferred_element_type=jnp.float32,
    )
    visible = columns.reshape(channels, 2, stations_local, total_stations)
    first_row = lax.axis_index("stn") * stations_local
    rows_global = first_row + jnp.arange(stations_local, dtype=jnp.int32)
    cross_only = rows_global[:, None] != jnp.arange(total_stations, dtype=jnp.int32)[None, :]
    return jnp.where(cross_only[None, None], visible, jnp.zeros_like(visible))


def solution(mesh):
    in_specs = (
        P("stn", None, None),
        P(None, "stn", "chan", None, None),
        P("stn", "chan", None, None),
        P(None, "stn"),
        P(),
        P("chan"),
        P(),
        P(),
    )
    out_specs = P("chan", None, "stn", None)
    return jax.shard_map(body, mesh=mesh, in_specs=in_specs, out_specs=out_specs, check_vma=False)
```

```python
import math

import jax
import jax.numpy as jnp
from jax import lax
from jax.experimental import pallas as pl
from jax.experimental.pallas import tpu as pltpu
from jax.sharding import PartitionSpec as P

TWO_PI = 2.0 * math.pi


def interpolate(values, coords, strip_rows, tile_cols):
    row_pos = coords[0] * (strip_rows - 1)
    col_pos = coords[1] * (tile_cols - 1)
    row_low = jnp.clip(jnp.floor(row_pos), 0.0, strip_rows - 2.0)
    col_low = jnp.clip(jnp.floor(col_pos), 0.0, tile_cols - 2.0)
    frac_y = row_pos - row_low
    frac_x = col_pos - col_low
    corner = row_low.astype(jnp.int32) * tile_cols + col_low.astype(jnp.int32)
    lower_pair = (1.0 - frac_x) * values[corner] + frac_x * values[corner + 1]
    upper_pair = (1.0 - frac_x) * values[corner + tile_cols] + frac_x * values[
        corner + tile_cols + 1
    ]
    return (1.0 - frac_y) * lower_pair + frac_y * upper_pair


UNROLL = 32


def _interp_kernel(r_ref, c_ref, s_ref, o_ref):
    rows = s_ref.shape[0]
    two_nb = s_ref.shape[1]
    nb = two_nb // 2
    cols = nb * 128
    chunk = o_ref.shape[0]
    base = pl.program_id(0) * chunk
    sub = lax.broadcasted_iota(jnp.int32, (two_nb, 128), 0)
    lane = lax.broadcasted_iota(jnp.int32, (two_nb, 128), 1)
    col = ((sub % nb) * 128 + lane).astype(jnp.float32)
    upper = sub >= nb
    rowid = lax.broadcasted_iota(jnp.int32, (8, 128), 0)

    def group(g, carry):
        for h in range(UNROLL // 8):
            acc = jnp.zeros((8, 128), jnp.float32)
            for u in range(8):
                j = base + g * UNROLL + h * 8 + u
                t = s_ref[r_ref[j]]
                y = jnp.full((two_nb, 128), c_ref[0, j], jnp.float32) * (rows - 1)
                x = jnp.full((two_nb, 128), c_ref[1, j], jnp.float32) * (cols - 1)
                ry = jnp.clip(jnp.floor(y), 0.0, rows - 2.0)
                kx = jnp.clip(jnp.floor(x), 0.0, cols - 2.0)
                fy = y - ry
                fx = x - kx
                wy = jnp.where(upper, fy, 1.0 - fy)
                wx = jnp.where(col == kx, 1.0 - fx, jnp.where(col == kx + 1.0, fx, 0.0))
                row = jnp.sum(t * (wy * wx), axis=0, keepdims=True)
                acc = jnp.where(rowid == u, row, acc)
            start = pl.multiple_of(g * UNROLL + h * 8, 8)
            o_ref[pl.ds(start, 8), :] = jnp.sum(acc, axis=1, keepdims=True)
        return carry

    lax.fori_loop(0, chunk // UNROLL, group, 0)


def interpolate_kernel(screen2d, coords):
    rows, cols = screen2d.shape
    nb = cols // 128
    q = coords.shape[1]
    chunk = min(2048, q)
    r = jnp.clip(jnp.floor(coords[0] * (rows - 1)), 0.0, rows - 2.0).astype(jnp.int32)
    pair = jnp.concatenate([screen2d, jnp.roll(screen2d, -1, axis=0)], axis=1)
    pair = pair.reshape(rows, 2 * nb, 128)
    out = pl.pallas_call(
        _interp_kernel,
        grid_spec=pltpu.PrefetchScalarGridSpec(
            num_scalar_prefetch=2,
            grid=(q // chunk,),
            in_specs=[pl.BlockSpec((rows, 2 * nb, 128), lambda i, rr, cc: (0, 0, 0))],
            out_specs=pl.BlockSpec((chunk, 1), lambda i, rr, cc: (i, 0)),
        ),
        out_shape=jax.ShapeDtypeStruct((q, 1), jnp.float32),
    )(r, coords, pair)
    return out[:, 0]


def _balanced_kernel(n_ref, r_ref, c_ref, s_ref, o_ref):
    rows = s_ref.shape[1]
    two_nb = s_ref.shape[2]
    nb = two_nb // 2
    cols = nb * 128
    senders = n_ref.shape[0] // 2
    seg = o_ref.shape[0] // senders
    unroll = min(UNROLL, seg)
    h = pl.program_id(0)
    sub = lax.broadcasted_iota(jnp.int32, (two_nb, 128), 0)
    lane = lax.broadcasted_iota(jnp.int32, (two_nb, 128), 1)
    col = ((sub % nb) * 128 + lane).astype(jnp.float32)
    upper = sub >= nb
    rowid = lax.broadcasted_iota(jnp.int32, (8, 128), 0)

    def segment(s, carry):
        def group(g, carry2):
            for part in range(unroll // 8):
                acc = jnp.zeros((8, 128), jnp.float32)
                first = s * seg + g * unroll + part * 8
                for u in range(8):
                    j = h * senders * seg + first + u
                    t = s_ref[0, r_ref[j]]
                    y = jnp.full((two_nb, 128), c_ref[0, j], jnp.float32) * (rows - 1)
                    x = jnp.full((two_nb, 128), c_ref[1, j], jnp.float32) * (cols - 1)
                    ry = jnp.clip(jnp.floor(y), 0.0, rows - 2.0)
                    kx = jnp.clip(jnp.floor(x), 0.0, cols - 2.0)
                    fy = y - ry
                    fx = x - kx
                    wy = jnp.where(upper, fy, 1.0 - fy)
                    wx = jnp.where(col == kx, 1.0 - fx, jnp.where(col == kx + 1.0, fx, 0.0))
                    row = jnp.sum(t * (wy * wx), axis=0, keepdims=True)
                    acc = jnp.where(rowid == u, row, acc)
                o_ref[pl.ds(pl.multiple_of(first, 8), 8), :] = jnp.sum(acc, axis=1, keepdims=True)
            return carry2

        trips = (n_ref[h * senders + s] + unroll - 1) // unroll
        lax.fori_loop(0, trips, group, 0)
        return carry

    lax.fori_loop(0, senders, segment, 0)


def pair_table(screen2d):
    rows, cols = screen2d.shape
    pair = jnp.concatenate([screen2d, jnp.roll(screen2d, -1, axis=0)], axis=1)
    return pair.reshape(rows, 2 * (cols // 128), 128)


def interpolate_balanced(tables, coords, live):
    _, rows, two_nb, _ = tables.shape
    _, halves, senders, seg = coords.shape
    flat = coords.reshape(2, halves * senders * seg)
    r = jnp.clip(jnp.floor(flat[0] * (rows - 1)), 0.0, rows - 2.0).astype(jnp.int32)
    out = pl.pallas_call(
        _balanced_kernel,
        grid_spec=pltpu.PrefetchScalarGridSpec(
            num_scalar_prefetch=3,
            grid=(halves,),
            in_specs=[pl.BlockSpec((1, rows, two_nb, 128), lambda i, n, rr, cc: (i, 0, 0, 0))],
            out_specs=pl.BlockSpec((senders * seg, 1), lambda i, n, rr, cc: (i, 0)),
        ),
        out_shape=jax.ShapeDtypeStruct((halves * senders * seg, 1), jnp.float32),
    )(live, r, flat, tables)
    return out.reshape(halves, senders, seg)


def _scatter_kernel(n_ref, d_ref, v_ref, o_ref):
    rows = n_ref.shape[0]
    width = d_ref.shape[0] // rows
    step = 8 if width % 8 == 0 else 1
    for row in range(rows):
        def body(i, carry, row=row):
            for u in range(step):
                slot = row * width + i * step + u
                o_ref[d_ref[slot]] = v_ref[slot]
            return carry

        lax.fori_loop(0, (n_ref[row] + step - 1) // step, body, 0)


def scatter_kernel(dest, vals, size):
    live = jnp.sum((dest < size - 1).astype(jnp.int32), axis=1)
    return pl.pallas_call(
        _scatter_kernel,
        grid_spec=pltpu.PrefetchScalarGridSpec(
            num_scalar_prefetch=3,
            grid=(1,),
            in_specs=[],
            out_specs=pl.BlockSpec((size,), lambda i, n, d, v: (0,), memory_space=pltpu.SMEM),
        ),
        out_shape=jax.ShapeDtypeStruct((size,), jnp.float32),
    )(live, dest.reshape(-1), vals.reshape(-1))


def make_phasors(station_rows, iono_rows, directions, freq_ratio):
    delays = (
        station_rows[:, 0:1] * directions[0][None, :]
        + station_rows[:, 1:2] * directions[1][None, :]
    )
    delays = delays + station_rows[:, 2:3] * directions[2][None, :]
    angles = (TWO_PI * freq_ratio)[None, :, None] * delays[:, None, :] + iono_rows[
        :, None, :
    ] / freq_ratio[None, :, None]
    return jnp.concatenate([jnp.cos(angles), jnp.sin(angles)], axis=-1).astype(jnp.bfloat16)


def spectrum(source_flux, spectral_index, freq_ratio, count):
    return (
        source_flux[None, :]
        * jnp.exp(spectral_index[None, :] * jnp.log(freq_ratio)[:, None])
        / math.sqrt(count)
    )


def weight_rows(phasors, intensity):
    sources = intensity.shape[1]
    real_part = (phasors[:, :, :sources].astype(jnp.float32) * intensity[None]).astype(jnp.bfloat16)
    imag_part = (phasors[:, :, sources:].astype(jnp.float32) * intensity[None]).astype(jnp.bfloat16)
    upper_rows = jnp.concatenate([real_part, imag_part], axis=-1)
    lower_rows = jnp.concatenate([imag_part, -real_part], axis=-1)
    return jnp.concatenate([upper_rows, lower_rows], axis=0)


def body(
    screen,
    pierce_coords,
    query_dest,
    positions,
    directions,
    freq_ratio,
    source_flux,
    spectral_index,
):
    groups = lax.axis_size("stn")
    tile_cols = screen.shape[2]
    strip_rows = screen.shape[0] * screen.shape[1]
    values = screen.reshape(-1)
    capacity = query_dest.shape[3]
    stations_local = positions.shape[1]
    local_sources = source_flux.shape[0] // lax.axis_size("chan")
    queries = stations_local * local_sources
    half = capacity // 2
    coords = pierce_coords.reshape(2, groups, capacity)
    dead = query_dest.reshape(groups, capacity) >= queries
    coords = jnp.where(dead[None], -1.0, coords).reshape(2, groups, half, 2)
    swap = lambda a: a.reshape(a.shape[0], groups // 2, 2, half)[:, :, ::-1, :].reshape(a.shape[0], groups, half)
    send = jnp.stack([coords[..., 0], swap(coords[..., 1])], axis=2)
    received = lax.all_to_all(send, "stn", split_axis=1, concat_axis=1, tiled=True)
    kin = received.transpose(0, 2, 1, 3)
    live = jnp.sum((kin[0] >= 0.0).astype(jnp.int32), axis=2).reshape(-1)
    screen2d = values.reshape(strip_rows, tile_cols)
    partner = lax.ppermute(screen2d, "stn", [(i, i ^ 1) for i in range(groups)])
    tables = jnp.stack([pair_table(screen2d), pair_table(partner)])
    sampled = interpolate_balanced(tables, kin, live).transpose(1, 0, 2)
    back = lax.all_to_all(sampled, "stn", split_axis=0, concat_axis=0, tiled=True)
    returned = jnp.stack([back[:, 0, :], swap(back[None, :, 1, :])[0]], axis=-1).reshape(groups, capacity)
    buffer = scatter_kernel(query_dest.reshape(groups, capacity), returned, queries + 1)
    own_iono = buffer[:queries].reshape(stations_local, local_sources)
    station_rows = positions.T
    total_stations = stations_local * groups
    channels = freq_ratio.shape[0]
    n_chan = lax.axis_size("chan")
    if channels % groups:
        return _rows_path(own_iono, station_rows, directions, freq_ratio, source_flux, spectral_index)
    iono_phase = lax.all_gather(own_iono, "chan", axis=1, tiled=True)
    packed = jnp.concatenate([iono_phase, station_rows], axis=1)
    gathered = lax.all_gather(packed, "stn", axis=0, tiled=True)
    all_iono = gathered[:, : n_chan * local_sources]
    all_rows = gathered[:, n_chan * local_sources :]
    per_dev = channels // groups
    my_freq = lax.dynamic_slice_in_dim(freq_ratio, lax.axis_index("stn") * per_dev, per_dev)
    phasors = make_phasors(all_rows, all_iono, directions, my_freq)
    intensity = spectrum(source_flux, spectral_index, my_freq, source_flux.shape[0])
    weighted = weight_rows(phasors, intensity)
    columns = jnp.einsum("ack,nck->can", weighted, phasors, preferred_element_type=jnp.float32)
    visible = columns.reshape(per_dev, 2, total_stations, total_stations)
    ids = jnp.arange(total_stations, dtype=jnp.int32)
    cross_only = ids[:, None] != ids[None, :]
    visible = jnp.where(cross_only[None, None], visible, jnp.zeros_like(visible))
    return lax.all_to_all(visible, "stn", split_axis=2, concat_axis=0, tiled=True)


def _rows_path(own_iono, station_rows, directions, freq_ratio, source_flux, spectral_index):
    groups = lax.axis_size("stn")
    stations_local = station_rows.shape[0]
    iono_phase = lax.all_gather(own_iono, "chan", axis=1, tiled=True)
    own_phasors = make_phasors(station_rows, iono_phase, directions, freq_ratio)
    intensity = spectrum(source_flux, spectral_index, freq_ratio, source_flux.shape[0])
    weighted = weight_rows(own_phasors, intensity)
    total_stations = stations_local * groups
    channels = freq_ratio.shape[0]
    columns = jnp.einsum(
        "ack,nck->can",
        weighted,
        make_phasors(
            lax.all_gather(station_rows, "stn", axis=0, tiled=True),
            lax.all_gather(iono_phase, "stn", axis=0, tiled=True),
            directions,
            freq_ratio,
        ),
        preferred_element_type=jnp.float32,
    )
    visible = columns.reshape(channels, 2, stations_local, total_stations)
    first_row = lax.axis_index("stn") * stations_local
    rows_global = first_row + jnp.arange(stations_local, dtype=jnp.int32)
    cross_only = rows_global[:, None] != jnp.arange(total_stations, dtype=jnp.int32)[None, :]
    return jnp.where(cross_only[None, None], visible, jnp.zeros_like(visible))


def solution(mesh):
    in_specs = (
        P("stn", None, None),
        P(None, "stn", "chan", None, None),
        P("stn", "chan", None, None),
        P(None, "stn"),
        P(),
        P("chan"),
        P(),
        P(),
    )
    out_specs = P("chan", None, "stn", None)
    return jax.shard_map(body, mesh=mesh, in_specs=in_specs, out_specs=out_specs, check_vma=False)
```

```python
import math

import jax
import jax.numpy as jnp
from jax import lax
from jax.experimental import pallas as pl
from jax.experimental.pallas import tpu as pltpu
from jax.sharding import PartitionSpec as P

TWO_PI = 2.0 * math.pi


def interpolate(values, coords, strip_rows, tile_cols):
    row_pos = coords[0] * (strip_rows - 1)
    col_pos = coords[1] * (tile_cols - 1)
    row_low = jnp.clip(jnp.floor(row_pos), 0.0, strip_rows - 2.0)
    col_low = jnp.clip(jnp.floor(col_pos), 0.0, tile_cols - 2.0)
    frac_y = row_pos - row_low
    frac_x = col_pos - col_low
    corner = row_low.astype(jnp.int32) * tile_cols + col_low.astype(jnp.int32)
    lower_pair = (1.0 - frac_x) * values[corner] + frac_x * values[corner + 1]
    upper_pair = (1.0 - frac_x) * values[corner + tile_cols] + frac_x * values[
        corner + tile_cols + 1
    ]
    return (1.0 - frac_y) * lower_pair + frac_y * upper_pair


UNROLL = 32


def _interp_kernel(r_ref, c_ref, s_ref, o_ref):
    rows = s_ref.shape[0]
    two_nb = s_ref.shape[1]
    nb = two_nb // 2
    cols = nb * 128
    chunk = o_ref.shape[0]
    base = pl.program_id(0) * chunk
    sub = lax.broadcasted_iota(jnp.int32, (two_nb, 128), 0)
    lane = lax.broadcasted_iota(jnp.int32, (two_nb, 128), 1)
    col = ((sub % nb) * 128 + lane).astype(jnp.float32)
    upper = sub >= nb
    rowid = lax.broadcasted_iota(jnp.int32, (8, 128), 0)

    def group(g, carry):
        for h in range(UNROLL // 8):
            acc = jnp.zeros((8, 128), jnp.float32)
            for u in range(8):
                j = base + g * UNROLL + h * 8 + u
                t = s_ref[r_ref[j]]
                y = jnp.full((two_nb, 128), c_ref[0, j], jnp.float32) * (rows - 1)
                x = jnp.full((two_nb, 128), c_ref[1, j], jnp.float32) * (cols - 1)
                ry = jnp.clip(jnp.floor(y), 0.0, rows - 2.0)
                kx = jnp.clip(jnp.floor(x), 0.0, cols - 2.0)
                fy = y - ry
                fx = x - kx
                wy = jnp.where(upper, fy, 1.0 - fy)
                wx = jnp.where(col == kx, 1.0 - fx, jnp.where(col == kx + 1.0, fx, 0.0))
                row = jnp.sum(t * (wy * wx), axis=0, keepdims=True)
                acc = jnp.where(rowid == u, row, acc)
            start = pl.multiple_of(g * UNROLL + h * 8, 8)
            o_ref[pl.ds(start, 8), :] = jnp.sum(acc, axis=1, keepdims=True)
        return carry

    lax.fori_loop(0, chunk // UNROLL, group, 0)


def interpolate_kernel(screen2d, coords):
    rows, cols = screen2d.shape
    nb = cols // 128
    q = coords.shape[1]
    chunk = min(2048, q)
    r = jnp.clip(jnp.floor(coords[0] * (rows - 1)), 0.0, rows - 2.0).astype(jnp.int32)
    pair = jnp.concatenate([screen2d, jnp.roll(screen2d, -1, axis=0)], axis=1)
    pair = pair.reshape(rows, 2 * nb, 128)
    out = pl.pallas_call(
        _interp_kernel,
        grid_spec=pltpu.PrefetchScalarGridSpec(
            num_scalar_prefetch=2,
            grid=(q // chunk,),
            in_specs=[pl.BlockSpec((rows, 2 * nb, 128), lambda i, rr, cc: (0, 0, 0))],
            out_specs=pl.BlockSpec((chunk, 1), lambda i, rr, cc: (i, 0)),
        ),
        out_shape=jax.ShapeDtypeStruct((q, 1), jnp.float32),
    )(r, coords, pair)
    return out[:, 0]


def _balanced_kernel(n_ref, r_ref, c_ref, s_ref, o_ref):
    rows = s_ref.shape[1]
    two_nb = s_ref.shape[2]
    nb = two_nb // 2
    cols = nb * 128
    senders = n_ref.shape[0] // 2
    seg = o_ref.shape[0] // senders
    unroll = min(UNROLL, seg)
    h = pl.program_id(0)
    sub = lax.broadcasted_iota(jnp.int32, (two_nb, 128), 0)
    lane = lax.broadcasted_iota(jnp.int32, (two_nb, 128), 1)
    col = ((sub % nb) * 128 + lane).astype(jnp.float32)
    upper = sub >= nb
    rowid = lax.broadcasted_iota(jnp.int32, (8, 128), 0)

    def segment(s, carry):
        def group(g, carry2):
            for part in range(unroll // 8):
                acc = jnp.zeros((8, 128), jnp.float32)
                first = s * seg + g * unroll + part * 8
                for u in range(8):
                    j = h * senders * seg + first + u
                    t = s_ref[0, r_ref[j]]
                    y = jnp.full((two_nb, 128), c_ref[0, j], jnp.float32) * (rows - 1)
                    x = jnp.full((two_nb, 128), c_ref[1, j], jnp.float32) * (cols - 1)
                    ry = jnp.clip(jnp.floor(y), 0.0, rows - 2.0)
                    kx = jnp.clip(jnp.floor(x), 0.0, cols - 2.0)
                    fy = y - ry
                    fx = x - kx
                    wy = jnp.where(upper, fy, 1.0 - fy)
                    wx = jnp.where(col == kx, 1.0 - fx, jnp.where(col == kx + 1.0, fx, 0.0))
                    row = jnp.sum(t * (wy * wx), axis=0, keepdims=True)
                    acc = jnp.where(rowid == u, row, acc)
                o_ref[pl.ds(pl.multiple_of(first, 8), 8), :] = jnp.sum(acc, axis=1, keepdims=True)
            return carry2

        trips = (n_ref[h * senders + s] + unroll - 1) // unroll
        lax.fori_loop(0, trips, group, 0)
        return carry

    lax.fori_loop(0, senders, segment, 0)


def pair_table(screen2d):
    rows, cols = screen2d.shape
    pair = jnp.concatenate([screen2d, jnp.roll(screen2d, -1, axis=0)], axis=1)
    return pair.reshape(rows, 2 * (cols // 128), 128)


def interpolate_balanced(tables, coords, live):
    _, rows, two_nb, _ = tables.shape
    _, halves, senders, seg = coords.shape
    flat = coords.reshape(2, halves * senders * seg)
    r = jnp.clip(jnp.floor(flat[0] * (rows - 1)), 0.0, rows - 2.0).astype(jnp.int32)
    out = pl.pallas_call(
        _balanced_kernel,
        grid_spec=pltpu.PrefetchScalarGridSpec(
            num_scalar_prefetch=3,
            grid=(halves,),
            in_specs=[pl.BlockSpec((1, rows, two_nb, 128), lambda i, n, rr, cc: (i, 0, 0, 0))],
            out_specs=pl.BlockSpec((senders * seg, 1), lambda i, n, rr, cc: (i, 0)),
        ),
        out_shape=jax.ShapeDtypeStruct((halves * senders * seg, 1), jnp.float32),
    )(live, r, flat, tables)
    return out.reshape(halves, senders, seg)


def _scatter_kernel(n_ref, d_ref, v_ref, o_ref):
    rows = n_ref.shape[0]
    width = d_ref.shape[0] // rows
    step = 8 if width % 8 == 0 else 1
    for row in range(rows):
        def body(i, carry, row=row):
            for u in range(step):
                slot = row * width + i * step + u
                o_ref[d_ref[slot]] = v_ref[slot]
            return carry

        lax.fori_loop(0, (n_ref[row] + step - 1) // step, body, 0)


def scatter_kernel(dest, vals, size):
    live = jnp.sum((dest < size - 1).astype(jnp.int32), axis=1)
    return pl.pallas_call(
        _scatter_kernel,
        grid_spec=pltpu.PrefetchScalarGridSpec(
            num_scalar_prefetch=3,
            grid=(1,),
            in_specs=[],
            out_specs=pl.BlockSpec((size,), lambda i, n, d, v: (0,), memory_space=pltpu.SMEM),
        ),
        out_shape=jax.ShapeDtypeStruct((size,), jnp.float32),
    )(live, dest.reshape(-1), vals.reshape(-1))


def make_phasors(station_rows, iono_rows, directions, freq_ratio):
    delays = (
        station_rows[:, 0:1] * directions[0][None, :]
        + station_rows[:, 1:2] * directions[1][None, :]
    )
    delays = delays + station_rows[:, 2:3] * directions[2][None, :]
    angles = (TWO_PI * freq_ratio)[None, :, None] * delays[:, None, :] + iono_rows[
        :, None, :
    ] / freq_ratio[None, :, None]
    return jnp.concatenate([jnp.cos(angles), jnp.sin(angles)], axis=-1).astype(jnp.bfloat16)


def spectrum(source_flux, spectral_index, freq_ratio, count):
    return (
        source_flux[None, :]
        * jnp.exp(spectral_index[None, :] * jnp.log(freq_ratio)[:, None])
        / math.sqrt(count)
    )


def weight_rows(phasors, intensity):
    sources = intensity.shape[1]
    real_part = (phasors[:, :, :sources].astype(jnp.float32) * intensity[None]).astype(jnp.bfloat16)
    imag_part = (phasors[:, :, sources:].astype(jnp.float32) * intensity[None]).astype(jnp.bfloat16)
    upper_rows = jnp.concatenate([real_part, imag_part], axis=-1)
    lower_rows = jnp.concatenate([imag_part, -real_part], axis=-1)
    return jnp.concatenate([upper_rows, lower_rows], axis=0)


def body(
    screen,
    pierce_coords,
    query_dest,
    positions,
    directions,
    freq_ratio,
    source_flux,
    spectral_index,
):
    groups = lax.axis_size("stn")
    tile_cols = screen.shape[2]
    strip_rows = screen.shape[0] * screen.shape[1]
    values = screen.reshape(-1)
    capacity = query_dest.shape[3]
    stations_local = positions.shape[1]
    local_sources = source_flux.shape[0] // lax.axis_size("chan")
    queries = stations_local * local_sources
    half = capacity // 2
    coords = pierce_coords.reshape(2, groups, capacity)
    dead = query_dest.reshape(groups, capacity) >= queries
    coords = jnp.where(dead[None], -1.0, coords).reshape(2, groups, half, 2)
    swap = lambda a: a.reshape(a.shape[0], groups // 2, 2, half)[:, :, ::-1, :].reshape(a.shape[0], groups, half)
    send = jnp.stack([coords[..., 0], swap(coords[..., 1])], axis=2)
    received = lax.all_to_all(send, "stn", split_axis=1, concat_axis=1, tiled=True)
    kin = received.transpose(0, 2, 1, 3)
    live = jnp.sum((kin[0] >= 0.0).astype(jnp.int32), axis=2).reshape(-1)
    screen2d = values.reshape(strip_rows, tile_cols)
    partner = lax.ppermute(screen2d, "stn", [(i, i ^ 1) for i in range(groups)])
    tables = jnp.stack([pair_table(screen2d), pair_table(partner)])
    sampled = interpolate_balanced(tables, kin, live).transpose(1, 0, 2)
    back = lax.all_to_all(sampled, "stn", split_axis=0, concat_axis=0, tiled=True)
    returned = jnp.stack([back[:, 0, :], swap(back[None, :, 1, :])[0]], axis=-1).reshape(groups, capacity)
    buffer = scatter_kernel(query_dest.reshape(groups, capacity), returned, queries + 1)
    own_iono = buffer[:queries].reshape(stations_local, local_sources)
    station_rows = positions.T
    total_stations = stations_local * groups
    channels = freq_ratio.shape[0]
    n_chan = lax.axis_size("chan")
    if channels % groups:
        return _rows_path(own_iono, station_rows, directions, freq_ratio, source_flux, spectral_index)
    iono_phase = lax.all_gather(own_iono, "chan", axis=1, tiled=True)
    packed = jnp.concatenate([iono_phase, station_rows], axis=1)
    gathered = lax.all_gather(packed, "stn", axis=0, tiled=True)
    all_iono = gathered[:, : n_chan * local_sources]
    all_rows = gathered[:, n_chan * local_sources :]
    per_dev = channels // groups
    my_freq = lax.dynamic_slice_in_dim(freq_ratio, lax.axis_index("stn") * per_dev, per_dev)
    phasors = make_phasors(all_rows, all_iono, directions, my_freq)
    intensity = spectrum(source_flux, spectral_index, my_freq, source_flux.shape[0])
    weighted = weight_rows(phasors, intensity)
    columns = jnp.einsum("ack,nck->can", weighted, phasors, preferred_element_type=jnp.float32)
    visible = columns.reshape(per_dev, 2, total_stations, total_stations)
    ids = jnp.arange(total_stations, dtype=jnp.int32)
    cross_only = ids[:, None] != ids[None, :]
    visible = jnp.where(cross_only[None, None], visible, jnp.zeros_like(visible))
    moved = lax.all_to_all(visible.astype(jnp.bfloat16), "stn", split_axis=2, concat_axis=0, tiled=True)
    return moved.astype(jnp.float32)


def _rows_path(own_iono, station_rows, directions, freq_ratio, source_flux, spectral_index):
    groups = lax.axis_size("stn")
    stations_local = station_rows.shape[0]
    iono_phase = lax.all_gather(own_iono, "chan", axis=1, tiled=True)
    own_phasors = make_phasors(station_rows, iono_phase, directions, freq_ratio)
    intensity = spectrum(source_flux, spectral_index, freq_ratio, source_flux.shape[0])
    weighted = weight_rows(own_phasors, intensity)
    total_stations = stations_local * groups
    channels = freq_ratio.shape[0]
    columns = jnp.einsum(
        "ack,nck->can",
        weighted,
        make_phasors(
            lax.all_gather(station_rows, "stn", axis=0, tiled=True),
            lax.all_gather(iono_phase, "stn", axis=0, tiled=True),
            directions,
            freq_ratio,
        ),
        preferred_element_type=jnp.float32,
    )
    visible = columns.reshape(channels, 2, stations_local, total_stations)
    first_row = lax.axis_index("stn") * stations_local
    rows_global = first_row + jnp.arange(stations_local, dtype=jnp.int32)
    cross_only = rows_global[:, None] != jnp.arange(total_stations, dtype=jnp.int32)[None, :]
    return jnp.where(cross_only[None, None], visible, jnp.zeros_like(visible))


def solution(mesh):
    in_specs = (
        P("stn", None, None),
        P(None, "stn", "chan", None, None),
        P("stn", "chan", None, None),
        P(None, "stn"),
        P(),
        P("chan"),
        P(),
        P(),
    )
    out_specs = P("chan", None, "stn", None)
    return jax.shard_map(body, mesh=mesh, in_specs=in_specs, out_specs=out_specs, check_vma=False)
```

```python
import math

import jax
import jax.numpy as jnp
from jax import lax
from jax.experimental import pallas as pl
from jax.experimental.pallas import tpu as pltpu
from jax.sharding import PartitionSpec as P

TWO_PI = 2.0 * math.pi


def interpolate(values, coords, strip_rows, tile_cols):
    row_pos = coords[0] * (strip_rows - 1)
    col_pos = coords[1] * (tile_cols - 1)
    row_low = jnp.clip(jnp.floor(row_pos), 0.0, strip_rows - 2.0)
    col_low = jnp.clip(jnp.floor(col_pos), 0.0, tile_cols - 2.0)
    frac_y = row_pos - row_low
    frac_x = col_pos - col_low
    corner = row_low.astype(jnp.int32) * tile_cols + col_low.astype(jnp.int32)
    lower_pair = (1.0 - frac_x) * values[corner] + frac_x * values[corner + 1]
    upper_pair = (1.0 - frac_x) * values[corner + tile_cols] + frac_x * values[
        corner + tile_cols + 1
    ]
    return (1.0 - frac_y) * lower_pair + frac_y * upper_pair


UNROLL = 32


def _interp_kernel(r_ref, c_ref, s_ref, o_ref):
    rows = s_ref.shape[0]
    two_nb = s_ref.shape[1]
    nb = two_nb // 2
    cols = nb * 128
    chunk = o_ref.shape[0]
    base = pl.program_id(0) * chunk
    sub = lax.broadcasted_iota(jnp.int32, (two_nb, 128), 0)
    lane = lax.broadcasted_iota(jnp.int32, (two_nb, 128), 1)
    col = ((sub % nb) * 128 + lane).astype(jnp.float32)
    upper = sub >= nb
    rowid = lax.broadcasted_iota(jnp.int32, (8, 128), 0)

    def group(g, carry):
        for h in range(UNROLL // 8):
            acc = jnp.zeros((8, 128), jnp.float32)
            for u in range(8):
                j = base + g * UNROLL + h * 8 + u
                t = s_ref[r_ref[j]]
                y = jnp.full((two_nb, 128), c_ref[0, j], jnp.float32) * (rows - 1)
                x = jnp.full((two_nb, 128), c_ref[1, j], jnp.float32) * (cols - 1)
                ry = jnp.clip(jnp.floor(y), 0.0, rows - 2.0)
                kx = jnp.clip(jnp.floor(x), 0.0, cols - 2.0)
                fy = y - ry
                fx = x - kx
                wy = jnp.where(upper, fy, 1.0 - fy)
                wx = jnp.where(col == kx, 1.0 - fx, jnp.where(col == kx + 1.0, fx, 0.0))
                row = jnp.sum(t * (wy * wx), axis=0, keepdims=True)
                acc = jnp.where(rowid == u, row, acc)
            start = pl.multiple_of(g * UNROLL + h * 8, 8)
            o_ref[pl.ds(start, 8), :] = jnp.sum(acc, axis=1, keepdims=True)
        return carry

    lax.fori_loop(0, chunk // UNROLL, group, 0)


def interpolate_kernel(screen2d, coords):
    rows, cols = screen2d.shape
    nb = cols // 128
    q = coords.shape[1]
    chunk = min(2048, q)
    r = jnp.clip(jnp.floor(coords[0] * (rows - 1)), 0.0, rows - 2.0).astype(jnp.int32)
    pair = jnp.concatenate([screen2d, jnp.roll(screen2d, -1, axis=0)], axis=1)
    pair = pair.reshape(rows, 2 * nb, 128)
    out = pl.pallas_call(
        _interp_kernel,
        grid_spec=pltpu.PrefetchScalarGridSpec(
            num_scalar_prefetch=2,
            grid=(q // chunk,),
            in_specs=[pl.BlockSpec((rows, 2 * nb, 128), lambda i, rr, cc: (0, 0, 0))],
            out_specs=pl.BlockSpec((chunk, 1), lambda i, rr, cc: (i, 0)),
        ),
        out_shape=jax.ShapeDtypeStruct((q, 1), jnp.float32),
    )(r, coords, pair)
    return out[:, 0]


def _balanced_kernel(n_ref, r_ref, c_ref, s_ref, o_ref):
    rows = s_ref.shape[1]
    two_nb = s_ref.shape[2]
    nb = two_nb // 2
    cols = nb * 128
    senders = n_ref.shape[0] // 2
    seg = o_ref.shape[0] // senders
    unroll = min(UNROLL, seg)
    h = pl.program_id(0)
    sub = lax.broadcasted_iota(jnp.int32, (two_nb, 128), 0)
    lane = lax.broadcasted_iota(jnp.int32, (two_nb, 128), 1)
    col = ((sub % nb) * 128 + lane).astype(jnp.float32)
    upper = sub >= nb
    rowid = lax.broadcasted_iota(jnp.int32, (8, 128), 0)

    def segment(s, carry):
        def group(g, carry2):
            for part in range(unroll // 8):
                acc = jnp.zeros((8, 128), jnp.float32)
                first = s * seg + g * unroll + part * 8
                for u in range(8):
                    j = h * senders * seg + first + u
                    t = s_ref[0, r_ref[j]]
                    y = jnp.full((two_nb, 128), c_ref[0, j], jnp.float32) * (rows - 1)
                    x = jnp.full((two_nb, 128), c_ref[1, j], jnp.float32) * (cols - 1)
                    ry = jnp.clip(jnp.floor(y), 0.0, rows - 2.0)
                    kx = jnp.clip(jnp.floor(x), 0.0, cols - 2.0)
                    fy = y - ry
                    fx = x - kx
                    wy = jnp.where(upper, fy, 1.0 - fy)
                    wx = jnp.where(col == kx, 1.0 - fx, jnp.where(col == kx + 1.0, fx, 0.0))
                    row = jnp.sum(t * (wy * wx), axis=0, keepdims=True)
                    acc = jnp.where(rowid == u, row, acc)
                o_ref[pl.ds(pl.multiple_of(first, 8), 8), :] = jnp.sum(acc, axis=1, keepdims=True)
            return carry2

        trips = (n_ref[h * senders + s] + unroll - 1) // unroll
        lax.fori_loop(0, trips, group, 0)
        return carry

    lax.fori_loop(0, senders, segment, 0)


def pair_table(screen2d):
    rows, cols = screen2d.shape
    pair = jnp.concatenate([screen2d, jnp.roll(screen2d, -1, axis=0)], axis=1)
    return pair.reshape(rows, 2 * (cols // 128), 128)


def interpolate_balanced(tables, coords, live):
    _, rows, two_nb, _ = tables.shape
    _, halves, senders, seg = coords.shape
    flat = coords.reshape(2, halves * senders * seg)
    r = jnp.clip(jnp.floor(flat[0] * (rows - 1)), 0.0, rows - 2.0).astype(jnp.int32)
    out = pl.pallas_call(
        _balanced_kernel,
        grid_spec=pltpu.PrefetchScalarGridSpec(
            num_scalar_prefetch=3,
            grid=(halves,),
            in_specs=[pl.BlockSpec((1, rows, two_nb, 128), lambda i, n, rr, cc: (i, 0, 0, 0))],
            out_specs=pl.BlockSpec((senders * seg, 1), lambda i, n, rr, cc: (i, 0)),
        ),
        out_shape=jax.ShapeDtypeStruct((halves * senders * seg, 1), jnp.float32),
    )(live, r, flat, tables)
    return out.reshape(halves, senders, seg)


def _scatter_kernel(n_ref, d_ref, v_ref, o_ref):
    rows = n_ref.shape[0]
    width = d_ref.shape[0] // rows
    half = width // 2
    step = 8 if width % 8 == 0 else 2
    for row in range(rows):
        def body(i, carry, row=row):
            for u in range(step):
                slot = row * width + i * step + u
                parity = u % 2
                source = ((row ^ parity) * 2 + parity) * half + i * (step // 2) + u // 2
                o_ref[d_ref[slot]] = v_ref[source]
            return carry

        lax.fori_loop(0, (n_ref[row] + step - 1) // step, body, 0)


def scatter_kernel(dest, vals, size):
    live = jnp.sum((dest < size - 1).astype(jnp.int32), axis=1)
    return pl.pallas_call(
        _scatter_kernel,
        grid_spec=pltpu.PrefetchScalarGridSpec(
            num_scalar_prefetch=3,
            grid=(1,),
            in_specs=[],
            out_specs=pl.BlockSpec((size,), lambda i, n, d, v: (0,), memory_space=pltpu.SMEM),
        ),
        out_shape=jax.ShapeDtypeStruct((size,), jnp.float32),
    )(live, dest.reshape(-1), vals.reshape(-1))


def make_phasors(station_rows, iono_rows, directions, freq_ratio):
    delays = (
        station_rows[:, 0:1] * directions[0][None, :]
        + station_rows[:, 1:2] * directions[1][None, :]
    )
    delays = delays + station_rows[:, 2:3] * directions[2][None, :]
    angles = (TWO_PI * freq_ratio)[None, :, None] * delays[:, None, :] + iono_rows[
        :, None, :
    ] / freq_ratio[None, :, None]
    return jnp.concatenate([jnp.cos(angles), jnp.sin(angles)], axis=-1).astype(jnp.bfloat16)


def spectrum(source_flux, spectral_index, freq_ratio, count):
    return (
        source_flux[None, :]
        * jnp.exp(spectral_index[None, :] * jnp.log(freq_ratio)[:, None])
        / math.sqrt(count)
    )


def weight_rows(phasors, intensity):
    sources = intensity.shape[1]
    real_part = (phasors[:, :, :sources].astype(jnp.float32) * intensity[None]).astype(jnp.bfloat16)
    imag_part = (phasors[:, :, sources:].astype(jnp.float32) * intensity[None]).astype(jnp.bfloat16)
    upper_rows = jnp.concatenate([real_part, imag_part], axis=-1)
    lower_rows = jnp.concatenate([imag_part, -real_part], axis=-1)
    return jnp.concatenate([upper_rows, lower_rows], axis=0)


def body(
    screen,
    pierce_coords,
    query_dest,
    positions,
    directions,
    freq_ratio,
    source_flux,
    spectral_index,
):
    groups = lax.axis_size("stn")
    tile_cols = screen.shape[2]
    strip_rows = screen.shape[0] * screen.shape[1]
    values = screen.reshape(-1)
    capacity = query_dest.shape[3]
    stations_local = positions.shape[1]
    local_sources = source_flux.shape[0] // lax.axis_size("chan")
    queries = stations_local * local_sources
    half = capacity // 2
    coords = pierce_coords.reshape(2, groups, capacity)
    dead = query_dest.reshape(groups, capacity) >= queries
    coords = jnp.where(dead[None], -1.0, coords).reshape(2, groups, half, 2)
    swap = lambda a: a.reshape(a.shape[0], groups // 2, 2, half)[:, :, ::-1, :].reshape(a.shape[0], groups, half)
    send = jnp.stack([coords[..., 0], swap(coords[..., 1])], axis=2)
    received = lax.all_to_all(send, "stn", split_axis=1, concat_axis=1, tiled=True)
    kin = received.transpose(0, 2, 1, 3)
    live = jnp.sum((kin[0] >= 0.0).astype(jnp.int32), axis=2).reshape(-1)
    screen2d = values.reshape(strip_rows, tile_cols)
    partner = lax.ppermute(screen2d, "stn", [(i, i ^ 1) for i in range(groups)])
    tables = jnp.stack([pair_table(screen2d), pair_table(partner)])
    sampled = interpolate_balanced(tables, kin, live).transpose(1, 0, 2)
    back = lax.all_to_all(sampled, "stn", split_axis=0, concat_axis=0, tiled=True)
    buffer = scatter_kernel(query_dest.reshape(groups, capacity), back, queries + 1)
    own_iono = buffer[:queries].reshape(stations_local, local_sources)
    station_rows = positions.T
    total_stations = stations_local * groups
    channels = freq_ratio.shape[0]
    n_chan = lax.axis_size("chan")
    if channels % groups:
        return _rows_path(own_iono, station_rows, directions, freq_ratio, source_flux, spectral_index)
    iono_phase = lax.all_gather(own_iono, "chan", axis=1, tiled=True)
    packed = jnp.concatenate([iono_phase, station_rows], axis=1)
    gathered = lax.all_gather(packed, "stn", axis=0, tiled=True)
    all_iono = gathered[:, : n_chan * local_sources]
    all_rows = gathered[:, n_chan * local_sources :]
    per_dev = channels // groups
    my_freq = lax.dynamic_slice_in_dim(freq_ratio, lax.axis_index("stn") * per_dev, per_dev)
    phasors = make_phasors(all_rows, all_iono, directions, my_freq)
    intensity = spectrum(source_flux, spectral_index, my_freq, source_flux.shape[0])
    weighted = weight_rows(phasors, intensity)
    columns = jnp.einsum("ack,nck->can", weighted, phasors, preferred_element_type=jnp.float32)
    visible = columns.reshape(per_dev, 2, total_stations, total_stations)
    ids = jnp.arange(total_stations, dtype=jnp.int32)
    cross_only = ids[:, None] != ids[None, :]
    visible = jnp.where(cross_only[None, None], visible, jnp.zeros_like(visible))
    moved = lax.all_to_all(visible.astype(jnp.bfloat16), "stn", split_axis=2, concat_axis=0, tiled=True)
    return moved.astype(jnp.float32)


def _rows_path(own_iono, station_rows, directions, freq_ratio, source_flux, spectral_index):
    groups = lax.axis_size("stn")
    stations_local = station_rows.shape[0]
    iono_phase = lax.all_gather(own_iono, "chan", axis=1, tiled=True)
    own_phasors = make_phasors(station_rows, iono_phase, directions, freq_ratio)
    intensity = spectrum(source_flux, spectral_index, freq_ratio, source_flux.shape[0])
    weighted = weight_rows(own_phasors, intensity)
    total_stations = stations_local * groups
    channels = freq_ratio.shape[0]
    columns = jnp.einsum(
        "ack,nck->can",
        weighted,
        make_phasors(
            lax.all_gather(station_rows, "stn", axis=0, tiled=True),
            lax.all_gather(iono_phase, "stn", axis=0, tiled=True),
            directions,
            freq_ratio,
        ),
        preferred_element_type=jnp.float32,
    )
    visible = columns.reshape(channels, 2, stations_local, total_stations)
    first_row = lax.axis_index("stn") * stations_local
    rows_global = first_row + jnp.arange(stations_local, dtype=jnp.int32)
    cross_only = rows_global[:, None] != jnp.arange(total_stations, dtype=jnp.int32)[None, :]
    return jnp.where(cross_only[None, None], visible, jnp.zeros_like(visible))


def solution(mesh):
    in_specs = (
        P("stn", None, None),
        P(None, "stn", "chan", None, None),
        P("stn", "chan", None, None),
        P(None, "stn"),
        P(),
        P("chan"),
        P(),
        P(),
    )
    out_specs = P("chan", None, "stn", None)
    return jax.shard_map(body, mesh=mesh, in_specs=in_specs, out_specs=out_specs, check_vma=False)
```

```python
import math

import jax
import jax.numpy as jnp
from jax import lax
from jax.experimental import pallas as pl
from jax.experimental.pallas import tpu as pltpu
from jax.sharding import PartitionSpec as P

TWO_PI = 2.0 * math.pi


def interpolate(values, coords, strip_rows, tile_cols):
    row_pos = coords[0] * (strip_rows - 1)
    col_pos = coords[1] * (tile_cols - 1)
    row_low = jnp.clip(jnp.floor(row_pos), 0.0, strip_rows - 2.0)
    col_low = jnp.clip(jnp.floor(col_pos), 0.0, tile_cols - 2.0)
    frac_y = row_pos - row_low
    frac_x = col_pos - col_low
    corner = row_low.astype(jnp.int32) * tile_cols + col_low.astype(jnp.int32)
    lower_pair = (1.0 - frac_x) * values[corner] + frac_x * values[corner + 1]
    upper_pair = (1.0 - frac_x) * values[corner + tile_cols] + frac_x * values[
        corner + tile_cols + 1
    ]
    return (1.0 - frac_y) * lower_pair + frac_y * upper_pair


UNROLL = 32


def _interp_kernel(r_ref, c_ref, s_ref, o_ref):
    rows = s_ref.shape[0]
    two_nb = s_ref.shape[1]
    nb = two_nb // 2
    cols = nb * 128
    chunk = o_ref.shape[0]
    base = pl.program_id(0) * chunk
    sub = lax.broadcasted_iota(jnp.int32, (two_nb, 128), 0)
    lane = lax.broadcasted_iota(jnp.int32, (two_nb, 128), 1)
    col = ((sub % nb) * 128 + lane).astype(jnp.float32)
    upper = sub >= nb
    rowid = lax.broadcasted_iota(jnp.int32, (8, 128), 0)

    def group(g, carry):
        for h in range(UNROLL // 8):
            acc = jnp.zeros((8, 128), jnp.float32)
            for u in range(8):
                j = base + g * UNROLL + h * 8 + u
                t = s_ref[r_ref[j]]
                y = jnp.full((two_nb, 128), c_ref[0, j], jnp.float32) * (rows - 1)
                x = jnp.full((two_nb, 128), c_ref[1, j], jnp.float32) * (cols - 1)
                ry = jnp.clip(jnp.floor(y), 0.0, rows - 2.0)
                kx = jnp.clip(jnp.floor(x), 0.0, cols - 2.0)
                fy = y - ry
                fx = x - kx
                wy = jnp.where(upper, fy, 1.0 - fy)
                wx = jnp.where(col == kx, 1.0 - fx, jnp.where(col == kx + 1.0, fx, 0.0))
                row = jnp.sum(t * (wy * wx), axis=0, keepdims=True)
                acc = jnp.where(rowid == u, row, acc)
            start = pl.multiple_of(g * UNROLL + h * 8, 8)
            o_ref[pl.ds(start, 8), :] = jnp.sum(acc, axis=1, keepdims=True)
        return carry

    lax.fori_loop(0, chunk // UNROLL, group, 0)


def interpolate_kernel(screen2d, coords):
    rows, cols = screen2d.shape
    nb = cols // 128
    q = coords.shape[1]
    chunk = min(2048, q)
    r = jnp.clip(jnp.floor(coords[0] * (rows - 1)), 0.0, rows - 2.0).astype(jnp.int32)
    pair = jnp.concatenate([screen2d, jnp.roll(screen2d, -1, axis=0)], axis=1)
    pair = pair.reshape(rows, 2 * nb, 128)
    out = pl.pallas_call(
        _interp_kernel,
        grid_spec=pltpu.PrefetchScalarGridSpec(
            num_scalar_prefetch=2,
            grid=(q // chunk,),
            in_specs=[pl.BlockSpec((rows, 2 * nb, 128), lambda i, rr, cc: (0, 0, 0))],
            out_specs=pl.BlockSpec((chunk, 1), lambda i, rr, cc: (i, 0)),
        ),
        out_shape=jax.ShapeDtypeStruct((q, 1), jnp.float32),
    )(r, coords, pair)
    return out[:, 0]


def _balanced_kernel(n_ref, r_ref, c_ref, own_ref, partner_ref, o_ref):
    rows = own_ref.shape[0]
    nb = own_ref.shape[1]
    cols = nb * 128
    senders = n_ref.shape[0] // 2
    seg = o_ref.shape[0] // (2 * senders)
    unroll = min(UNROLL, seg)
    sub = lax.broadcasted_iota(jnp.int32, (nb, 128), 0)
    lane = lax.broadcasted_iota(jnp.int32, (nb, 128), 1)
    col = (sub * 128 + lane).astype(jnp.float32)
    rowid = lax.broadcasted_iota(jnp.int32, (8, 128), 0)

    for h, s_ref in enumerate((own_ref, partner_ref)):
        def segment(s, carry, h=h, s_ref=s_ref):
            def group(g, carry2):
                for part in range(unroll // 8):
                    acc = jnp.zeros((8, 128), jnp.float32)
                    first = (h * senders + s) * seg + g * unroll + part * 8
                    for u in range(8):
                        j = first + u
                        r = r_ref[j]
                        lower = s_ref[r]
                        upper = s_ref[r + 1]
                        y = jnp.full((nb, 128), c_ref[0, j], jnp.float32) * (rows - 1)
                        x = jnp.full((nb, 128), c_ref[1, j], jnp.float32) * (cols - 1)
                        ry = jnp.clip(jnp.floor(y), 0.0, rows - 2.0)
                        kx = jnp.clip(jnp.floor(x), 0.0, cols - 2.0)
                        fy = y - ry
                        fx = x - kx
                        blend = (1.0 - fy) * lower + fy * upper
                        wx = jnp.where(col == kx, 1.0 - fx, jnp.where(col == kx + 1.0, fx, 0.0))
                        row = jnp.sum(blend * wx, axis=0, keepdims=True)
                        acc = jnp.where(rowid == u, row, acc)
                    o_ref[pl.ds(pl.multiple_of(first, 8), 8), :] = jnp.sum(acc, axis=1, keepdims=True)
                return carry2

            trips = (n_ref[h * senders + s] + unroll - 1) // unroll
            lax.fori_loop(0, trips, group, 0)
            return carry

        lax.fori_loop(0, senders, segment, 0)


def interpolate_balanced(own, partner, coords, live):
    rows, cols = own.shape
    nb = cols // 128
    _, halves, senders, seg = coords.shape
    flat = coords.reshape(2, halves * senders * seg)
    r = jnp.clip(jnp.floor(flat[0] * (rows - 1)), 0.0, rows - 2.0).astype(jnp.int32)
    spec = pl.BlockSpec((rows, nb, 128), lambda i, n, rr, cc: (0, 0, 0))
    out = pl.pallas_call(
        _balanced_kernel,
        grid_spec=pltpu.PrefetchScalarGridSpec(
            num_scalar_prefetch=3,
            grid=(1,),
            in_specs=[spec, spec],
            out_specs=pl.BlockSpec((halves * senders * seg, 1), lambda i, n, rr, cc: (0, 0)),
        ),
        out_shape=jax.ShapeDtypeStruct((halves * senders * seg, 1), jnp.float32),
    )(live, r, flat, own.reshape(rows, nb, 128), partner.reshape(rows, nb, 128))
    return out.reshape(halves, senders, seg)


def _scatter_kernel(n_ref, d_ref, v_ref, o_ref):
    rows = n_ref.shape[0]
    width = d_ref.shape[0] // rows
    half = width // 2
    step = 8 if width % 8 == 0 else 2
    for row in range(rows):
        def body(i, carry, row=row):
            for u in range(step):
                slot = row * width + i * step + u
                parity = u % 2
                source = ((row ^ parity) * 2 + parity) * half + i * (step // 2) + u // 2
                o_ref[d_ref[slot]] = v_ref[source]
            return carry

        lax.fori_loop(0, (n_ref[row] + step - 1) // step, body, 0)


def scatter_kernel(dest, vals, size):
    live = jnp.sum((dest < size - 1).astype(jnp.int32), axis=1)
    return pl.pallas_call(
        _scatter_kernel,
        grid_spec=pltpu.PrefetchScalarGridSpec(
            num_scalar_prefetch=3,
            grid=(1,),
            in_specs=[],
            out_specs=pl.BlockSpec((size,), lambda i, n, d, v: (0,), memory_space=pltpu.SMEM),
        ),
        out_shape=jax.ShapeDtypeStruct((size,), jnp.float32),
    )(live, dest.reshape(-1), vals.reshape(-1))


def make_phasors(station_rows, iono_rows, directions, freq_ratio):
    delays = (
        station_rows[:, 0:1] * directions[0][None, :]
        + station_rows[:, 1:2] * directions[1][None, :]
    )
    delays = delays + station_rows[:, 2:3] * directions[2][None, :]
    angles = (TWO_PI * freq_ratio)[None, :, None] * delays[:, None, :] + iono_rows[
        :, None, :
    ] / freq_ratio[None, :, None]
    return jnp.concatenate([jnp.cos(angles), jnp.sin(angles)], axis=-1).astype(jnp.bfloat16)


def spectrum(source_flux, spectral_index, freq_ratio, count):
    return (
        source_flux[None, :]
        * jnp.exp(spectral_index[None, :] * jnp.log(freq_ratio)[:, None])
        / math.sqrt(count)
    )


def weight_rows(phasors, intensity):
    sources = intensity.shape[1]
    real_part = (phasors[:, :, :sources].astype(jnp.float32) * intensity[None]).astype(jnp.bfloat16)
    imag_part = (phasors[:, :, sources:].astype(jnp.float32) * intensity[None]).astype(jnp.bfloat16)
    upper_rows = jnp.concatenate([real_part, imag_part], axis=-1)
    lower_rows = jnp.concatenate([imag_part, -real_part], axis=-1)
    return jnp.concatenate([upper_rows, lower_rows], axis=0)


def body(
    screen,
    pierce_coords,
    query_dest,
    positions,
    directions,
    freq_ratio,
    source_flux,
    spectral_index,
):
    groups = lax.axis_size("stn")
    tile_cols = screen.shape[2]
    strip_rows = screen.shape[0] * screen.shape[1]
    values = screen.reshape(-1)
    capacity = query_dest.shape[3]
    stations_local = positions.shape[1]
    local_sources = source_flux.shape[0] // lax.axis_size("chan")
    queries = stations_local * local_sources
    half = capacity // 2
    coords = pierce_coords.reshape(2, groups, capacity)
    dead = query_dest.reshape(groups, capacity) >= queries
    coords = jnp.where(dead[None], -1.0, coords).reshape(2, groups, half, 2)
    swap = lambda a: a.reshape(a.shape[0], groups // 2, 2, half)[:, :, ::-1, :].reshape(a.shape[0], groups, half)
    send = jnp.stack([coords[..., 0], swap(coords[..., 1])], axis=2)
    received = lax.all_to_all(send, "stn", split_axis=1, concat_axis=1, tiled=True)
    kin = received.transpose(0, 2, 1, 3)
    live = jnp.sum((kin[0] >= 0.0).astype(jnp.int32), axis=2).reshape(-1)
    screen2d = values.reshape(strip_rows, tile_cols)
    partner = lax.ppermute(screen2d, "stn", [(i, i ^ 1) for i in range(groups)])
    sampled = interpolate_balanced(screen2d, partner, kin, live).transpose(1, 0, 2)
    back = lax.all_to_all(sampled, "stn", split_axis=0, concat_axis=0, tiled=True)
    buffer = scatter_kernel(query_dest.reshape(groups, capacity), back, queries + 1)
    own_iono = buffer[:queries].reshape(stations_local, local_sources)
    station_rows = positions.T
    total_stations = stations_local * groups
    channels = freq_ratio.shape[0]
    n_chan = lax.axis_size("chan")
    if channels % groups:
        return _rows_path(own_iono, station_rows, directions, freq_ratio, source_flux, spectral_index)
    iono_phase = lax.all_gather(own_iono, "chan", axis=1, tiled=True)
    packed = jnp.concatenate([iono_phase, station_rows], axis=1)
    gathered = lax.all_gather(packed, "stn", axis=0, tiled=True)
    all_iono = gathered[:, : n_chan * local_sources]
    all_rows = gathered[:, n_chan * local_sources :]
    per_dev = channels // groups
    my_freq = lax.dynamic_slice_in_dim(freq_ratio, lax.axis_index("stn") * per_dev, per_dev)
    phasors = make_phasors(all_rows, all_iono, directions, my_freq)
    intensity = spectrum(source_flux, spectral_index, my_freq, source_flux.shape[0])
    weighted = weight_rows(phasors, intensity)
    columns = jnp.einsum("ack,nck->can", weighted, phasors, preferred_element_type=jnp.float32)
    visible = columns.reshape(per_dev, 2, total_stations, total_stations)
    ids = jnp.arange(total_stations, dtype=jnp.int32)
    cross_only = ids[:, None] != ids[None, :]
    visible = jnp.where(cross_only[None, None], visible, jnp.zeros_like(visible))
    moved = lax.all_to_all(visible.astype(jnp.bfloat16), "stn", split_axis=2, concat_axis=0, tiled=True)
    return moved.astype(jnp.float32)


def _rows_path(own_iono, station_rows, directions, freq_ratio, source_flux, spectral_index):
    groups = lax.axis_size("stn")
    stations_local = station_rows.shape[0]
    iono_phase = lax.all_gather(own_iono, "chan", axis=1, tiled=True)
    own_phasors = make_phasors(station_rows, iono_phase, directions, freq_ratio)
    intensity = spectrum(source_flux, spectral_index, freq_ratio, source_flux.shape[0])
    weighted = weight_rows(own_phasors, intensity)
    total_stations = stations_local * groups
    channels = freq_ratio.shape[0]
    columns = jnp.einsum(
        "ack,nck->can",
        weighted,
        make_phasors(
            lax.all_gather(station_rows, "stn", axis=0, tiled=True),
            lax.all_gather(iono_phase, "stn", axis=0, tiled=True),
            directions,
            freq_ratio,
        ),
        preferred_element_type=jnp.float32,
    )
    visible = columns.reshape(channels, 2, stations_local, total_stations)
    first_row = lax.axis_index("stn") * stations_local
    rows_global = first_row + jnp.arange(stations_local, dtype=jnp.int32)
    cross_only = rows_global[:, None] != jnp.arange(total_stations, dtype=jnp.int32)[None, :]
    return jnp.where(cross_only[None, None], visible, jnp.zeros_like(visible))


def solution(mesh):
    in_specs = (
        P("stn", None, None),
        P(None, "stn", "chan", None, None),
        P("stn", "chan", None, None),
        P(None, "stn"),
        P(),
        P("chan"),
        P(),
        P(),
    )
    out_specs = P("chan", None, "stn", None)
    return jax.shard_map(body, mesh=mesh, in_specs=in_specs, out_specs=out_specs, check_vma=False)
```

```python
import math

import jax
import jax.numpy as jnp
from jax import lax
from jax.experimental import pallas as pl
from jax.experimental.pallas import tpu as pltpu
from jax.sharding import PartitionSpec as P

TWO_PI = 2.0 * math.pi


def interpolate(values, coords, strip_rows, tile_cols):
    row_pos = coords[0] * (strip_rows - 1)
    col_pos = coords[1] * (tile_cols - 1)
    row_low = jnp.clip(jnp.floor(row_pos), 0.0, strip_rows - 2.0)
    col_low = jnp.clip(jnp.floor(col_pos), 0.0, tile_cols - 2.0)
    frac_y = row_pos - row_low
    frac_x = col_pos - col_low
    corner = row_low.astype(jnp.int32) * tile_cols + col_low.astype(jnp.int32)
    lower_pair = (1.0 - frac_x) * values[corner] + frac_x * values[corner + 1]
    upper_pair = (1.0 - frac_x) * values[corner + tile_cols] + frac_x * values[
        corner + tile_cols + 1
    ]
    return (1.0 - frac_y) * lower_pair + frac_y * upper_pair


UNROLL = 32
KBITS = 12


def _interp_kernel(r_ref, c_ref, s_ref, o_ref):
    rows = s_ref.shape[0]
    two_nb = s_ref.shape[1]
    nb = two_nb // 2
    cols = nb * 128
    chunk = o_ref.shape[0]
    base = pl.program_id(0) * chunk
    sub = lax.broadcasted_iota(jnp.int32, (two_nb, 128), 0)
    lane = lax.broadcasted_iota(jnp.int32, (two_nb, 128), 1)
    col = ((sub % nb) * 128 + lane).astype(jnp.float32)
    upper = sub >= nb
    rowid = lax.broadcasted_iota(jnp.int32, (8, 128), 0)

    def group(g, carry):
        for h in range(UNROLL // 8):
            acc = jnp.zeros((8, 128), jnp.float32)
            for u in range(8):
                j = base + g * UNROLL + h * 8 + u
                t = s_ref[r_ref[j]]
                y = jnp.full((two_nb, 128), c_ref[0, j], jnp.float32) * (rows - 1)
                x = jnp.full((two_nb, 128), c_ref[1, j], jnp.float32) * (cols - 1)
                ry = jnp.clip(jnp.floor(y), 0.0, rows - 2.0)
                kx = jnp.clip(jnp.floor(x), 0.0, cols - 2.0)
                fy = y - ry
                fx = x - kx
                wy = jnp.where(upper, fy, 1.0 - fy)
                wx = jnp.where(col == kx, 1.0 - fx, jnp.where(col == kx + 1.0, fx, 0.0))
                row = jnp.sum(t * (wy * wx), axis=0, keepdims=True)
                acc = jnp.where(rowid == u, row, acc)
            start = pl.multiple_of(g * UNROLL + h * 8, 8)
            o_ref[pl.ds(start, 8), :] = jnp.sum(acc, axis=1, keepdims=True)
        return carry

    lax.fori_loop(0, chunk // UNROLL, group, 0)


def interpolate_kernel(screen2d, coords):
    rows, cols = screen2d.shape
    nb = cols // 128
    q = coords.shape[1]
    chunk = min(2048, q)
    r = jnp.clip(jnp.floor(coords[0] * (rows - 1)), 0.0, rows - 2.0).astype(jnp.int32)
    pair = jnp.concatenate([screen2d, jnp.roll(screen2d, -1, axis=0)], axis=1)
    pair = pair.reshape(rows, 2 * nb, 128)
    out = pl.pallas_call(
        _interp_kernel,
        grid_spec=pltpu.PrefetchScalarGridSpec(
            num_scalar_prefetch=2,
            grid=(q // chunk,),
            in_specs=[pl.BlockSpec((rows, 2 * nb, 128), lambda i, rr, cc: (0, 0, 0))],
            out_specs=pl.BlockSpec((chunk, 1), lambda i, rr, cc: (i, 0)),
        ),
        out_shape=jax.ShapeDtypeStruct((q, 1), jnp.float32),
    )(r, coords, pair)
    return out[:, 0]


def _balanced_kernel(n_ref, r_ref, c_ref, own_ref, partner_ref, o_ref):
    rows = own_ref.shape[0]
    nb = own_ref.shape[1]
    cols = nb * 128
    senders = n_ref.shape[0] // 2
    seg = o_ref.shape[0] // (2 * senders)
    unroll = min(UNROLL, seg)
    sub = lax.broadcasted_iota(jnp.int32, (nb, 128), 0)
    lane = lax.broadcasted_iota(jnp.int32, (nb, 128), 1)
    col = sub * 128 + lane
    rowid = lax.broadcasted_iota(jnp.int32, (8, 128), 0)

    for h, s_ref in enumerate((own_ref, partner_ref)):
        def segment(s, carry, h=h, s_ref=s_ref):
            def group(g, carry2):
                for part in range(unroll // 8):
                    acc = jnp.zeros((8, 128), jnp.float32)
                    first = (h * senders + s) * seg + g * unroll + part * 8
                    for u in range(8):
                        j = first + u
                        rk = r_ref[j]
                        r = rk >> KBITS
                        k = rk & ((1 << KBITS) - 1)
                        lower = s_ref[r]
                        upper = s_ref[r + 1]
                        fy = c_ref[0, j]
                        fx = c_ref[1, j]
                        blend = (1.0 - fy) * lower + fy * upper
                        wx = jnp.where(col == k, 1.0 - fx, jnp.where(col == k + 1, fx, 0.0))
                        row = jnp.sum(blend * wx, axis=0, keepdims=True)
                        acc = jnp.where(rowid == u, row, acc)
                    o_ref[pl.ds(pl.multiple_of(first, 8), 8), :] = jnp.sum(acc, axis=1, keepdims=True)
                return carry2

            trips = (n_ref[h * senders + s] + unroll - 1) // unroll
            lax.fori_loop(0, trips, group, 0)
            return carry

        lax.fori_loop(0, senders, segment, 0)


def interpolate_balanced(own, partner, coords, live):
    rows, cols = own.shape
    nb = cols // 128
    _, halves, senders, seg = coords.shape
    flat = coords.reshape(2, halves * senders * seg)
    y = flat[0] * (rows - 1)
    x = flat[1] * (cols - 1)
    r = jnp.clip(jnp.floor(y), 0.0, rows - 2.0)
    k = jnp.clip(jnp.floor(x), 0.0, cols - 2.0)
    rk = (r.astype(jnp.int32) << KBITS) | k.astype(jnp.int32)
    frac = jnp.stack([y - r, x - k])
    spec = pl.BlockSpec((rows, nb, 128), lambda i, n, rr, cc: (0, 0, 0))
    out = pl.pallas_call(
        _balanced_kernel,
        grid_spec=pltpu.PrefetchScalarGridSpec(
            num_scalar_prefetch=3,
            grid=(1,),
            in_specs=[spec, spec],
            out_specs=pl.BlockSpec((halves * senders * seg, 1), lambda i, n, rr, cc: (0, 0)),
        ),
        out_shape=jax.ShapeDtypeStruct((halves * senders * seg, 1), jnp.float32),
    )(live, rk, frac, own.reshape(rows, nb, 128), partner.reshape(rows, nb, 128))
    return out.reshape(halves, senders, seg)


def _scatter_kernel(n_ref, d_ref, v_ref, o_ref):
    rows = n_ref.shape[0]
    width = d_ref.shape[0] // rows
    half = width // 2
    step = 8 if width % 8 == 0 else 2
    for row in range(rows):
        def body(i, carry, row=row):
            for u in range(step):
                slot = row * width + i * step + u
                parity = u % 2
                source = ((row ^ parity) * 2 + parity) * half + i * (step // 2) + u // 2
                o_ref[d_ref[slot]] = v_ref[source]
            return carry

        lax.fori_loop(0, (n_ref[row] + step - 1) // step, body, 0)


def scatter_kernel(dest, vals, size):
    live = jnp.sum((dest < size - 1).astype(jnp.int32), axis=1)
    return pl.pallas_call(
        _scatter_kernel,
        grid_spec=pltpu.PrefetchScalarGridSpec(
            num_scalar_prefetch=3,
            grid=(1,),
            in_specs=[],
            out_specs=pl.BlockSpec((size,), lambda i, n, d, v: (0,), memory_space=pltpu.SMEM),
        ),
        out_shape=jax.ShapeDtypeStruct((size,), jnp.float32),
    )(live, dest.reshape(-1), vals.reshape(-1))


def make_phasors(station_rows, iono_rows, directions, freq_ratio):
    delays = (
        station_rows[:, 0:1] * directions[0][None, :]
        + station_rows[:, 1:2] * directions[1][None, :]
    )
    delays = delays + station_rows[:, 2:3] * directions[2][None, :]
    angles = (TWO_PI * freq_ratio)[None, :, None] * delays[:, None, :] + iono_rows[
        :, None, :
    ] / freq_ratio[None, :, None]
    return jnp.concatenate([jnp.cos(angles), jnp.sin(angles)], axis=-1).astype(jnp.bfloat16)


def spectrum(source_flux, spectral_index, freq_ratio, count):
    return (
        source_flux[None, :]
        * jnp.exp(spectral_index[None, :] * jnp.log(freq_ratio)[:, None])
        / math.sqrt(count)
    )


def weight_rows(phasors, intensity):
    sources = intensity.shape[1]
    real_part = (phasors[:, :, :sources].astype(jnp.float32) * intensity[None]).astype(jnp.bfloat16)
    imag_part = (phasors[:, :, sources:].astype(jnp.float32) * intensity[None]).astype(jnp.bfloat16)
    upper_rows = jnp.concatenate([real_part, imag_part], axis=-1)
    lower_rows = jnp.concatenate([imag_part, -real_part], axis=-1)
    return jnp.concatenate([upper_rows, lower_rows], axis=0)


def body(
    screen,
    pierce_coords,
    query_dest,
    positions,
    directions,
    freq_ratio,
    source_flux,
    spectral_index,
):
    groups = lax.axis_size("stn")
    tile_cols = screen.shape[2]
    strip_rows = screen.shape[0] * screen.shape[1]
    values = screen.reshape(-1)
    capacity = query_dest.shape[3]
    stations_local = positions.shape[1]
    local_sources = source_flux.shape[0] // lax.axis_size("chan")
    queries = stations_local * local_sources
    half = capacity // 2
    coords = pierce_coords.reshape(2, groups, capacity)
    dead = query_dest.reshape(groups, capacity) >= queries
    coords = jnp.where(dead[None], -1.0, coords).reshape(2, groups, half, 2)
    swap = lambda a: a.reshape(a.shape[0], groups // 2, 2, half)[:, :, ::-1, :].reshape(a.shape[0], groups, half)
    send = jnp.stack([coords[..., 0], swap(coords[..., 1])], axis=2)
    received = lax.all_to_all(send, "stn", split_axis=1, concat_axis=1, tiled=True)
    kin = received.transpose(0, 2, 1, 3)
    live = jnp.sum((kin[0] >= 0.0).astype(jnp.int32), axis=2).reshape(-1)
    screen2d = values.reshape(strip_rows, tile_cols)
    partner = lax.ppermute(screen2d, "stn", [(i, i ^ 1) for i in range(groups)])
    sampled = interpolate_balanced(screen2d, partner, kin, live).transpose(1, 0, 2)
    back = lax.all_to_all(sampled, "stn", split_axis=0, concat_axis=0, tiled=True)
    buffer = scatter_kernel(query_dest.reshape(groups, capacity), back, queries + 1)
    own_iono = buffer[:queries].reshape(stations_local, local_sources)
    station_rows = positions.T
    total_stations = stations_local * groups
    channels = freq_ratio.shape[0]
    n_chan = lax.axis_size("chan")
    if channels % groups:
        return _rows_path(own_iono, station_rows, directions, freq_ratio, source_flux, spectral_index)
    iono_phase = lax.all_gather(own_iono, "chan", axis=1, tiled=True)
    packed = jnp.concatenate([iono_phase, station_rows], axis=1)
    gathered = lax.all_gather(packed, "stn", axis=0, tiled=True)
    all_iono = gathered[:, : n_chan * local_sources]
    all_rows = gathered[:, n_chan * local_sources :]
    per_dev = channels // groups
    my_freq = lax.dynamic_slice_in_dim(freq_ratio, lax.axis_index("stn") * per_dev, per_dev)
    phasors = make_phasors(all_rows, all_iono, directions, my_freq)
    intensity = spectrum(source_flux, spectral_index, my_freq, source_flux.shape[0])
    weighted = weight_rows(phasors, intensity)
    columns = jnp.einsum("ack,nck->can", weighted, phasors, preferred_element_type=jnp.float32)
    visible = columns.reshape(per_dev, 2, total_stations, total_stations)
    ids = jnp.arange(total_stations, dtype=jnp.int32)
    cross_only = ids[:, None] != ids[None, :]
    visible = jnp.where(cross_only[None, None], visible, jnp.zeros_like(visible))
    moved = lax.all_to_all(visible.astype(jnp.bfloat16), "stn", split_axis=2, concat_axis=0, tiled=True)
    return moved.astype(jnp.float32)


def _rows_path(own_iono, station_rows, directions, freq_ratio, source_flux, spectral_index):
    groups = lax.axis_size("stn")
    stations_local = station_rows.shape[0]
    iono_phase = lax.all_gather(own_iono, "chan", axis=1, tiled=True)
    own_phasors = make_phasors(station_rows, iono_phase, directions, freq_ratio)
    intensity = spectrum(source_flux, spectral_index, freq_ratio, source_flux.shape[0])
    weighted = weight_rows(own_phasors, intensity)
    total_stations = stations_local * groups
    channels = freq_ratio.shape[0]
    columns = jnp.einsum(
        "ack,nck->can",
        weighted,
        make_phasors(
            lax.all_gather(station_rows, "stn", axis=0, tiled=True),
            lax.all_gather(iono_phase, "stn", axis=0, tiled=True),
            directions,
            freq_ratio,
        ),
        preferred_element_type=jnp.float32,
    )
    visible = columns.reshape(channels, 2, stations_local, total_stations)
    first_row = lax.axis_index("stn") * stations_local
    rows_global = first_row + jnp.arange(stations_local, dtype=jnp.int32)
    cross_only = rows_global[:, None] != jnp.arange(total_stations, dtype=jnp.int32)[None, :]
    return jnp.where(cross_only[None, None], visible, jnp.zeros_like(visible))


def solution(mesh):
    in_specs = (
        P("stn", None, None),
        P(None, "stn", "chan", None, None),
        P("stn", "chan", None, None),
        P(None, "stn"),
        P(),
        P("chan"),
        P(),
        P(),
    )
    out_specs = P("chan", None, "stn", None)
    return jax.shard_map(body, mesh=mesh, in_specs=in_specs, out_specs=out_specs, check_vma=False)
```

```python
import math

import jax
import jax.numpy as jnp
from jax import lax
from jax.experimental import pallas as pl
from jax.experimental.pallas import tpu as pltpu
from jax.sharding import PartitionSpec as P

TWO_PI = 2.0 * math.pi


def interpolate(values, coords, strip_rows, tile_cols):
    row_pos = coords[0] * (strip_rows - 1)
    col_pos = coords[1] * (tile_cols - 1)
    row_low = jnp.clip(jnp.floor(row_pos), 0.0, strip_rows - 2.0)
    col_low = jnp.clip(jnp.floor(col_pos), 0.0, tile_cols - 2.0)
    frac_y = row_pos - row_low
    frac_x = col_pos - col_low
    corner = row_low.astype(jnp.int32) * tile_cols + col_low.astype(jnp.int32)
    lower_pair = (1.0 - frac_x) * values[corner] + frac_x * values[corner + 1]
    upper_pair = (1.0 - frac_x) * values[corner + tile_cols] + frac_x * values[
        corner + tile_cols + 1
    ]
    return (1.0 - frac_y) * lower_pair + frac_y * upper_pair


UNROLL = 32
KBITS = 12


def _interp_kernel(r_ref, c_ref, s_ref, o_ref):
    rows = s_ref.shape[0]
    two_nb = s_ref.shape[1]
    nb = two_nb // 2
    cols = nb * 128
    chunk = o_ref.shape[0]
    base = pl.program_id(0) * chunk
    sub = lax.broadcasted_iota(jnp.int32, (two_nb, 128), 0)
    lane = lax.broadcasted_iota(jnp.int32, (two_nb, 128), 1)
    col = ((sub % nb) * 128 + lane).astype(jnp.float32)
    upper = sub >= nb
    rowid = lax.broadcasted_iota(jnp.int32, (8, 128), 0)

    def group(g, carry):
        for h in range(UNROLL // 8):
            acc = jnp.zeros((8, 128), jnp.float32)
            for u in range(8):
                j = base + g * UNROLL + h * 8 + u
                t = s_ref[r_ref[j]]
                y = jnp.full((two_nb, 128), c_ref[0, j], jnp.float32) * (rows - 1)
                x = jnp.full((two_nb, 128), c_ref[1, j], jnp.float32) * (cols - 1)
                ry = jnp.clip(jnp.floor(y), 0.0, rows - 2.0)
                kx = jnp.clip(jnp.floor(x), 0.0, cols - 2.0)
                fy = y - ry
                fx = x - kx
                wy = jnp.where(upper, fy, 1.0 - fy)
                wx = jnp.where(col == kx, 1.0 - fx, jnp.where(col == kx + 1.0, fx, 0.0))
                row = jnp.sum(t * (wy * wx), axis=0, keepdims=True)
                acc = jnp.where(rowid == u, row, acc)
            start = pl.multiple_of(g * UNROLL + h * 8, 8)
            o_ref[pl.ds(start, 8), :] = jnp.sum(acc, axis=1, keepdims=True)
        return carry

    lax.fori_loop(0, chunk // UNROLL, group, 0)


def interpolate_kernel(screen2d, coords):
    rows, cols = screen2d.shape
    nb = cols // 128
    q = coords.shape[1]
    chunk = min(2048, q)
    r = jnp.clip(jnp.floor(coords[0] * (rows - 1)), 0.0, rows - 2.0).astype(jnp.int32)
    pair = jnp.concatenate([screen2d, jnp.roll(screen2d, -1, axis=0)], axis=1)
    pair = pair.reshape(rows, 2 * nb, 128)
    out = pl.pallas_call(
        _interp_kernel,
        grid_spec=pltpu.PrefetchScalarGridSpec(
            num_scalar_prefetch=2,
            grid=(q // chunk,),
            in_specs=[pl.BlockSpec((rows, 2 * nb, 128), lambda i, rr, cc: (0, 0, 0))],
            out_specs=pl.BlockSpec((chunk, 1), lambda i, rr, cc: (i, 0)),
        ),
        out_shape=jax.ShapeDtypeStruct((q, 1), jnp.float32),
    )(r, coords, pair)
    return out[:, 0]


def _balanced_kernel(n_ref, r_ref, c_ref, own_ref, partner_ref, o_ref):
    rows = own_ref.shape[0]
    nb = own_ref.shape[1]
    cols = nb * 128
    senders = n_ref.shape[0] // 2
    seg = o_ref.shape[0] // (2 * senders)
    unroll = min(UNROLL, seg)
    sub = lax.broadcasted_iota(jnp.int32, (nb, 128), 0)
    lane = lax.broadcasted_iota(jnp.int32, (nb, 128), 1)
    col = sub * 128 + lane
    rowid = lax.broadcasted_iota(jnp.int32, (8, 128), 0)

    for h, s_ref in enumerate((own_ref, partner_ref)):
        def segment(s, carry, h=h, s_ref=s_ref):
            def group(g, carry2):
                for part in range(unroll // 8):
                    acc = jnp.zeros((8, 128), jnp.float32)
                    first = (h * senders + s) * seg + g * unroll + part * 8
                    for u in range(8):
                        j = first + u
                        rk = r_ref[j]
                        r = rk >> KBITS
                        k = rk & ((1 << KBITS) - 1)
                        lower = s_ref[r]
                        upper = s_ref[r + 1]
                        fy = c_ref[0, j]
                        fx = c_ref[1, j]
                        blend = (1.0 - fy) * lower + fy * upper
                        wx = jnp.where(col == k, 1.0 - fx, jnp.where(col == k + 1, fx, 0.0))
                        row = jnp.sum(blend * wx, axis=0, keepdims=True)
                        acc = jnp.where(rowid == u, row, acc)
                    o_ref[pl.ds(pl.multiple_of(first, 8), 8), :] = jnp.sum(acc, axis=1, keepdims=True)
                return carry2

            trips = (n_ref[h * senders + s] + unroll - 1) // unroll
            lax.fori_loop(0, trips, group, 0)
            return carry

        lax.fori_loop(0, senders, segment, 0)


def interpolate_balanced(own, partner, coords, live):
    rows, nb, _ = own.shape
    cols = nb * 128
    _, halves, senders, seg = coords.shape
    flat = coords.reshape(2, halves * senders * seg)
    y = flat[0] * (rows - 1)
    x = flat[1] * (cols - 1)
    r = jnp.clip(jnp.floor(y), 0.0, rows - 2.0)
    k = jnp.clip(jnp.floor(x), 0.0, cols - 2.0)
    rk = (r.astype(jnp.int32) << KBITS) | k.astype(jnp.int32)
    frac = jnp.stack([y - r, x - k])
    spec = pl.BlockSpec((rows, nb, 128), lambda i, n, rr, cc: (0, 0, 0))
    out = pl.pallas_call(
        _balanced_kernel,
        grid_spec=pltpu.PrefetchScalarGridSpec(
            num_scalar_prefetch=3,
            grid=(1,),
            in_specs=[spec, spec],
            out_specs=pl.BlockSpec((halves * senders * seg, 1), lambda i, n, rr, cc: (0, 0)),
        ),
        out_shape=jax.ShapeDtypeStruct((halves * senders * seg, 1), jnp.float32),
    )(live, rk, frac, own, partner)
    return out.reshape(halves, senders, seg)


def _scatter_kernel(n_ref, d_ref, v_ref, o_ref):
    rows = n_ref.shape[0]
    width = d_ref.shape[0] // rows
    half = width // 2
    step = 8 if width % 8 == 0 else 2
    for row in range(rows):
        def body(i, carry, row=row):
            for u in range(step):
                slot = row * width + i * step + u
                parity = u % 2
                source = ((row ^ parity) * 2 + parity) * half + i * (step // 2) + u // 2
                o_ref[d_ref[slot]] = v_ref[source]
            return carry

        lax.fori_loop(0, (n_ref[row] + step - 1) // step, body, 0)


def scatter_kernel(dest, vals, size):
    live = jnp.sum((dest < size - 1).astype(jnp.int32), axis=1)
    return pl.pallas_call(
        _scatter_kernel,
        grid_spec=pltpu.PrefetchScalarGridSpec(
            num_scalar_prefetch=3,
            grid=(1,),
            in_specs=[],
            out_specs=pl.BlockSpec((size,), lambda i, n, d, v: (0,), memory_space=pltpu.SMEM),
        ),
        out_shape=jax.ShapeDtypeStruct((size,), jnp.float32),
    )(live, dest.reshape(-1), vals.reshape(-1))


def make_phasors(station_rows, iono_rows, directions, freq_ratio):
    delays = (
        station_rows[:, 0:1] * directions[0][None, :]
        + station_rows[:, 1:2] * directions[1][None, :]
    )
    delays = delays + station_rows[:, 2:3] * directions[2][None, :]
    angles = (TWO_PI * freq_ratio)[None, :, None] * delays[:, None, :] + iono_rows[
        :, None, :
    ] / freq_ratio[None, :, None]
    return jnp.concatenate([jnp.cos(angles), jnp.sin(angles)], axis=-1).astype(jnp.bfloat16)


def spectrum(source_flux, spectral_index, freq_ratio, count):
    return (
        source_flux[None, :]
        * jnp.exp(spectral_index[None, :] * jnp.log(freq_ratio)[:, None])
        / math.sqrt(count)
    )


def weight_rows(phasors, intensity):
    sources = intensity.shape[1]
    real_part = (phasors[:, :, :sources].astype(jnp.float32) * intensity[None]).astype(jnp.bfloat16)
    imag_part = (phasors[:, :, sources:].astype(jnp.float32) * intensity[None]).astype(jnp.bfloat16)
    upper_rows = jnp.concatenate([real_part, imag_part], axis=-1)
    lower_rows = jnp.concatenate([imag_part, -real_part], axis=-1)
    return jnp.concatenate([upper_rows, lower_rows], axis=0)


def body(
    screen,
    pierce_coords,
    query_dest,
    positions,
    directions,
    freq_ratio,
    source_flux,
    spectral_index,
):
    groups = lax.axis_size("stn")
    tile_cols = screen.shape[2]
    strip_rows = screen.shape[0] * screen.shape[1]
    values = screen.reshape(-1)
    capacity = query_dest.shape[3]
    stations_local = positions.shape[1]
    local_sources = source_flux.shape[0] // lax.axis_size("chan")
    queries = stations_local * local_sources
    half = capacity // 2
    coords = pierce_coords.reshape(2, groups, capacity)
    dead = query_dest.reshape(groups, capacity) >= queries
    coords = jnp.where(dead[None], -1.0, coords).reshape(2, groups, half, 2)
    swap = lambda a: a.reshape(a.shape[0], groups // 2, 2, half)[:, :, ::-1, :].reshape(a.shape[0], groups, half)
    send = jnp.stack([coords[..., 0], swap(coords[..., 1])], axis=2)
    received = lax.all_to_all(send, "stn", split_axis=1, concat_axis=1, tiled=True)
    kin = received.transpose(0, 2, 1, 3)
    live = jnp.sum((kin[0] >= 0.0).astype(jnp.int32), axis=2).reshape(-1)
    own = screen.reshape(strip_rows, tile_cols // 128, 128)
    partner = lax.ppermute(own, "stn", [(i, i ^ 1) for i in range(groups)])
    sampled = interpolate_balanced(own, partner, kin, live).transpose(1, 0, 2)
    back = lax.all_to_all(sampled, "stn", split_axis=0, concat_axis=0, tiled=True)
    buffer = scatter_kernel(query_dest.reshape(groups, capacity), back, queries + 1)
    own_iono = buffer[:queries].reshape(stations_local, local_sources)
    station_rows = positions.T
    total_stations = stations_local * groups
    channels = freq_ratio.shape[0]
    n_chan = lax.axis_size("chan")
    if channels % groups:
        return _rows_path(own_iono, station_rows, directions, freq_ratio, source_flux, spectral_index)
    iono_phase = lax.all_gather(own_iono, "chan", axis=1, tiled=True)
    packed = jnp.concatenate([iono_phase, station_rows], axis=1)
    gathered = lax.all_gather(packed, "stn", axis=0, tiled=True)
    all_iono = gathered[:, : n_chan * local_sources]
    all_rows = gathered[:, n_chan * local_sources :]
    per_dev = channels // groups
    my_freq = lax.dynamic_slice_in_dim(freq_ratio, lax.axis_index("stn") * per_dev, per_dev)
    phasors = make_phasors(all_rows, all_iono, directions, my_freq)
    intensity = spectrum(source_flux, spectral_index, my_freq, source_flux.shape[0])
    weighted = weight_rows(phasors, intensity)
    columns = jnp.einsum("ack,nck->can", weighted, phasors, preferred_element_type=jnp.float32)
    visible = columns.reshape(per_dev, 2, total_stations, total_stations)
    ids = jnp.arange(total_stations, dtype=jnp.int32)
    cross_only = ids[:, None] != ids[None, :]
    visible = jnp.where(cross_only[None, None], visible, jnp.zeros_like(visible))
    moved = lax.all_to_all(visible.astype(jnp.bfloat16), "stn", split_axis=2, concat_axis=0, tiled=True)
    return moved.astype(jnp.float32)


def _rows_path(own_iono, station_rows, directions, freq_ratio, source_flux, spectral_index):
    groups = lax.axis_size("stn")
    stations_local = station_rows.shape[0]
    iono_phase = lax.all_gather(own_iono, "chan", axis=1, tiled=True)
    own_phasors = make_phasors(station_rows, iono_phase, directions, freq_ratio)
    intensity = spectrum(source_flux, spectral_index, freq_ratio, source_flux.shape[0])
    weighted = weight_rows(own_phasors, intensity)
    total_stations = stations_local * groups
    channels = freq_ratio.shape[0]
    columns = jnp.einsum(
        "ack,nck->can",
        weighted,
        make_phasors(
            lax.all_gather(station_rows, "stn", axis=0, tiled=True),
            lax.all_gather(iono_phase, "stn", axis=0, tiled=True),
            directions,
            freq_ratio,
        ),
        preferred_element_type=jnp.float32,
    )
    visible = columns.reshape(channels, 2, stations_local, total_stations)
    first_row = lax.axis_index("stn") * stations_local
    rows_global = first_row + jnp.arange(stations_local, dtype=jnp.int32)
    cross_only = rows_global[:, None] != jnp.arange(total_stations, dtype=jnp.int32)[None, :]
    return jnp.where(cross_only[None, None], visible, jnp.zeros_like(visible))


def solution(mesh):
    in_specs = (
        P("stn", None, None),
        P(None, "stn", "chan", None, None),
        P("stn", "chan", None, None),
        P(None, "stn"),
        P(),
        P("chan"),
        P(),
        P(),
    )
    out_specs = P("chan", None, "stn", None)
    return jax.shard_map(body, mesh=mesh, in_specs=in_specs, out_specs=out_specs, check_vma=False)
```

```python
import functools
import math

import jax
import jax.numpy as jnp
from jax import lax
from jax.experimental import pallas as pl
from jax.experimental.pallas import tpu as pltpu
from jax.sharding import PartitionSpec as P

TWO_PI = 2.0 * math.pi


def interpolate(values, coords, strip_rows, tile_cols):
    row_pos = coords[0] * (strip_rows - 1)
    col_pos = coords[1] * (tile_cols - 1)
    row_low = jnp.clip(jnp.floor(row_pos), 0.0, strip_rows - 2.0)
    col_low = jnp.clip(jnp.floor(col_pos), 0.0, tile_cols - 2.0)
    frac_y = row_pos - row_low
    frac_x = col_pos - col_low
    corner = row_low.astype(jnp.int32) * tile_cols + col_low.astype(jnp.int32)
    lower_pair = (1.0 - frac_x) * values[corner] + frac_x * values[corner + 1]
    upper_pair = (1.0 - frac_x) * values[corner + tile_cols] + frac_x * values[
        corner + tile_cols + 1
    ]
    return (1.0 - frac_y) * lower_pair + frac_y * upper_pair


UNROLL = 32
KBITS = 12


def _interp_kernel(r_ref, c_ref, s_ref, o_ref):
    rows = s_ref.shape[0]
    two_nb = s_ref.shape[1]
    nb = two_nb // 2
    cols = nb * 128
    chunk = o_ref.shape[0]
    base = pl.program_id(0) * chunk
    sub = lax.broadcasted_iota(jnp.int32, (two_nb, 128), 0)
    lane = lax.broadcasted_iota(jnp.int32, (two_nb, 128), 1)
    col = ((sub % nb) * 128 + lane).astype(jnp.float32)
    upper = sub >= nb
    rowid = lax.broadcasted_iota(jnp.int32, (8, 128), 0)

    def group(g, carry):
        for h in range(UNROLL // 8):
            acc = jnp.zeros((8, 128), jnp.float32)
            for u in range(8):
                j = base + g * UNROLL + h * 8 + u
                t = s_ref[r_ref[j]]
                y = jnp.full((two_nb, 128), c_ref[0, j], jnp.float32) * (rows - 1)
                x = jnp.full((two_nb, 128), c_ref[1, j], jnp.float32) * (cols - 1)
                ry = jnp.clip(jnp.floor(y), 0.0, rows - 2.0)
                kx = jnp.clip(jnp.floor(x), 0.0, cols - 2.0)
                fy = y - ry
                fx = x - kx
                wy = jnp.where(upper, fy, 1.0 - fy)
                wx = jnp.where(col == kx, 1.0 - fx, jnp.where(col == kx + 1.0, fx, 0.0))
                row = jnp.sum(t * (wy * wx), axis=0, keepdims=True)
                acc = jnp.where(rowid == u, row, acc)
            start = pl.multiple_of(g * UNROLL + h * 8, 8)
            o_ref[pl.ds(start, 8), :] = jnp.sum(acc, axis=1, keepdims=True)
        return carry

    lax.fori_loop(0, chunk // UNROLL, group, 0)


def interpolate_kernel(screen2d, coords):
    rows, cols = screen2d.shape
    nb = cols // 128
    q = coords.shape[1]
    chunk = min(2048, q)
    r = jnp.clip(jnp.floor(coords[0] * (rows - 1)), 0.0, rows - 2.0).astype(jnp.int32)
    pair = jnp.concatenate([screen2d, jnp.roll(screen2d, -1, axis=0)], axis=1)
    pair = pair.reshape(rows, 2 * nb, 128)
    out = pl.pallas_call(
        _interp_kernel,
        grid_spec=pltpu.PrefetchScalarGridSpec(
            num_scalar_prefetch=2,
            grid=(q // chunk,),
            in_specs=[pl.BlockSpec((rows, 2 * nb, 128), lambda i, rr, cc: (0, 0, 0))],
            out_specs=pl.BlockSpec((chunk, 1), lambda i, rr, cc: (i, 0)),
        ),
        out_shape=jax.ShapeDtypeStruct((q, 1), jnp.float32),
    )(r, coords, pair)
    return out[:, 0]


def _balanced_kernel(first_part, n_ref, r_ref, c_ref, *refs):
    screens, o_ref = refs[:-1], refs[-1]
    rows = screens[0].shape[0]
    nb = screens[0].shape[1]
    parts_here = len(screens)
    seg = SEG[0]
    senders = o_ref.shape[0] // (parts_here * seg)
    unroll = min(UNROLL, seg)
    sub = lax.broadcasted_iota(jnp.int32, (nb, 128), 0)
    lane = lax.broadcasted_iota(jnp.int32, (nb, 128), 1)
    col = sub * 128 + lane
    rowid = lax.broadcasted_iota(jnp.int32, (8, 128), 0)

    for h, s_ref in enumerate(screens):
        part = first_part + h

        def segment(s, carry, h=h, part=part, s_ref=s_ref):
            def group(g, carry2):
                for piece in range(unroll // 8):
                    acc = jnp.zeros((8, 128), jnp.float32)
                    local = (h * senders + s) * seg + g * unroll + piece * 8
                    start = (part * senders + s) * seg + g * unroll + piece * 8
                    for u in range(8):
                        j = start + u
                        rk = r_ref[j]
                        r = rk >> KBITS
                        k = rk & ((1 << KBITS) - 1)
                        lower = s_ref[r]
                        upper = s_ref[r + 1]
                        fy = c_ref[0, j]
                        fx = c_ref[1, j]
                        blend = (1.0 - fy) * lower + fy * upper
                        wx = jnp.where(col == k, 1.0 - fx, jnp.where(col == k + 1, fx, 0.0))
                        row = jnp.sum(blend * wx, axis=0, keepdims=True)
                        acc = jnp.where(rowid == u, row, acc)
                    o_ref[pl.ds(pl.multiple_of(local, 8), 8), :] = jnp.sum(acc, axis=1, keepdims=True)
                return carry2

            trips = (n_ref[part * senders + s] + unroll - 1) // unroll
            lax.fori_loop(0, trips, group, 0)
            return carry

        lax.fori_loop(0, senders, segment, 0)


SEG = [0]


def interpolate_parts(screens, coords, live, split):
    rows, nb, _ = screens[0].shape
    cols = nb * 128
    _, parts, senders, seg = coords.shape
    SEG[0] = seg
    flat = coords.reshape(2, parts * senders * seg)
    y = flat[0] * (rows - 1)
    x = flat[1] * (cols - 1)
    r = jnp.clip(jnp.floor(y), 0.0, rows - 2.0)
    k = jnp.clip(jnp.floor(x), 0.0, cols - 2.0)
    rk = (r.astype(jnp.int32) << KBITS) | k.astype(jnp.int32)
    frac = jnp.stack([y - r, x - k])
    spec = pl.BlockSpec((rows, nb, 128), lambda i, n, rr, cc: (0, 0, 0))
    outs = []
    for lo, hi in ((0, split), (split, parts)):
        if lo == hi:
            continue
        size = (hi - lo) * senders * seg
        out = pl.pallas_call(
            functools.partial(_balanced_kernel, lo),
            grid_spec=pltpu.PrefetchScalarGridSpec(
                num_scalar_prefetch=3,
                grid=(1,),
                in_specs=[spec] * (hi - lo),
                out_specs=pl.BlockSpec((size, 1), lambda i, n, rr, cc: (0, 0)),
            ),
            out_shape=jax.ShapeDtypeStruct((size, 1), jnp.float32),
        )(live, rk, frac, *screens[lo:hi])
        outs.append(out)
    return jnp.concatenate(outs, axis=0).reshape(parts, senders, seg)


PARTS = [2]


def _scatter_kernel(n_ref, d_ref, v_ref, o_ref):
    rows = n_ref.shape[0]
    width = d_ref.shape[0] // rows
    parts = PARTS[0]
    part_len = width // parts
    step = 8 if width % 8 == 0 else parts
    for row in range(rows):
        def body(i, carry, row=row):
            for u in range(step):
                slot = row * width + i * step + u
                q = u % parts
                source = ((row ^ q) * parts + q) * part_len + i * (step // parts) + u // parts
                o_ref[d_ref[slot]] = v_ref[source]
            return carry

        lax.fori_loop(0, (n_ref[row] + step - 1) // step, body, 0)


def scatter_kernel(dest, vals, size):
    live = jnp.sum((dest < size - 1).astype(jnp.int32), axis=1)
    return pl.pallas_call(
        _scatter_kernel,
        grid_spec=pltpu.PrefetchScalarGridSpec(
            num_scalar_prefetch=3,
            grid=(1,),
            in_specs=[],
            out_specs=pl.BlockSpec((size,), lambda i, n, d, v: (0,), memory_space=pltpu.SMEM),
        ),
        out_shape=jax.ShapeDtypeStruct((size,), jnp.float32),
    )(live, dest.reshape(-1), vals.reshape(-1))


def make_phasors(station_rows, iono_rows, directions, freq_ratio):
    delays = (
        station_rows[:, 0:1] * directions[0][None, :]
        + station_rows[:, 1:2] * directions[1][None, :]
    )
    delays = delays + station_rows[:, 2:3] * directions[2][None, :]
    angles = (TWO_PI * freq_ratio)[None, :, None] * delays[:, None, :] + iono_rows[
        :, None, :
    ] / freq_ratio[None, :, None]
    return jnp.concatenate([jnp.cos(angles), jnp.sin(angles)], axis=-1).astype(jnp.bfloat16)


def spectrum(source_flux, spectral_index, freq_ratio, count):
    return (
        source_flux[None, :]
        * jnp.exp(spectral_index[None, :] * jnp.log(freq_ratio)[:, None])
        / math.sqrt(count)
    )


def weight_rows(phasors, intensity):
    sources = intensity.shape[1]
    real_part = (phasors[:, :, :sources].astype(jnp.float32) * intensity[None]).astype(jnp.bfloat16)
    imag_part = (phasors[:, :, sources:].astype(jnp.float32) * intensity[None]).astype(jnp.bfloat16)
    upper_rows = jnp.concatenate([real_part, imag_part], axis=-1)
    lower_rows = jnp.concatenate([imag_part, -real_part], axis=-1)
    return jnp.concatenate([upper_rows, lower_rows], axis=0)


def body(
    screen,
    pierce_coords,
    query_dest,
    positions,
    directions,
    freq_ratio,
    source_flux,
    spectral_index,
):
    groups = lax.axis_size("stn")
    tile_cols = screen.shape[2]
    strip_rows = screen.shape[0] * screen.shape[1]
    values = screen.reshape(-1)
    capacity = query_dest.shape[3]
    stations_local = positions.shape[1]
    local_sources = source_flux.shape[0] // lax.axis_size("chan")
    queries = stations_local * local_sources
    parts = 4 if groups % 4 == 0 and capacity % (4 * 8) == 0 else 2
    part_len = capacity // parts
    coords = pierce_coords.reshape(2, groups, capacity)
    dead = query_dest.reshape(groups, capacity) >= queries
    coords = jnp.where(dead[None], -1.0, coords).reshape(2, groups // parts, parts, part_len, parts)

    def to_dest(q):
        piece = coords[..., q]
        return jnp.stack([piece[:, :, d ^ q, :] for d in range(parts)], axis=2)

    send = jnp.stack([to_dest(q) for q in range(parts)], axis=3).reshape(2, groups, parts, part_len)
    received = lax.all_to_all(send, "stn", split_axis=1, concat_axis=1, tiled=True)
    kin = received.transpose(0, 2, 1, 3)
    live = jnp.sum((kin[0] >= 0.0).astype(jnp.int32), axis=2).reshape(-1)
    own = screen.reshape(strip_rows, tile_cols // 128, 128)
    screens = [own] + [
        lax.ppermute(own, "stn", [(i, i ^ q) for i in range(groups)]) for q in range(1, parts)
    ]
    sampled = interpolate_parts(screens, kin, live, 2).transpose(1, 0, 2)
    back = lax.all_to_all(sampled, "stn", split_axis=0, concat_axis=0, tiled=True)
    PARTS[0] = parts
    buffer = scatter_kernel(query_dest.reshape(groups, capacity), back, queries + 1)
    own_iono = buffer[:queries].reshape(stations_local, local_sources)
    station_rows = positions.T
    total_stations = stations_local * groups
    channels = freq_ratio.shape[0]
    n_chan = lax.axis_size("chan")
    if channels % groups:
        return _rows_path(own_iono, station_rows, directions, freq_ratio, source_flux, spectral_index)
    iono_phase = lax.all_gather(own_iono, "chan", axis=1, tiled=True)
    packed = jnp.concatenate([iono_phase, station_rows], axis=1)
    gathered = lax.all_gather(packed, "stn", axis=0, tiled=True)
    all_iono = gathered[:, : n_chan * local_sources]
    all_rows = gathered[:, n_chan * local_sources :]
    per_dev = channels // groups
    my_freq = lax.dynamic_slice_in_dim(freq_ratio, lax.axis_index("stn") * per_dev, per_dev)
    phasors = make_phasors(all_rows, all_iono, directions, my_freq)
    intensity = spectrum(source_flux, spectral_index, my_freq, source_flux.shape[0])
    weighted = weight_rows(phasors, intensity)
    columns = jnp.einsum("ack,nck->can", weighted, phasors, preferred_element_type=jnp.float32)
    visible = columns.reshape(per_dev, 2, total_stations, total_stations)
    ids = jnp.arange(total_stations, dtype=jnp.int32)
    cross_only = ids[:, None] != ids[None, :]
    visible = jnp.where(cross_only[None, None], visible, jnp.zeros_like(visible))
    moved = lax.all_to_all(visible.astype(jnp.bfloat16), "stn", split_axis=2, concat_axis=0, tiled=True)
    return moved.astype(jnp.float32)


def _rows_path(own_iono, station_rows, directions, freq_ratio, source_flux, spectral_index):
    groups = lax.axis_size("stn")
    stations_local = station_rows.shape[0]
    iono_phase = lax.all_gather(own_iono, "chan", axis=1, tiled=True)
    own_phasors = make_phasors(station_rows, iono_phase, directions, freq_ratio)
    intensity = spectrum(source_flux, spectral_index, freq_ratio, source_flux.shape[0])
    weighted = weight_rows(own_phasors, intensity)
    total_stations = stations_local * groups
    channels = freq_ratio.shape[0]
    columns = jnp.einsum(
        "ack,nck->can",
        weighted,
        make_phasors(
            lax.all_gather(station_rows, "stn", axis=0, tiled=True),
            lax.all_gather(iono_phase, "stn", axis=0, tiled=True),
            directions,
            freq_ratio,
        ),
        preferred_element_type=jnp.float32,
    )
    visible = columns.reshape(channels, 2, stations_local, total_stations)
    first_row = lax.axis_index("stn") * stations_local
    rows_global = first_row + jnp.arange(stations_local, dtype=jnp.int32)
    cross_only = rows_global[:, None] != jnp.arange(total_stations, dtype=jnp.int32)[None, :]
    return jnp.where(cross_only[None, None], visible, jnp.zeros_like(visible))


def solution(mesh):
    in_specs = (
        P("stn", None, None),
        P(None, "stn", "chan", None, None),
        P("stn", "chan", None, None),
        P(None, "stn"),
        P(),
        P("chan"),
        P(),
        P(),
    )
    out_specs = P("chan", None, "stn", None)
    return jax.shard_map(body, mesh=mesh, in_specs=in_specs, out_specs=out_specs, check_vma=False)
```

```python
import math

import jax
import jax.numpy as jnp
from jax import lax
from jax.experimental import pallas as pl
from jax.experimental.pallas import tpu as pltpu
from jax.sharding import PartitionSpec as P

TWO_PI = 2.0 * math.pi


def interpolate(values, coords, strip_rows, tile_cols):
    row_pos = coords[0] * (strip_rows - 1)
    col_pos = coords[1] * (tile_cols - 1)
    row_low = jnp.clip(jnp.floor(row_pos), 0.0, strip_rows - 2.0)
    col_low = jnp.clip(jnp.floor(col_pos), 0.0, tile_cols - 2.0)
    frac_y = row_pos - row_low
    frac_x = col_pos - col_low
    corner = row_low.astype(jnp.int32) * tile_cols + col_low.astype(jnp.int32)
    lower_pair = (1.0 - frac_x) * values[corner] + frac_x * values[corner + 1]
    upper_pair = (1.0 - frac_x) * values[corner + tile_cols] + frac_x * values[
        corner + tile_cols + 1
    ]
    return (1.0 - frac_y) * lower_pair + frac_y * upper_pair


UNROLL = 32
KBITS = 12


def _interp_kernel(r_ref, c_ref, s_ref, o_ref):
    rows = s_ref.shape[0]
    two_nb = s_ref.shape[1]
    nb = two_nb // 2
    cols = nb * 128
    chunk = o_ref.shape[0]
    base = pl.program_id(0) * chunk
    sub = lax.broadcasted_iota(jnp.int32, (two_nb, 128), 0)
    lane = lax.broadcasted_iota(jnp.int32, (two_nb, 128), 1)
    col = ((sub % nb) * 128 + lane).astype(jnp.float32)
    upper = sub >= nb
    rowid = lax.broadcasted_iota(jnp.int32, (8, 128), 0)

    def group(g, carry):
        for h in range(UNROLL // 8):
            acc = jnp.zeros((8, 128), jnp.float32)
            for u in range(8):
                j = base + g * UNROLL + h * 8 + u
                t = s_ref[r_ref[j]]
                y = jnp.full((two_nb, 128), c_ref[0, j], jnp.float32) * (rows - 1)
                x = jnp.full((two_nb, 128), c_ref[1, j], jnp.float32) * (cols - 1)
                ry = jnp.clip(jnp.floor(y), 0.0, rows - 2.0)
                kx = jnp.clip(jnp.floor(x), 0.0, cols - 2.0)
                fy = y - ry
                fx = x - kx
                wy = jnp.where(upper, fy, 1.0 - fy)
                wx = jnp.where(col == kx, 1.0 - fx, jnp.where(col == kx + 1.0, fx, 0.0))
                row = jnp.sum(t * (wy * wx), axis=0, keepdims=True)
                acc = jnp.where(rowid == u, row, acc)
            start = pl.multiple_of(g * UNROLL + h * 8, 8)
            o_ref[pl.ds(start, 8), :] = jnp.sum(acc, axis=1, keepdims=True)
        return carry

    lax.fori_loop(0, chunk // UNROLL, group, 0)


def interpolate_kernel(screen2d, coords):
    rows, cols = screen2d.shape
    nb = cols // 128
    q = coords.shape[1]
    chunk = min(2048, q)
    r = jnp.clip(jnp.floor(coords[0] * (rows - 1)), 0.0, rows - 2.0).astype(jnp.int32)
    pair = jnp.concatenate([screen2d, jnp.roll(screen2d, -1, axis=0)], axis=1)
    pair = pair.reshape(rows, 2 * nb, 128)
    out = pl.pallas_call(
        _interp_kernel,
        grid_spec=pltpu.PrefetchScalarGridSpec(
            num_scalar_prefetch=2,
            grid=(q // chunk,),
            in_specs=[pl.BlockSpec((rows, 2 * nb, 128), lambda i, rr, cc: (0, 0, 0))],
            out_specs=pl.BlockSpec((chunk, 1), lambda i, rr, cc: (i, 0)),
        ),
        out_shape=jax.ShapeDtypeStruct((q, 1), jnp.float32),
    )(r, coords, pair)
    return out[:, 0]


def _balanced_kernel(n_ref, r_ref, c_ref, own_ref, partner_ref, o_ref):
    rows = own_ref.shape[0]
    nb = own_ref.shape[1]
    cols = nb * 128
    senders = n_ref.shape[0] // 2
    seg = o_ref.shape[0] // (2 * senders)
    unroll = min(UNROLL, seg)
    sub = lax.broadcasted_iota(jnp.int32, (nb, 128), 0)
    lane = lax.broadcasted_iota(jnp.int32, (nb, 128), 1)
    col = sub * 128 + lane
    rowid = lax.broadcasted_iota(jnp.int32, (8, 128), 0)

    for h, s_ref in enumerate((own_ref, partner_ref)):
        def segment(s, carry, h=h, s_ref=s_ref):
            def group(g, carry2):
                for part in range(unroll // 8):
                    acc = jnp.zeros((8, 128), jnp.float32)
                    first = (h * senders + s) * seg + g * unroll + part * 8
                    for u in range(8):
                        j = first + u
                        rk = r_ref[j]
                        r = rk >> KBITS
                        k = rk & ((1 << KBITS) - 1)
                        lower = s_ref[r]
                        upper = s_ref[r + 1]
                        fy = c_ref[0, j]
                        fx = c_ref[1, j]
                        blend = (1.0 - fy) * lower + fy * upper
                        wx = jnp.where(col == k, 1.0 - fx, jnp.where(col == k + 1, fx, 0.0))
                        row = jnp.sum(blend * wx, axis=0, keepdims=True)
                        acc = jnp.where(rowid == u, row, acc)
                    o_ref[pl.ds(pl.multiple_of(first, 8), 8), :] = jnp.sum(acc, axis=1, keepdims=True)
                return carry2

            trips = (n_ref[h * senders + s] + unroll - 1) // unroll
            lax.fori_loop(0, trips, group, 0)
            return carry

        lax.fori_loop(0, senders, segment, 0)


def interpolate_balanced(own, partner, coords, live):
    rows, nb, _ = own.shape
    cols = nb * 128
    _, halves, senders, seg = coords.shape
    flat = coords.reshape(2, halves * senders * seg)
    y = flat[0] * (rows - 1)
    x = flat[1] * (cols - 1)
    r = jnp.clip(jnp.floor(y), 0.0, rows - 2.0)
    k = jnp.clip(jnp.floor(x), 0.0, cols - 2.0)
    rk = (r.astype(jnp.int32) << KBITS) | k.astype(jnp.int32)
    frac = jnp.stack([y - r, x - k])
    spec = pl.BlockSpec((rows, nb, 128), lambda i, n, rr, cc: (0, 0, 0))
    out = pl.pallas_call(
        _balanced_kernel,
        grid_spec=pltpu.PrefetchScalarGridSpec(
            num_scalar_prefetch=3,
            grid=(1,),
            in_specs=[spec, spec],
            out_specs=pl.BlockSpec((halves * senders * seg, 1), lambda i, n, rr, cc: (0, 0)),
        ),
        out_shape=jax.ShapeDtypeStruct((halves * senders * seg, 1), jnp.float32),
    )(live, rk, frac, own, partner)
    return out.reshape(halves, senders, seg)


def _scatter_kernel(n_ref, d_ref, v_ref, o_ref):
    rows = n_ref.shape[0]
    width = d_ref.shape[0] // rows
    half = width // 2
    step = 16 if width % 16 == 0 else 2
    for row in range(rows):
        def body(i, carry, row=row):
            for u in range(step):
                slot = row * width + i * step + u
                parity = u % 2
                source = ((row ^ parity) * 2 + parity) * half + i * (step // 2) + u // 2
                o_ref[d_ref[slot]] = v_ref[source]
            return carry

        lax.fori_loop(0, (n_ref[row] + step - 1) // step, body, 0)


def scatter_kernel(dest, vals, size):
    live = jnp.sum((dest < size - 1).astype(jnp.int32), axis=1)
    return pl.pallas_call(
        _scatter_kernel,
        grid_spec=pltpu.PrefetchScalarGridSpec(
            num_scalar_prefetch=3,
            grid=(1,),
            in_specs=[],
            out_specs=pl.BlockSpec((size,), lambda i, n, d, v: (0,), memory_space=pltpu.SMEM),
        ),
        out_shape=jax.ShapeDtypeStruct((size,), jnp.float32),
    )(live, dest.reshape(-1), vals.reshape(-1))


def make_phasors(station_rows, iono_rows, directions, freq_ratio):
    delays = (
        station_rows[:, 0:1] * directions[0][None, :]
        + station_rows[:, 1:2] * directions[1][None, :]
    )
    delays = delays + station_rows[:, 2:3] * directions[2][None, :]
    angles = (TWO_PI * freq_ratio)[None, :, None] * delays[:, None, :] + iono_rows[
        :, None, :
    ] / freq_ratio[None, :, None]
    return jnp.concatenate([jnp.cos(angles), jnp.sin(angles)], axis=-1).astype(jnp.bfloat16)


def spectrum(source_flux, spectral_index, freq_ratio, count):
    return (
        source_flux[None, :]
        * jnp.exp(spectral_index[None, :] * jnp.log(freq_ratio)[:, None])
        / math.sqrt(count)
    )


def weight_rows(phasors, intensity):
    sources = intensity.shape[1]
    real_part = (phasors[:, :, :sources].astype(jnp.float32) * intensity[None]).astype(jnp.bfloat16)
    imag_part = (phasors[:, :, sources:].astype(jnp.float32) * intensity[None]).astype(jnp.bfloat16)
    upper_rows = jnp.concatenate([real_part, imag_part], axis=-1)
    lower_rows = jnp.concatenate([imag_part, -real_part], axis=-1)
    return jnp.concatenate([upper_rows, lower_rows], axis=0)


def body(
    screen,
    pierce_coords,
    query_dest,
    positions,
    directions,
    freq_ratio,
    source_flux,
    spectral_index,
):
    groups = lax.axis_size("stn")
    tile_cols = screen.shape[2]
    strip_rows = screen.shape[0] * screen.shape[1]
    values = screen.reshape(-1)
    capacity = query_dest.shape[3]
    stations_local = positions.shape[1]
    local_sources = source_flux.shape[0] // lax.axis_size("chan")
    queries = stations_local * local_sources
    half = capacity // 2
    coords = pierce_coords.reshape(2, groups, capacity)
    dead = query_dest.reshape(groups, capacity) >= queries
    coords = jnp.where(dead[None], -1.0, coords).reshape(2, groups, half, 2)
    swap = lambda a: a.reshape(a.shape[0], groups // 2, 2, half)[:, :, ::-1, :].reshape(a.shape[0], groups, half)
    send = jnp.stack([coords[..., 0], swap(coords[..., 1])], axis=2)
    received = lax.all_to_all(send, "stn", split_axis=1, concat_axis=1, tiled=True)
    kin = received.transpose(0, 2, 1, 3)
    live = jnp.sum((kin[0] >= 0.0).astype(jnp.int32), axis=2).reshape(-1)
    own = screen.reshape(strip_rows, tile_cols // 128, 128)
    partner = lax.ppermute(own, "stn", [(i, i ^ 1) for i in range(groups)])
    sampled = interpolate_balanced(own, partner, kin, live).transpose(1, 0, 2)
    back = lax.all_to_all(sampled, "stn", split_axis=0, concat_axis=0, tiled=True)
    buffer = scatter_kernel(query_dest.reshape(groups, capacity), back, queries + 1)
    own_iono = buffer[:queries].reshape(stations_local, local_sources)
    station_rows = positions.T
    total_stations = stations_local * groups
    channels = freq_ratio.shape[0]
    n_chan = lax.axis_size("chan")
    if channels % groups:
        return _rows_path(own_iono, station_rows, directions, freq_ratio, source_flux, spectral_index)
    packed = jnp.concatenate([own_iono, station_rows], axis=1)
    gathered = lax.all_gather(packed, "stn", axis=0, tiled=True)
    all_rows = gathered[:, local_sources:]
    all_iono = lax.all_gather(gathered[:, :local_sources], "chan", axis=1, tiled=True)
    per_dev = channels // groups
    my_freq = lax.dynamic_slice_in_dim(freq_ratio, lax.axis_index("stn") * per_dev, per_dev)
    phasors = make_phasors(all_rows, all_iono, directions, my_freq)
    intensity = spectrum(source_flux, spectral_index, my_freq, source_flux.shape[0])
    weighted = weight_rows(phasors, intensity)
    columns = jnp.einsum("ack,nck->can", weighted, phasors, preferred_element_type=jnp.float32)
    visible = columns.reshape(per_dev, 2, total_stations, total_stations)
    ids = jnp.arange(total_stations, dtype=jnp.int32)
    cross_only = ids[:, None] != ids[None, :]
    visible = jnp.where(cross_only[None, None], visible, jnp.zeros_like(visible))
    moved = lax.all_to_all(visible.astype(jnp.bfloat16), "stn", split_axis=2, concat_axis=0, tiled=True)
    return moved.astype(jnp.float32)


def _rows_path(own_iono, station_rows, directions, freq_ratio, source_flux, spectral_index):
    groups = lax.axis_size("stn")
    stations_local = station_rows.shape[0]
    iono_phase = lax.all_gather(own_iono, "chan", axis=1, tiled=True)
    own_phasors = make_phasors(station_rows, iono_phase, directions, freq_ratio)
    intensity = spectrum(source_flux, spectral_index, freq_ratio, source_flux.shape[0])
    weighted = weight_rows(own_phasors, intensity)
    total_stations = stations_local * groups
    channels = freq_ratio.shape[0]
    columns = jnp.einsum(
        "ack,nck->can",
        weighted,
        make_phasors(
            lax.all_gather(station_rows, "stn", axis=0, tiled=True),
            lax.all_gather(iono_phase, "stn", axis=0, tiled=True),
            directions,
            freq_ratio,
        ),
        preferred_element_type=jnp.float32,
    )
    visible = columns.reshape(channels, 2, stations_local, total_stations)
    first_row = lax.axis_index("stn") * stations_local
    rows_global = first_row + jnp.arange(stations_local, dtype=jnp.int32)
    cross_only = rows_global[:, None] != jnp.arange(total_stations, dtype=jnp.int32)[None, :]
    return jnp.where(cross_only[None, None], visible, jnp.zeros_like(visible))


def solution(mesh):
    in_specs = (
        P("stn", None, None),
        P(None, "stn", "chan", None, None),
        P("stn", "chan", None, None),
        P(None, "stn"),
        P(),
        P("chan"),
        P(),
        P(),
    )
    out_specs = P("chan", None, "stn", None)
    return jax.shard_map(body, mesh=mesh, in_specs=in_specs, out_specs=out_specs, check_vma=False)
```

```python
import functools
import math

import jax
import jax.numpy as jnp
from jax import lax
from jax.experimental import pallas as pl
from jax.experimental.pallas import tpu as pltpu
from jax.sharding import PartitionSpec as P

TWO_PI = 2.0 * math.pi


def interpolate(values, coords, strip_rows, tile_cols):
    row_pos = coords[0] * (strip_rows - 1)
    col_pos = coords[1] * (tile_cols - 1)
    row_low = jnp.clip(jnp.floor(row_pos), 0.0, strip_rows - 2.0)
    col_low = jnp.clip(jnp.floor(col_pos), 0.0, tile_cols - 2.0)
    frac_y = row_pos - row_low
    frac_x = col_pos - col_low
    corner = row_low.astype(jnp.int32) * tile_cols + col_low.astype(jnp.int32)
    lower_pair = (1.0 - frac_x) * values[corner] + frac_x * values[corner + 1]
    upper_pair = (1.0 - frac_x) * values[corner + tile_cols] + frac_x * values[
        corner + tile_cols + 1
    ]
    return (1.0 - frac_y) * lower_pair + frac_y * upper_pair


UNROLL = 32
KBITS = 12


def _interp_kernel(r_ref, c_ref, s_ref, o_ref):
    rows = s_ref.shape[0]
    two_nb = s_ref.shape[1]
    nb = two_nb // 2
    cols = nb * 128
    chunk = o_ref.shape[0]
    base = pl.program_id(0) * chunk
    sub = lax.broadcasted_iota(jnp.int32, (two_nb, 128), 0)
    lane = lax.broadcasted_iota(jnp.int32, (two_nb, 128), 1)
    col = ((sub % nb) * 128 + lane).astype(jnp.float32)
    upper = sub >= nb
    rowid = lax.broadcasted_iota(jnp.int32, (8, 128), 0)

    def group(g, carry):
        for h in range(UNROLL // 8):
            acc = jnp.zeros((8, 128), jnp.float32)
            for u in range(8):
                j = base + g * UNROLL + h * 8 + u
                t = s_ref[r_ref[j]]
                y = jnp.full((two_nb, 128), c_ref[0, j], jnp.float32) * (rows - 1)
                x = jnp.full((two_nb, 128), c_ref[1, j], jnp.float32) * (cols - 1)
                ry = jnp.clip(jnp.floor(y), 0.0, rows - 2.0)
                kx = jnp.clip(jnp.floor(x), 0.0, cols - 2.0)
                fy = y - ry
                fx = x - kx
                wy = jnp.where(upper, fy, 1.0 - fy)
                wx = jnp.where(col == kx, 1.0 - fx, jnp.where(col == kx + 1.0, fx, 0.0))
                row = jnp.sum(t * (wy * wx), axis=0, keepdims=True)
                acc = jnp.where(rowid == u, row, acc)
            start = pl.multiple_of(g * UNROLL + h * 8, 8)
            o_ref[pl.ds(start, 8), :] = jnp.sum(acc, axis=1, keepdims=True)
        return carry

    lax.fori_loop(0, chunk // UNROLL, group, 0)


def interpolate_kernel(screen2d, coords):
    rows, cols = screen2d.shape
    nb = cols // 128
    q = coords.shape[1]
    chunk = min(2048, q)
    r = jnp.clip(jnp.floor(coords[0] * (rows - 1)), 0.0, rows - 2.0).astype(jnp.int32)
    pair = jnp.concatenate([screen2d, jnp.roll(screen2d, -1, axis=0)], axis=1)
    pair = pair.reshape(rows, 2 * nb, 128)
    out = pl.pallas_call(
        _interp_kernel,
        grid_spec=pltpu.PrefetchScalarGridSpec(
            num_scalar_prefetch=2,
            grid=(q // chunk,),
            in_specs=[pl.BlockSpec((rows, 2 * nb, 128), lambda i, rr, cc: (0, 0, 0))],
            out_specs=pl.BlockSpec((chunk, 1), lambda i, rr, cc: (i, 0)),
        ),
        out_shape=jax.ShapeDtypeStruct((q, 1), jnp.float32),
    )(r, coords, pair)
    return out[:, 0]


def _balanced_kernel(first_part, n_ref, r_ref, c_ref, *refs):
    screens, o_ref = refs[:-1], refs[-1]
    rows = screens[0].shape[0]
    nb = screens[0].shape[1]
    parts_here = len(screens)
    seg = SEG[0]
    senders = o_ref.shape[0] // (parts_here * seg)
    unroll = min(UNROLL, seg)
    sub = lax.broadcasted_iota(jnp.int32, (nb, 128), 0)
    lane = lax.broadcasted_iota(jnp.int32, (nb, 128), 1)
    col = sub * 128 + lane
    rowid = lax.broadcasted_iota(jnp.int32, (8, 128), 0)

    for h, s_ref in enumerate(screens):
        part = first_part + h

        def segment(s, carry, h=h, part=part, s_ref=s_ref):
            def group(g, carry2):
                for piece in range(unroll // 8):
                    acc = jnp.zeros((8, 128), jnp.float32)
                    local = (h * senders + s) * seg + g * unroll + piece * 8
                    start = (part * senders + s) * seg + g * unroll + piece * 8
                    for u in range(8):
                        j = start + u
                        rk = r_ref[j]
                        r = rk >> KBITS
                        k = rk & ((1 << KBITS) - 1)
                        lower = s_ref[r]
                        upper = s_ref[r + 1]
                        fy = c_ref[0, j]
                        fx = c_ref[1, j]
                        blend = (1.0 - fy) * lower + fy * upper
                        wx = jnp.where(col == k, 1.0 - fx, jnp.where(col == k + 1, fx, 0.0))
                        row = jnp.sum(blend * wx, axis=0, keepdims=True)
                        acc = jnp.where(rowid == u, row, acc)
                    o_ref[pl.ds(pl.multiple_of(local, 8), 8), :] = jnp.sum(acc, axis=1, keepdims=True)
                return carry2

            trips = (n_ref[part * senders + s] + unroll - 1) // unroll
            lax.fori_loop(0, trips, group, 0)
            return carry

        lax.fori_loop(0, senders, segment, 0)


SEG = [0]


def interpolate_parts(screens, coords, live, later):
    rows, nb, _ = screens[0].shape
    cols = nb * 128
    _, parts, senders, seg = coords.shape
    SEG[0] = seg
    flat = coords.reshape(2, parts * senders * seg)
    y = flat[0] * (rows - 1)
    x = flat[1] * (cols - 1)
    r = jnp.clip(jnp.floor(y), 0.0, rows - 2.0)
    k = jnp.clip(jnp.floor(x), 0.0, cols - 2.0)
    rk = (r.astype(jnp.int32) << KBITS) | k.astype(jnp.int32)
    frac = jnp.stack([y - r, x - k])
    spec = pl.BlockSpec((rows, nb, 128), lambda i, n, rr, cc: (0, 0, 0))
    outs = []
    lo = 0
    while lo < parts:
        if lo:
            screens = later(outs[-1])
        hi = lo + len(screens)
        size = (hi - lo) * senders * seg
        out = pl.pallas_call(
            functools.partial(_balanced_kernel, lo),
            grid_spec=pltpu.PrefetchScalarGridSpec(
                num_scalar_prefetch=3,
                grid=(1,),
                in_specs=[spec] * (hi - lo),
                out_specs=pl.BlockSpec((size, 1), lambda i, n, rr, cc: (0, 0)),
            ),
            out_shape=jax.ShapeDtypeStruct((size, 1), jnp.float32),
        )(live, rk, frac, *screens)
        outs.append(out)
        lo = hi
    return jnp.concatenate(outs, axis=0).reshape(parts, senders, seg)


PARTS = [2]


def _scatter_kernel(n_ref, d_ref, v_ref, o_ref):
    rows = n_ref.shape[0]
    width = d_ref.shape[0] // rows
    parts = PARTS[0]
    part_len = width // parts
    step = 8 if width % 8 == 0 else parts
    for row in range(rows):
        def body(i, carry, row=row):
            for u in range(step):
                slot = row * width + i * step + u
                q = u % parts
                source = ((row ^ q) * parts + q) * part_len + i * (step // parts) + u // parts
                o_ref[d_ref[slot]] = v_ref[source]
            return carry

        lax.fori_loop(0, (n_ref[row] + step - 1) // step, body, 0)


def scatter_kernel(dest, vals, size):
    live = jnp.sum((dest < size - 1).astype(jnp.int32), axis=1)
    return pl.pallas_call(
        _scatter_kernel,
        grid_spec=pltpu.PrefetchScalarGridSpec(
            num_scalar_prefetch=3,
            grid=(1,),
            in_specs=[],
            out_specs=pl.BlockSpec((size,), lambda i, n, d, v: (0,), memory_space=pltpu.SMEM),
        ),
        out_shape=jax.ShapeDtypeStruct((size,), jnp.float32),
    )(live, dest.reshape(-1), vals.reshape(-1))


def make_phasors(station_rows, iono_rows, directions, freq_ratio):
    delays = (
        station_rows[:, 0:1] * directions[0][None, :]
        + station_rows[:, 1:2] * directions[1][None, :]
    )
    delays = delays + station_rows[:, 2:3] * directions[2][None, :]
    angles = (TWO_PI * freq_ratio)[None, :, None] * delays[:, None, :] + iono_rows[
        :, None, :
    ] / freq_ratio[None, :, None]
    return jnp.concatenate([jnp.cos(angles), jnp.sin(angles)], axis=-1).astype(jnp.bfloat16)


def spectrum(source_flux, spectral_index, freq_ratio, count):
    return (
        source_flux[None, :]
        * jnp.exp(spectral_index[None, :] * jnp.log(freq_ratio)[:, None])
        / math.sqrt(count)
    )


def weight_rows(phasors, intensity):
    sources = intensity.shape[1]
    real_part = (phasors[:, :, :sources].astype(jnp.float32) * intensity[None]).astype(jnp.bfloat16)
    imag_part = (phasors[:, :, sources:].astype(jnp.float32) * intensity[None]).astype(jnp.bfloat16)
    upper_rows = jnp.concatenate([real_part, imag_part], axis=-1)
    lower_rows = jnp.concatenate([imag_part, -real_part], axis=-1)
    return jnp.concatenate([upper_rows, lower_rows], axis=0)


def body(
    screen,
    pierce_coords,
    query_dest,
    positions,
    directions,
    freq_ratio,
    source_flux,
    spectral_index,
):
    groups = lax.axis_size("stn")
    tile_cols = screen.shape[2]
    strip_rows = screen.shape[0] * screen.shape[1]
    values = screen.reshape(-1)
    capacity = query_dest.shape[3]
    stations_local = positions.shape[1]
    local_sources = source_flux.shape[0] // lax.axis_size("chan")
    queries = stations_local * local_sources
    parts = 4 if groups % 4 == 0 and capacity % (4 * 8) == 0 else 2
    part_len = capacity // parts
    coords = pierce_coords.reshape(2, groups, capacity)
    dead = query_dest.reshape(groups, capacity) >= queries
    coords = jnp.where(dead[None], -1.0, coords).reshape(2, groups // parts, parts, part_len, parts)

    def to_dest(q):
        piece = coords[..., q]
        return jnp.stack([piece[:, :, d ^ q, :] for d in range(parts)], axis=2)

    send = jnp.stack([to_dest(q) for q in range(parts)], axis=3).reshape(2, groups, parts, part_len)
    received = lax.all_to_all(send, "stn", split_axis=1, concat_axis=1, tiled=True)
    kin = received.transpose(0, 2, 1, 3)
    own = screen.reshape(strip_rows, tile_cols // 128, 128)
    swap_core = [(i, i ^ 1) for i in range(groups)]
    screens = [own, lax.ppermute(own, "stn", swap_core)]
    later = None
    if parts == 4:
        late, kin = lax.optimization_barrier((own, kin))
        far = lax.ppermute(late, "stn", [(i, i ^ 2) for i in range(groups)])

        def later(first_out):
            far_ready, _ = lax.optimization_barrier((far, first_out))
            return [far_ready, lax.ppermute(far_ready, "stn", swap_core)]
    live = jnp.sum((kin[0] >= 0.0).astype(jnp.int32), axis=2).reshape(-1)
    sampled = interpolate_parts(screens, kin, live, later).transpose(1, 0, 2)
    back = lax.all_to_all(sampled, "stn", split_axis=0, concat_axis=0, tiled=True)
    PARTS[0] = parts
    buffer = scatter_kernel(query_dest.reshape(groups, capacity), back, queries + 1)
    own_iono = buffer[:queries].reshape(stations_local, local_sources)
    station_rows = positions.T
    total_stations = stations_local * groups
    channels = freq_ratio.shape[0]
    n_chan = lax.axis_size("chan")
    if channels % groups:
        return _rows_path(own_iono, station_rows, directions, freq_ratio, source_flux, spectral_index)
    iono_phase = lax.all_gather(own_iono, "chan", axis=1, tiled=True)
    packed = jnp.concatenate([iono_phase, station_rows], axis=1)
    gathered = lax.all_gather(packed, "stn", axis=0, tiled=True)
    all_iono = gathered[:, : n_chan * local_sources]
    all_rows = gathered[:, n_chan * local_sources :]
    per_dev = channels // groups
    my_freq = lax.dynamic_slice_in_dim(freq_ratio, lax.axis_index("stn") * per_dev, per_dev)
    phasors = make_phasors(all_rows, all_iono, directions, my_freq)
    intensity = spectrum(source_flux, spectral_index, my_freq, source_flux.shape[0])
    weighted = weight_rows(phasors, intensity)
    columns = jnp.einsum("ack,nck->can", weighted, phasors, preferred_element_type=jnp.float32)
    visible = columns.reshape(per_dev, 2, total_stations, total_stations)
    ids = jnp.arange(total_stations, dtype=jnp.int32)
    cross_only = ids[:, None] != ids[None, :]
    visible = jnp.where(cross_only[None, None], visible, jnp.zeros_like(visible))
    moved = lax.all_to_all(visible.astype(jnp.bfloat16), "stn", split_axis=2, concat_axis=0, tiled=True)
    return moved.astype(jnp.float32)


def _rows_path(own_iono, station_rows, directions, freq_ratio, source_flux, spectral_index):
    groups = lax.axis_size("stn")
    stations_local = station_rows.shape[0]
    iono_phase = lax.all_gather(own_iono, "chan", axis=1, tiled=True)
    own_phasors = make_phasors(station_rows, iono_phase, directions, freq_ratio)
    intensity = spectrum(source_flux, spectral_index, freq_ratio, source_flux.shape[0])
    weighted = weight_rows(own_phasors, intensity)
    total_stations = stations_local * groups
    channels = freq_ratio.shape[0]
    columns = jnp.einsum(
        "ack,nck->can",
        weighted,
        make_phasors(
            lax.all_gather(station_rows, "stn", axis=0, tiled=True),
            lax.all_gather(iono_phase, "stn", axis=0, tiled=True),
            directions,
            freq_ratio,
        ),
        preferred_element_type=jnp.float32,
    )
    visible = columns.reshape(channels, 2, stations_local, total_stations)
    first_row = lax.axis_index("stn") * stations_local
    rows_global = first_row + jnp.arange(stations_local, dtype=jnp.int32)
    cross_only = rows_global[:, None] != jnp.arange(total_stations, dtype=jnp.int32)[None, :]
    return jnp.where(cross_only[None, None], visible, jnp.zeros_like(visible))


def solution(mesh):
    in_specs = (
        P("stn", None, None),
        P(None, "stn", "chan", None, None),
        P("stn", "chan", None, None),
        P(None, "stn"),
        P(),
        P("chan"),
        P(),
        P(),
    )
    out_specs = P("chan", None, "stn", None)
    return jax.shard_map(body, mesh=mesh, in_specs=in_specs, out_specs=out_specs, check_vma=False)
```

```python
import math

import jax
import jax.numpy as jnp
from jax import lax
from jax.experimental import pallas as pl
from jax.experimental.pallas import tpu as pltpu
from jax.sharding import PartitionSpec as P

TWO_PI = 2.0 * math.pi


def interpolate(values, coords, strip_rows, tile_cols):
    row_pos = coords[0] * (strip_rows - 1)
    col_pos = coords[1] * (tile_cols - 1)
    row_low = jnp.clip(jnp.floor(row_pos), 0.0, strip_rows - 2.0)
    col_low = jnp.clip(jnp.floor(col_pos), 0.0, tile_cols - 2.0)
    frac_y = row_pos - row_low
    frac_x = col_pos - col_low
    corner = row_low.astype(jnp.int32) * tile_cols + col_low.astype(jnp.int32)
    lower_pair = (1.0 - frac_x) * values[corner] + frac_x * values[corner + 1]
    upper_pair = (1.0 - frac_x) * values[corner + tile_cols] + frac_x * values[
        corner + tile_cols + 1
    ]
    return (1.0 - frac_y) * lower_pair + frac_y * upper_pair


UNROLL = 64
KBITS = 12


def _interp_kernel(r_ref, c_ref, s_ref, o_ref):
    rows = s_ref.shape[0]
    two_nb = s_ref.shape[1]
    nb = two_nb // 2
    cols = nb * 128
    chunk = o_ref.shape[0]
    base = pl.program_id(0) * chunk
    sub = lax.broadcasted_iota(jnp.int32, (two_nb, 128), 0)
    lane = lax.broadcasted_iota(jnp.int32, (two_nb, 128), 1)
    col = ((sub % nb) * 128 + lane).astype(jnp.float32)
    upper = sub >= nb
    rowid = lax.broadcasted_iota(jnp.int32, (8, 128), 0)

    def group(g, carry):
        for h in range(UNROLL // 8):
            acc = jnp.zeros((8, 128), jnp.float32)
            for u in range(8):
                j = base + g * UNROLL + h * 8 + u
                t = s_ref[r_ref[j]]
                y = jnp.full((two_nb, 128), c_ref[0, j], jnp.float32) * (rows - 1)
                x = jnp.full((two_nb, 128), c_ref[1, j], jnp.float32) * (cols - 1)
                ry = jnp.clip(jnp.floor(y), 0.0, rows - 2.0)
                kx = jnp.clip(jnp.floor(x), 0.0, cols - 2.0)
                fy = y - ry
                fx = x - kx
                wy = jnp.where(upper, fy, 1.0 - fy)
                wx = jnp.where(col == kx, 1.0 - fx, jnp.where(col == kx + 1.0, fx, 0.0))
                row = jnp.sum(t * (wy * wx), axis=0, keepdims=True)
                acc = jnp.where(rowid == u, row, acc)
            start = pl.multiple_of(g * UNROLL + h * 8, 8)
            o_ref[pl.ds(start, 8), :] = jnp.sum(acc, axis=1, keepdims=True)
        return carry

    lax.fori_loop(0, chunk // UNROLL, group, 0)


def interpolate_kernel(screen2d, coords):
    rows, cols = screen2d.shape
    nb = cols // 128
    q = coords.shape[1]
    chunk = min(2048, q)
    r = jnp.clip(jnp.floor(coords[0] * (rows - 1)), 0.0, rows - 2.0).astype(jnp.int32)
    pair = jnp.concatenate([screen2d, jnp.roll(screen2d, -1, axis=0)], axis=1)
    pair = pair.reshape(rows, 2 * nb, 128)
    out = pl.pallas_call(
        _interp_kernel,
        grid_spec=pltpu.PrefetchScalarGridSpec(
            num_scalar_prefetch=2,
            grid=(q // chunk,),
            in_specs=[pl.BlockSpec((rows, 2 * nb, 128), lambda i, rr, cc: (0, 0, 0))],
            out_specs=pl.BlockSpec((chunk, 1), lambda i, rr, cc: (i, 0)),
        ),
        out_shape=jax.ShapeDtypeStruct((q, 1), jnp.float32),
    )(r, coords, pair)
    return out[:, 0]


def _balanced_kernel(n_ref, r_ref, c_ref, own_ref, partner_ref, o_ref):
    rows = own_ref.shape[0]
    nb = own_ref.shape[1]
    cols = nb * 128
    senders = n_ref.shape[0] // 2
    seg = o_ref.shape[0] // (2 * senders)
    unroll = min(UNROLL, seg)
    sub = lax.broadcasted_iota(jnp.int32, (nb, 128), 0)
    lane = lax.broadcasted_iota(jnp.int32, (nb, 128), 1)
    col = sub * 128 + lane
    rowid = lax.broadcasted_iota(jnp.int32, (8, 128), 0)

    for h, s_ref in enumerate((own_ref, partner_ref)):
        def segment(s, carry, h=h, s_ref=s_ref):
            def group(g, carry2):
                for part in range(unroll // 8):
                    acc = jnp.zeros((8, 128), jnp.float32)
                    first = (h * senders + s) * seg + g * unroll + part * 8
                    for u in range(8):
                        j = first + u
                        rk = r_ref[j]
                        r = rk >> KBITS
                        k = rk & ((1 << KBITS) - 1)
                        lower = s_ref[r]
                        upper = s_ref[r + 1]
                        fy = c_ref[0, j]
                        fx = c_ref[1, j]
                        blend = (1.0 - fy) * lower + fy * upper
                        wx = jnp.where(col == k, 1.0 - fx, jnp.where(col == k + 1, fx, 0.0))
                        row = jnp.sum(blend * wx, axis=0, keepdims=True)
                        acc = jnp.where(rowid == u, row, acc)
                    o_ref[pl.ds(pl.multiple_of(first, 8), 8), :] = jnp.sum(acc, axis=1, keepdims=True)
                return carry2

            trips = (n_ref[h * senders + s] + unroll - 1) // unroll
            lax.fori_loop(0, trips, group, 0)
            return carry

        lax.fori_loop(0, senders, segment, 0)


def interpolate_balanced(own, partner, coords, live):
    rows, nb, _ = own.shape
    cols = nb * 128
    _, halves, senders, seg = coords.shape
    flat = coords.reshape(2, halves * senders * seg)
    y = flat[0] * (rows - 1)
    x = flat[1] * (cols - 1)
    r = jnp.clip(jnp.floor(y), 0.0, rows - 2.0)
    k = jnp.clip(jnp.floor(x), 0.0, cols - 2.0)
    rk = (r.astype(jnp.int32) << KBITS) | k.astype(jnp.int32)
    frac = jnp.stack([y - r, x - k])
    spec = pl.BlockSpec((rows, nb, 128), lambda i, n, rr, cc: (0, 0, 0))
    out = pl.pallas_call(
        _balanced_kernel,
        grid_spec=pltpu.PrefetchScalarGridSpec(
            num_scalar_prefetch=3,
            grid=(1,),
            in_specs=[spec, spec],
            out_specs=pl.BlockSpec((halves * senders * seg, 1), lambda i, n, rr, cc: (0, 0)),
        ),
        out_shape=jax.ShapeDtypeStruct((halves * senders * seg, 1), jnp.float32),
    )(live, rk, frac, own, partner)
    return out.reshape(halves, senders, seg)


def _scatter_kernel(n_ref, d_ref, v_ref, o_ref):
    rows = n_ref.shape[0]
    width = d_ref.shape[0] // rows
    half = width // 2
    step = 16 if width % 16 == 0 else 2
    for row in range(rows):
        def body(i, carry, row=row):
            for u in range(step):
                slot = row * width + i * step + u
                parity = u % 2
                source = ((row ^ parity) * 2 + parity) * half + i * (step // 2) + u // 2
                o_ref[d_ref[slot]] = v_ref[source]
            return carry

        lax.fori_loop(0, (n_ref[row] + step - 1) // step, body, 0)


def scatter_kernel(dest, vals, size):
    live = jnp.sum((dest < size - 1).astype(jnp.int32), axis=1)
    return pl.pallas_call(
        _scatter_kernel,
        grid_spec=pltpu.PrefetchScalarGridSpec(
            num_scalar_prefetch=3,
            grid=(1,),
            in_specs=[],
            out_specs=pl.BlockSpec((size,), lambda i, n, d, v: (0,), memory_space=pltpu.SMEM),
        ),
        out_shape=jax.ShapeDtypeStruct((size,), jnp.float32),
    )(live, dest.reshape(-1), vals.reshape(-1))


def make_phasors(station_rows, iono_rows, directions, freq_ratio):
    delays = (
        station_rows[:, 0:1] * directions[0][None, :]
        + station_rows[:, 1:2] * directions[1][None, :]
    )
    delays = delays + station_rows[:, 2:3] * directions[2][None, :]
    angles = (TWO_PI * freq_ratio)[None, :, None] * delays[:, None, :] + iono_rows[
        :, None, :
    ] / freq_ratio[None, :, None]
    return jnp.concatenate([jnp.cos(angles), jnp.sin(angles)], axis=-1).astype(jnp.bfloat16)


def spectrum(source_flux, spectral_index, freq_ratio, count):
    return (
        source_flux[None, :]
        * jnp.exp(spectral_index[None, :] * jnp.log(freq_ratio)[:, None])
        / math.sqrt(count)
    )


def weight_rows(phasors, intensity):
    sources = intensity.shape[1]
    real_part = (phasors[:, :, :sources].astype(jnp.float32) * intensity[None]).astype(jnp.bfloat16)
    imag_part = (phasors[:, :, sources:].astype(jnp.float32) * intensity[None]).astype(jnp.bfloat16)
    upper_rows = jnp.concatenate([real_part, imag_part], axis=-1)
    lower_rows = jnp.concatenate([imag_part, -real_part], axis=-1)
    return jnp.concatenate([upper_rows, lower_rows], axis=0)


def body(
    screen,
    pierce_coords,
    query_dest,
    positions,
    directions,
    freq_ratio,
    source_flux,
    spectral_index,
):
    groups = lax.axis_size("stn")
    tile_cols = screen.shape[2]
    strip_rows = screen.shape[0] * screen.shape[1]
    values = screen.reshape(-1)
    capacity = query_dest.shape[3]
    stations_local = positions.shape[1]
    local_sources = source_flux.shape[0] // lax.axis_size("chan")
    queries = stations_local * local_sources
    half = capacity // 2
    coords = pierce_coords.reshape(2, groups, capacity)
    dead = query_dest.reshape(groups, capacity) >= queries
    coords = jnp.where(dead[None], -1.0, coords).reshape(2, groups, half, 2)
    swap = lambda a: a.reshape(a.shape[0], groups // 2, 2, half)[:, :, ::-1, :].reshape(a.shape[0], groups, half)
    send = jnp.stack([coords[..., 0], swap(coords[..., 1])], axis=2)
    received = lax.all_to_all(send, "stn", split_axis=1, concat_axis=1, tiled=True)
    kin = received.transpose(0, 2, 1, 3)
    live = jnp.sum((kin[0] >= 0.0).astype(jnp.int32), axis=2).reshape(-1)
    own = screen.reshape(strip_rows, tile_cols // 128, 128)
    partner = lax.ppermute(own, "stn", [(i, i ^ 1) for i in range(groups)])
    sampled = interpolate_balanced(own, partner, kin, live).transpose(1, 0, 2)
    back = lax.all_to_all(sampled, "stn", split_axis=0, concat_axis=0, tiled=True)
    buffer = scatter_kernel(query_dest.reshape(groups, capacity), back, queries + 1)
    own_iono = buffer[:queries].reshape(stations_local, local_sources)
    station_rows = positions.T
    total_stations = stations_local * groups
    channels = freq_ratio.shape[0]
    n_chan = lax.axis_size("chan")
    if channels % groups:
        return _rows_path(own_iono, station_rows, directions, freq_ratio, source_flux, spectral_index)
    iono_phase = lax.all_gather(own_iono, "chan", axis=1, tiled=True)
    packed = jnp.concatenate([iono_phase, station_rows], axis=1)
    gathered = lax.all_gather(packed, "stn", axis=0, tiled=True)
    all_iono = gathered[:, : n_chan * local_sources]
    all_rows = gathered[:, n_chan * local_sources :]
    per_dev = channels // groups
    my_freq = lax.dynamic_slice_in_dim(freq_ratio, lax.axis_index("stn") * per_dev, per_dev)
    phasors = make_phasors(all_rows, all_iono, directions, my_freq)
    intensity = spectrum(source_flux, spectral_index, my_freq, source_flux.shape[0])
    weighted = weight_rows(phasors, intensity)
    columns = jnp.einsum("ack,nck->can", weighted, phasors, preferred_element_type=jnp.float32)
    visible = columns.reshape(per_dev, 2, total_stations, total_stations)
    ids = jnp.arange(total_stations, dtype=jnp.int32)
    cross_only = ids[:, None] != ids[None, :]
    visible = jnp.where(cross_only[None, None], visible, jnp.zeros_like(visible))
    moved = lax.all_to_all(visible.astype(jnp.bfloat16), "stn", split_axis=2, concat_axis=0, tiled=True)
    return moved.astype(jnp.float32)


def _rows_path(own_iono, station_rows, directions, freq_ratio, source_flux, spectral_index):
    groups = lax.axis_size("stn")
    stations_local = station_rows.shape[0]
    iono_phase = lax.all_gather(own_iono, "chan", axis=1, tiled=True)
    own_phasors = make_phasors(station_rows, iono_phase, directions, freq_ratio)
    intensity = spectrum(source_flux, spectral_index, freq_ratio, source_flux.shape[0])
    weighted = weight_rows(own_phasors, intensity)
    total_stations = stations_local * groups
    channels = freq_ratio.shape[0]
    columns = jnp.einsum(
        "ack,nck->can",
        weighted,
        make_phasors(
            lax.all_gather(station_rows, "stn", axis=0, tiled=True),
            lax.all_gather(iono_phase, "stn", axis=0, tiled=True),
            directions,
            freq_ratio,
        ),
        preferred_element_type=jnp.float32,
    )
    visible = columns.reshape(channels, 2, stations_local, total_stations)
    first_row = lax.axis_index("stn") * stations_local
    rows_global = first_row + jnp.arange(stations_local, dtype=jnp.int32)
    cross_only = rows_global[:, None] != jnp.arange(total_stations, dtype=jnp.int32)[None, :]
    return jnp.where(cross_only[None, None], visible, jnp.zeros_like(visible))


def solution(mesh):
    in_specs = (
        P("stn", None, None),
        P(None, "stn", "chan", None, None),
        P("stn", "chan", None, None),
        P(None, "stn"),
        P(),
        P("chan"),
        P(),
        P(),
    )
    out_specs = P("chan", None, "stn", None)
    return jax.shard_map(body, mesh=mesh, in_specs=in_specs, out_specs=out_specs, check_vma=False)
```

```python
import math

import jax
import jax.numpy as jnp
from jax import lax
from jax.experimental import pallas as pl
from jax.experimental.pallas import tpu as pltpu
from jax.sharding import PartitionSpec as P

TWO_PI = 2.0 * math.pi


def interpolate(values, coords, strip_rows, tile_cols):
    row_pos = coords[0] * (strip_rows - 1)
    col_pos = coords[1] * (tile_cols - 1)
    row_low = jnp.clip(jnp.floor(row_pos), 0.0, strip_rows - 2.0)
    col_low = jnp.clip(jnp.floor(col_pos), 0.0, tile_cols - 2.0)
    frac_y = row_pos - row_low
    frac_x = col_pos - col_low
    corner = row_low.astype(jnp.int32) * tile_cols + col_low.astype(jnp.int32)
    lower_pair = (1.0 - frac_x) * values[corner] + frac_x * values[corner + 1]
    upper_pair = (1.0 - frac_x) * values[corner + tile_cols] + frac_x * values[
        corner + tile_cols + 1
    ]
    return (1.0 - frac_y) * lower_pair + frac_y * upper_pair


UNROLL = 128
KBITS = 12


def _interp_kernel(r_ref, c_ref, s_ref, o_ref):
    rows = s_ref.shape[0]
    two_nb = s_ref.shape[1]
    nb = two_nb // 2
    cols = nb * 128
    chunk = o_ref.shape[0]
    base = pl.program_id(0) * chunk
    sub = lax.broadcasted_iota(jnp.int32, (two_nb, 128), 0)
    lane = lax.broadcasted_iota(jnp.int32, (two_nb, 128), 1)
    col = ((sub % nb) * 128 + lane).astype(jnp.float32)
    upper = sub >= nb
    rowid = lax.broadcasted_iota(jnp.int32, (8, 128), 0)

    def group(g, carry):
        for h in range(UNROLL // 8):
            acc = jnp.zeros((8, 128), jnp.float32)
            for u in range(8):
                j = base + g * UNROLL + h * 8 + u
                t = s_ref[r_ref[j]]
                y = jnp.full((two_nb, 128), c_ref[0, j], jnp.float32) * (rows - 1)
                x = jnp.full((two_nb, 128), c_ref[1, j], jnp.float32) * (cols - 1)
                ry = jnp.clip(jnp.floor(y), 0.0, rows - 2.0)
                kx = jnp.clip(jnp.floor(x), 0.0, cols - 2.0)
                fy = y - ry
                fx = x - kx
                wy = jnp.where(upper, fy, 1.0 - fy)
                wx = jnp.where(col == kx, 1.0 - fx, jnp.where(col == kx + 1.0, fx, 0.0))
                row = jnp.sum(t * (wy * wx), axis=0, keepdims=True)
                acc = jnp.where(rowid == u, row, acc)
            start = pl.multiple_of(g * UNROLL + h * 8, 8)
            o_ref[pl.ds(start, 8), :] = jnp.sum(acc, axis=1, keepdims=True)
        return carry

    lax.fori_loop(0, chunk // UNROLL, group, 0)


def interpolate_kernel(screen2d, coords):
    rows, cols = screen2d.shape
    nb = cols // 128
    q = coords.shape[1]
    chunk = min(2048, q)
    r = jnp.clip(jnp.floor(coords[0] * (rows - 1)), 0.0, rows - 2.0).astype(jnp.int32)
    pair = jnp.concatenate([screen2d, jnp.roll(screen2d, -1, axis=0)], axis=1)
    pair = pair.reshape(rows, 2 * nb, 128)
    out = pl.pallas_call(
        _interp_kernel,
        grid_spec=pltpu.PrefetchScalarGridSpec(
            num_scalar_prefetch=2,
            grid=(q // chunk,),
            in_specs=[pl.BlockSpec((rows, 2 * nb, 128), lambda i, rr, cc: (0, 0, 0))],
            out_specs=pl.BlockSpec((chunk, 1), lambda i, rr, cc: (i, 0)),
        ),
        out_shape=jax.ShapeDtypeStruct((q, 1), jnp.float32),
    )(r, coords, pair)
    return out[:, 0]


def _balanced_kernel(n_ref, r_ref, c_ref, own_ref, partner_ref, o_ref):
    rows = own_ref.shape[0]
    nb = own_ref.shape[1]
    cols = nb * 128
    senders = n_ref.shape[0] // 2
    seg = o_ref.shape[0] // (2 * senders)
    unroll = min(UNROLL, seg)
    sub = lax.broadcasted_iota(jnp.int32, (nb, 128), 0)
    lane = lax.broadcasted_iota(jnp.int32, (nb, 128), 1)
    col = sub * 128 + lane
    rowid = lax.broadcasted_iota(jnp.int32, (8, 128), 0)

    for h, s_ref in enumerate((own_ref, partner_ref)):
        def segment(s, carry, h=h, s_ref=s_ref):
            def group(g, carry2):
                for part in range(unroll // 8):
                    acc = jnp.zeros((8, 128), jnp.float32)
                    first = (h * senders + s) * seg + g * unroll + part * 8
                    for u in range(8):
                        j = first + u
                        rk = r_ref[j]
                        r = rk >> KBITS
                        k = rk & ((1 << KBITS) - 1)
                        lower = s_ref[r]
                        upper = s_ref[r + 1]
                        fy = c_ref[0, j]
                        fx = c_ref[1, j]
                        blend = (1.0 - fy) * lower + fy * upper
                        wx = jnp.where(col == k, 1.0 - fx, jnp.where(col == k + 1, fx, 0.0))
                        row = jnp.sum(blend * wx, axis=0, keepdims=True)
                        acc = jnp.where(rowid == u, row, acc)
                    o_ref[pl.ds(pl.multiple_of(first, 8), 8), :] = jnp.sum(acc, axis=1, keepdims=True)
                return carry2

            trips = (n_ref[h * senders + s] + unroll - 1) // unroll
            lax.fori_loop(0, trips, group, 0)
            return carry

        lax.fori_loop(0, senders, segment, 0)


def interpolate_balanced(own, partner, coords, live):
    rows, nb, _ = own.shape
    cols = nb * 128
    _, halves, senders, seg = coords.shape
    flat = coords.reshape(2, halves * senders * seg)
    y = flat[0] * (rows - 1)
    x = flat[1] * (cols - 1)
    r = jnp.clip(jnp.floor(y), 0.0, rows - 2.0)
    k = jnp.clip(jnp.floor(x), 0.0, cols - 2.0)
    rk = (r.astype(jnp.int32) << KBITS) | k.astype(jnp.int32)
    frac = jnp.stack([y - r, x - k])
    spec = pl.BlockSpec((rows, nb, 128), lambda i, n, rr, cc: (0, 0, 0))
    out = pl.pallas_call(
        _balanced_kernel,
        grid_spec=pltpu.PrefetchScalarGridSpec(
            num_scalar_prefetch=3,
            grid=(1,),
            in_specs=[spec, spec],
            out_specs=pl.BlockSpec((halves * senders * seg, 1), lambda i, n, rr, cc: (0, 0)),
        ),
        out_shape=jax.ShapeDtypeStruct((halves * senders * seg, 1), jnp.float32),
    )(live, rk, frac, own, partner)
    return out.reshape(halves, senders, seg)


def _scatter_kernel(n_ref, d_ref, v_ref, o_ref):
    rows = n_ref.shape[0]
    width = d_ref.shape[0] // rows
    half = width // 2
    step = 16 if width % 16 == 0 else 2
    for row in range(rows):
        def body(i, carry, row=row):
            for u in range(step):
                slot = row * width + i * step + u
                parity = u % 2
                source = ((row ^ parity) * 2 + parity) * half + i * (step // 2) + u // 2
                o_ref[d_ref[slot]] = v_ref[source]
            return carry

        lax.fori_loop(0, (n_ref[row] + step - 1) // step, body, 0)


def scatter_kernel(dest, vals, size):
    live = jnp.sum((dest < size - 1).astype(jnp.int32), axis=1)
    return pl.pallas_call(
        _scatter_kernel,
        grid_spec=pltpu.PrefetchScalarGridSpec(
            num_scalar_prefetch=3,
            grid=(1,),
            in_specs=[],
            out_specs=pl.BlockSpec((size,), lambda i, n, d, v: (0,), memory_space=pltpu.SMEM),
        ),
        out_shape=jax.ShapeDtypeStruct((size,), jnp.float32),
    )(live, dest.reshape(-1), vals.reshape(-1))


def make_phasors(station_rows, iono_rows, directions, freq_ratio):
    delays = (
        station_rows[:, 0:1] * directions[0][None, :]
        + station_rows[:, 1:2] * directions[1][None, :]
    )
    delays = delays + station_rows[:, 2:3] * directions[2][None, :]
    angles = (TWO_PI * freq_ratio)[None, :, None] * delays[:, None, :] + iono_rows[
        :, None, :
    ] / freq_ratio[None, :, None]
    return jnp.concatenate([jnp.cos(angles), jnp.sin(angles)], axis=-1).astype(jnp.bfloat16)


def spectrum(source_flux, spectral_index, freq_ratio, count):
    return (
        source_flux[None, :]
        * jnp.exp(spectral_index[None, :] * jnp.log(freq_ratio)[:, None])
        / math.sqrt(count)
    )


def weight_rows(phasors, intensity):
    sources = intensity.shape[1]
    real_part = (phasors[:, :, :sources].astype(jnp.float32) * intensity[None]).astype(jnp.bfloat16)
    imag_part = (phasors[:, :, sources:].astype(jnp.float32) * intensity[None]).astype(jnp.bfloat16)
    upper_rows = jnp.concatenate([real_part, imag_part], axis=-1)
    lower_rows = jnp.concatenate([imag_part, -real_part], axis=-1)
    return jnp.concatenate([upper_rows, lower_rows], axis=0)


def body(
    screen,
    pierce_coords,
    query_dest,
    positions,
    directions,
    freq_ratio,
    source_flux,
    spectral_index,
):
    groups = lax.axis_size("stn")
    tile_cols = screen.shape[2]
    strip_rows = screen.shape[0] * screen.shape[1]
    values = screen.reshape(-1)
    capacity = query_dest.shape[3]
    stations_local = positions.shape[1]
    local_sources = source_flux.shape[0] // lax.axis_size("chan")
    queries = stations_local * local_sources
    half = capacity // 2
    coords = pierce_coords.reshape(2, groups, capacity)
    dead = query_dest.reshape(groups, capacity) >= queries
    coords = jnp.where(dead[None], -1.0, coords).reshape(2, groups, half, 2)
    swap = lambda a: a.reshape(a.shape[0], groups // 2, 2, half)[:, :, ::-1, :].reshape(a.shape[0], groups, half)
    send = jnp.stack([coords[..., 0], swap(coords[..., 1])], axis=2)
    received = lax.all_to_all(send, "stn", split_axis=1, concat_axis=1, tiled=True)
    kin = received.transpose(0, 2, 1, 3)
    live = jnp.sum((kin[0] >= 0.0).astype(jnp.int32), axis=2).reshape(-1)
    own = screen.reshape(strip_rows, tile_cols // 128, 128)
    partner = lax.ppermute(own, "stn", [(i, i ^ 1) for i in range(groups)])
    sampled = interpolate_balanced(own, partner, kin, live).transpose(1, 0, 2)
    back = lax.all_to_all(sampled, "stn", split_axis=0, concat_axis=0, tiled=True)
    buffer = scatter_kernel(query_dest.reshape(groups, capacity), back, queries + 1)
    own_iono = buffer[:queries].reshape(stations_local, local_sources)
    station_rows = positions.T
    total_stations = stations_local * groups
    channels = freq_ratio.shape[0]
    n_chan = lax.axis_size("chan")
    if channels % groups:
        return _rows_path(own_iono, station_rows, directions, freq_ratio, source_flux, spectral_index)
    iono_phase = lax.all_gather(own_iono, "chan", axis=1, tiled=True)
    packed = jnp.concatenate([iono_phase, station_rows], axis=1)
    gathered = lax.all_gather(packed, "stn", axis=0, tiled=True)
    all_iono = gathered[:, : n_chan * local_sources]
    all_rows = gathered[:, n_chan * local_sources :]
    per_dev = channels // groups
    my_freq = lax.dynamic_slice_in_dim(freq_ratio, lax.axis_index("stn") * per_dev, per_dev)
    phasors = make_phasors(all_rows, all_iono, directions, my_freq)
    intensity = spectrum(source_flux, spectral_index, my_freq, source_flux.shape[0])
    weighted = weight_rows(phasors, intensity)
    columns = jnp.einsum("ack,nck->can", weighted, phasors, preferred_element_type=jnp.float32)
    visible = columns.reshape(per_dev, 2, total_stations, total_stations)
    ids = jnp.arange(total_stations, dtype=jnp.int32)
    cross_only = ids[:, None] != ids[None, :]
    visible = jnp.where(cross_only[None, None], visible, jnp.zeros_like(visible))
    moved = lax.all_to_all(visible.astype(jnp.bfloat16), "stn", split_axis=2, concat_axis=0, tiled=True)
    return moved.astype(jnp.float32)


def _rows_path(own_iono, station_rows, directions, freq_ratio, source_flux, spectral_index):
    groups = lax.axis_size("stn")
    stations_local = station_rows.shape[0]
    iono_phase = lax.all_gather(own_iono, "chan", axis=1, tiled=True)
    own_phasors = make_phasors(station_rows, iono_phase, directions, freq_ratio)
    intensity = spectrum(source_flux, spectral_index, freq_ratio, source_flux.shape[0])
    weighted = weight_rows(own_phasors, intensity)
    total_stations = stations_local * groups
    channels = freq_ratio.shape[0]
    columns = jnp.einsum(
        "ack,nck->can",
        weighted,
        make_phasors(
            lax.all_gather(station_rows, "stn", axis=0, tiled=True),
            lax.all_gather(iono_phase, "stn", axis=0, tiled=True),
            directions,
            freq_ratio,
        ),
        preferred_element_type=jnp.float32,
    )
    visible = columns.reshape(channels, 2, stations_local, total_stations)
    first_row = lax.axis_index("stn") * stations_local
    rows_global = first_row + jnp.arange(stations_local, dtype=jnp.int32)
    cross_only = rows_global[:, None] != jnp.arange(total_stations, dtype=jnp.int32)[None, :]
    return jnp.where(cross_only[None, None], visible, jnp.zeros_like(visible))


def solution(mesh):
    in_specs = (
        P("stn", None, None),
        P(None, "stn", "chan", None, None),
        P("stn", "chan", None, None),
        P(None, "stn"),
        P(),
        P("chan"),
        P(),
        P(),
    )
    out_specs = P("chan", None, "stn", None)
    return jax.shard_map(body, mesh=mesh, in_specs=in_specs, out_specs=out_specs, check_vma=False)
```

```python
import math

import jax
import jax.numpy as jnp
from jax import lax
from jax.experimental import pallas as pl
from jax.experimental.pallas import tpu as pltpu
from jax.sharding import PartitionSpec as P

TWO_PI = 2.0 * math.pi


def interpolate(values, coords, strip_rows, tile_cols):
    row_pos = coords[0] * (strip_rows - 1)
    col_pos = coords[1] * (tile_cols - 1)
    row_low = jnp.clip(jnp.floor(row_pos), 0.0, strip_rows - 2.0)
    col_low = jnp.clip(jnp.floor(col_pos), 0.0, tile_cols - 2.0)
    frac_y = row_pos - row_low
    frac_x = col_pos - col_low
    corner = row_low.astype(jnp.int32) * tile_cols + col_low.astype(jnp.int32)
    lower_pair = (1.0 - frac_x) * values[corner] + frac_x * values[corner + 1]
    upper_pair = (1.0 - frac_x) * values[corner + tile_cols] + frac_x * values[
        corner + tile_cols + 1
    ]
    return (1.0 - frac_y) * lower_pair + frac_y * upper_pair


UNROLL = 256
KBITS = 12


def _interp_kernel(r_ref, c_ref, s_ref, o_ref):
    rows = s_ref.shape[0]
    two_nb = s_ref.shape[1]
    nb = two_nb // 2
    cols = nb * 128
    chunk = o_ref.shape[0]
    base = pl.program_id(0) * chunk
    sub = lax.broadcasted_iota(jnp.int32, (two_nb, 128), 0)
    lane = lax.broadcasted_iota(jnp.int32, (two_nb, 128), 1)
    col = ((sub % nb) * 128 + lane).astype(jnp.float32)
    upper = sub >= nb
    rowid = lax.broadcasted_iota(jnp.int32, (8, 128), 0)

    def group(g, carry):
        for h in range(UNROLL // 8):
            acc = jnp.zeros((8, 128), jnp.float32)
            for u in range(8):
                j = base + g * UNROLL + h * 8 + u
                t = s_ref[r_ref[j]]
                y = jnp.full((two_nb, 128), c_ref[0, j], jnp.float32) * (rows - 1)
                x = jnp.full((two_nb, 128), c_ref[1, j], jnp.float32) * (cols - 1)
                ry = jnp.clip(jnp.floor(y), 0.0, rows - 2.0)
                kx = jnp.clip(jnp.floor(x), 0.0, cols - 2.0)
                fy = y - ry
                fx = x - kx
                wy = jnp.where(upper, fy, 1.0 - fy)
                wx = jnp.where(col == kx, 1.0 - fx, jnp.where(col == kx + 1.0, fx, 0.0))
                row = jnp.sum(t * (wy * wx), axis=0, keepdims=True)
                acc = jnp.where(rowid == u, row, acc)
            start = pl.multiple_of(g * UNROLL + h * 8, 8)
            o_ref[pl.ds(start, 8), :] = jnp.sum(acc, axis=1, keepdims=True)
        return carry

    lax.fori_loop(0, chunk // UNROLL, group, 0)


def interpolate_kernel(screen2d, coords):
    rows, cols = screen2d.shape
    nb = cols // 128
    q = coords.shape[1]
    chunk = min(2048, q)
    r = jnp.clip(jnp.floor(coords[0] * (rows - 1)), 0.0, rows - 2.0).astype(jnp.int32)
    pair = jnp.concatenate([screen2d, jnp.roll(screen2d, -1, axis=0)], axis=1)
    pair = pair.reshape(rows, 2 * nb, 128)
    out = pl.pallas_call(
        _interp_kernel,
        grid_spec=pltpu.PrefetchScalarGridSpec(
            num_scalar_prefetch=2,
            grid=(q // chunk,),
            in_specs=[pl.BlockSpec((rows, 2 * nb, 128), lambda i, rr, cc: (0, 0, 0))],
            out_specs=pl.BlockSpec((chunk, 1), lambda i, rr, cc: (i, 0)),
        ),
        out_shape=jax.ShapeDtypeStruct((q, 1), jnp.float32),
    )(r, coords, pair)
    return out[:, 0]


def _balanced_kernel(n_ref, r_ref, c_ref, own_ref, partner_ref, o_ref):
    rows = own_ref.shape[0]
    nb = own_ref.shape[1]
    cols = nb * 128
    senders = n_ref.shape[0] // 2
    seg = o_ref.shape[0] // (2 * senders)
    unroll = min(UNROLL, seg)
    sub = lax.broadcasted_iota(jnp.int32, (nb, 128), 0)
    lane = lax.broadcasted_iota(jnp.int32, (nb, 128), 1)
    col = sub * 128 + lane
    rowid = lax.broadcasted_iota(jnp.int32, (8, 128), 0)

    for h, s_ref in enumerate((own_ref, partner_ref)):
        def segment(s, carry, h=h, s_ref=s_ref):
            def group(g, carry2):
                for part in range(unroll // 8):
                    acc = jnp.zeros((8, 128), jnp.float32)
                    first = (h * senders + s) * seg + g * unroll + part * 8
                    for u in range(8):
                        j = first + u
                        rk = r_ref[j]
                        r = rk >> KBITS
                        k = rk & ((1 << KBITS) - 1)
                        lower = s_ref[r]
                        upper = s_ref[r + 1]
                        fy = c_ref[0, j]
                        fx = c_ref[1, j]
                        blend = (1.0 - fy) * lower + fy * upper
                        wx = jnp.where(col == k, 1.0 - fx, jnp.where(col == k + 1, fx, 0.0))
                        row = jnp.sum(blend * wx, axis=0, keepdims=True)
                        acc = jnp.where(rowid == u, row, acc)
                    o_ref[pl.ds(pl.multiple_of(first, 8), 8), :] = jnp.sum(acc, axis=1, keepdims=True)
                return carry2

            trips = (n_ref[h * senders + s] + unroll - 1) // unroll
            lax.fori_loop(0, trips, group, 0)
            return carry

        lax.fori_loop(0, senders, segment, 0)


def interpolate_balanced(own, partner, coords, live):
    rows, nb, _ = own.shape
    cols = nb * 128
    _, halves, senders, seg = coords.shape
    flat = coords.reshape(2, halves * senders * seg)
    y = flat[0] * (rows - 1)
    x = flat[1] * (cols - 1)
    r = jnp.clip(jnp.floor(y), 0.0, rows - 2.0)
    k = jnp.clip(jnp.floor(x), 0.0, cols - 2.0)
    rk = (r.astype(jnp.int32) << KBITS) | k.astype(jnp.int32)
    frac = jnp.stack([y - r, x - k])
    spec = pl.BlockSpec((rows, nb, 128), lambda i, n, rr, cc: (0, 0, 0))
    out = pl.pallas_call(
        _balanced_kernel,
        grid_spec=pltpu.PrefetchScalarGridSpec(
            num_scalar_prefetch=3,
            grid=(1,),
            in_specs=[spec, spec],
            out_specs=pl.BlockSpec((halves * senders * seg, 1), lambda i, n, rr, cc: (0, 0)),
        ),
        out_shape=jax.ShapeDtypeStruct((halves * senders * seg, 1), jnp.float32),
    )(live, rk, frac, own, partner)
    return out.reshape(halves, senders, seg)


def _scatter_kernel(n_ref, d_ref, v_ref, o_ref):
    rows = n_ref.shape[0]
    width = d_ref.shape[0] // rows
    half = width // 2
    step = 16 if width % 16 == 0 else 2
    for row in range(rows):
        def body(i, carry, row=row):
            for u in range(step):
                slot = row * width + i * step + u
                parity = u % 2
                source = ((row ^ parity) * 2 + parity) * half + i * (step // 2) + u // 2
                o_ref[d_ref[slot]] = v_ref[source]
            return carry

        lax.fori_loop(0, (n_ref[row] + step - 1) // step, body, 0)


def scatter_kernel(dest, vals, size):
    live = jnp.sum((dest < size - 1).astype(jnp.int32), axis=1)
    return pl.pallas_call(
        _scatter_kernel,
        grid_spec=pltpu.PrefetchScalarGridSpec(
            num_scalar_prefetch=3,
            grid=(1,),
            in_specs=[],
            out_specs=pl.BlockSpec((size,), lambda i, n, d, v: (0,), memory_space=pltpu.SMEM),
        ),
        out_shape=jax.ShapeDtypeStruct((size,), jnp.float32),
    )(live, dest.reshape(-1), vals.reshape(-1))


def make_phasors(station_rows, iono_rows, directions, freq_ratio):
    delays = (
        station_rows[:, 0:1] * directions[0][None, :]
        + station_rows[:, 1:2] * directions[1][None, :]
    )
    delays = delays + station_rows[:, 2:3] * directions[2][None, :]
    angles = (TWO_PI * freq_ratio)[None, :, None] * delays[:, None, :] + iono_rows[
        :, None, :
    ] / freq_ratio[None, :, None]
    return jnp.concatenate([jnp.cos(angles), jnp.sin(angles)], axis=-1).astype(jnp.bfloat16)


def spectrum(source_flux, spectral_index, freq_ratio, count):
    return (
        source_flux[None, :]
        * jnp.exp(spectral_index[None, :] * jnp.log(freq_ratio)[:, None])
        / math.sqrt(count)
    )


def weight_rows(phasors, intensity):
    sources = intensity.shape[1]
    real_part = (phasors[:, :, :sources].astype(jnp.float32) * intensity[None]).astype(jnp.bfloat16)
    imag_part = (phasors[:, :, sources:].astype(jnp.float32) * intensity[None]).astype(jnp.bfloat16)
    upper_rows = jnp.concatenate([real_part, imag_part], axis=-1)
    lower_rows = jnp.concatenate([imag_part, -real_part], axis=-1)
    return jnp.concatenate([upper_rows, lower_rows], axis=0)


def body(
    screen,
    pierce_coords,
    query_dest,
    positions,
    directions,
    freq_ratio,
    source_flux,
    spectral_index,
):
    groups = lax.axis_size("stn")
    tile_cols = screen.shape[2]
    strip_rows = screen.shape[0] * screen.shape[1]
    values = screen.reshape(-1)
    capacity = query_dest.shape[3]
    stations_local = positions.shape[1]
    local_sources = source_flux.shape[0] // lax.axis_size("chan")
    queries = stations_local * local_sources
    half = capacity // 2
    coords = pierce_coords.reshape(2, groups, capacity)
    dead = query_dest.reshape(groups, capacity) >= queries
    coords = jnp.where(dead[None], -1.0, coords).reshape(2, groups, half, 2)
    swap = lambda a: a.reshape(a.shape[0], groups // 2, 2, half)[:, :, ::-1, :].reshape(a.shape[0], groups, half)
    send = jnp.stack([coords[..., 0], swap(coords[..., 1])], axis=2)
    received = lax.all_to_all(send, "stn", split_axis=1, concat_axis=1, tiled=True)
    kin = received.transpose(0, 2, 1, 3)
    live = jnp.sum((kin[0] >= 0.0).astype(jnp.int32), axis=2).reshape(-1)
    own = screen.reshape(strip_rows, tile_cols // 128, 128)
    partner = lax.ppermute(own, "stn", [(i, i ^ 1) for i in range(groups)])
    sampled = interpolate_balanced(own, partner, kin, live).transpose(1, 0, 2)
    back = lax.all_to_all(sampled, "stn", split_axis=0, concat_axis=0, tiled=True)
    buffer = scatter_kernel(query_dest.reshape(groups, capacity), back, queries + 1)
    own_iono = buffer[:queries].reshape(stations_local, local_sources)
    station_rows = positions.T
    total_stations = stations_local * groups
    channels = freq_ratio.shape[0]
    n_chan = lax.axis_size("chan")
    if channels % groups:
        return _rows_path(own_iono, station_rows, directions, freq_ratio, source_flux, spectral_index)
    iono_phase = lax.all_gather(own_iono, "chan", axis=1, tiled=True)
    packed = jnp.concatenate([iono_phase, station_rows], axis=1)
    gathered = lax.all_gather(packed, "stn", axis=0, tiled=True)
    all_iono = gathered[:, : n_chan * local_sources]
    all_rows = gathered[:, n_chan * local_sources :]
    per_dev = channels // groups
    my_freq = lax.dynamic_slice_in_dim(freq_ratio, lax.axis_index("stn") * per_dev, per_dev)
    phasors = make_phasors(all_rows, all_iono, directions, my_freq)
    intensity = spectrum(source_flux, spectral_index, my_freq, source_flux.shape[0])
    weighted = weight_rows(phasors, intensity)
    columns = jnp.einsum("ack,nck->can", weighted, phasors, preferred_element_type=jnp.float32)
    visible = columns.reshape(per_dev, 2, total_stations, total_stations)
    ids = jnp.arange(total_stations, dtype=jnp.int32)
    cross_only = ids[:, None] != ids[None, :]
    visible = jnp.where(cross_only[None, None], visible, jnp.zeros_like(visible))
    moved = lax.all_to_all(visible.astype(jnp.bfloat16), "stn", split_axis=2, concat_axis=0, tiled=True)
    return moved.astype(jnp.float32)


def _rows_path(own_iono, station_rows, directions, freq_ratio, source_flux, spectral_index):
    groups = lax.axis_size("stn")
    stations_local = station_rows.shape[0]
    iono_phase = lax.all_gather(own_iono, "chan", axis=1, tiled=True)
    own_phasors = make_phasors(station_rows, iono_phase, directions, freq_ratio)
    intensity = spectrum(source_flux, spectral_index, freq_ratio, source_flux.shape[0])
    weighted = weight_rows(own_phasors, intensity)
    total_stations = stations_local * groups
    channels = freq_ratio.shape[0]
    columns = jnp.einsum(
        "ack,nck->can",
        weighted,
        make_phasors(
            lax.all_gather(station_rows, "stn", axis=0, tiled=True),
            lax.all_gather(iono_phase, "stn", axis=0, tiled=True),
            directions,
            freq_ratio,
        ),
        preferred_element_type=jnp.float32,
    )
    visible = columns.reshape(channels, 2, stations_local, total_stations)
    first_row = lax.axis_index("stn") * stations_local
    rows_global = first_row + jnp.arange(stations_local, dtype=jnp.int32)
    cross_only = rows_global[:, None] != jnp.arange(total_stations, dtype=jnp.int32)[None, :]
    return jnp.where(cross_only[None, None], visible, jnp.zeros_like(visible))


def solution(mesh):
    in_specs = (
        P("stn", None, None),
        P(None, "stn", "chan", None, None),
        P("stn", "chan", None, None),
        P(None, "stn"),
        P(),
        P("chan"),
        P(),
        P(),
    )
    out_specs = P("chan", None, "stn", None)
    return jax.shard_map(body, mesh=mesh, in_specs=in_specs, out_specs=out_specs, check_vma=False)
```

```python
import math

import jax
import jax.numpy as jnp
from jax import lax
from jax.experimental import pallas as pl
from jax.experimental.pallas import tpu as pltpu
from jax.sharding import PartitionSpec as P

TWO_PI = 2.0 * math.pi


def interpolate(values, coords, strip_rows, tile_cols):
    row_pos = coords[0] * (strip_rows - 1)
    col_pos = coords[1] * (tile_cols - 1)
    row_low = jnp.clip(jnp.floor(row_pos), 0.0, strip_rows - 2.0)
    col_low = jnp.clip(jnp.floor(col_pos), 0.0, tile_cols - 2.0)
    frac_y = row_pos - row_low
    frac_x = col_pos - col_low
    corner = row_low.astype(jnp.int32) * tile_cols + col_low.astype(jnp.int32)
    lower_pair = (1.0 - frac_x) * values[corner] + frac_x * values[corner + 1]
    upper_pair = (1.0 - frac_x) * values[corner + tile_cols] + frac_x * values[
        corner + tile_cols + 1
    ]
    return (1.0 - frac_y) * lower_pair + frac_y * upper_pair


UNROLL = 128
KBITS = 12


def _interp_kernel(r_ref, c_ref, s_ref, o_ref):
    rows = s_ref.shape[0]
    two_nb = s_ref.shape[1]
    nb = two_nb // 2
    cols = nb * 128
    chunk = o_ref.shape[0]
    base = pl.program_id(0) * chunk
    sub = lax.broadcasted_iota(jnp.int32, (two_nb, 128), 0)
    lane = lax.broadcasted_iota(jnp.int32, (two_nb, 128), 1)
    col = ((sub % nb) * 128 + lane).astype(jnp.float32)
    upper = sub >= nb
    rowid = lax.broadcasted_iota(jnp.int32, (8, 128), 0)

    def group(g, carry):
        for h in range(UNROLL // 8):
            acc = jnp.zeros((8, 128), jnp.float32)
            for u in range(8):
                j = base + g * UNROLL + h * 8 + u
                t = s_ref[r_ref[j]]
                y = jnp.full((two_nb, 128), c_ref[0, j], jnp.float32) * (rows - 1)
                x = jnp.full((two_nb, 128), c_ref[1, j], jnp.float32) * (cols - 1)
                ry = jnp.clip(jnp.floor(y), 0.0, rows - 2.0)
                kx = jnp.clip(jnp.floor(x), 0.0, cols - 2.0)
                fy = y - ry
                fx = x - kx
                wy = jnp.where(upper, fy, 1.0 - fy)
                wx = jnp.where(col == kx, 1.0 - fx, jnp.where(col == kx + 1.0, fx, 0.0))
                row = jnp.sum(t * (wy * wx), axis=0, keepdims=True)
                acc = jnp.where(rowid == u, row, acc)
            start = pl.multiple_of(g * UNROLL + h * 8, 8)
            o_ref[pl.ds(start, 8), :] = jnp.sum(acc, axis=1, keepdims=True)
        return carry

    lax.fori_loop(0, chunk // UNROLL, group, 0)


def interpolate_kernel(screen2d, coords):
    rows, cols = screen2d.shape
    nb = cols // 128
    q = coords.shape[1]
    chunk = min(2048, q)
    r = jnp.clip(jnp.floor(coords[0] * (rows - 1)), 0.0, rows - 2.0).astype(jnp.int32)
    pair = jnp.concatenate([screen2d, jnp.roll(screen2d, -1, axis=0)], axis=1)
    pair = pair.reshape(rows, 2 * nb, 128)
    out = pl.pallas_call(
        _interp_kernel,
        grid_spec=pltpu.PrefetchScalarGridSpec(
            num_scalar_prefetch=2,
            grid=(q // chunk,),
            in_specs=[pl.BlockSpec((rows, 2 * nb, 128), lambda i, rr, cc: (0, 0, 0))],
            out_specs=pl.BlockSpec((chunk, 1), lambda i, rr, cc: (i, 0)),
        ),
        out_shape=jax.ShapeDtypeStruct((q, 1), jnp.float32),
    )(r, coords, pair)
    return out[:, 0]


def _balanced_kernel(n_ref, r_ref, c_ref, own_ref, partner_ref, o_ref):
    rows = own_ref.shape[0]
    nb = own_ref.shape[1]
    cols = nb * 128
    senders = n_ref.shape[0] // 2
    seg = o_ref.shape[0] // (2 * senders)
    unroll = min(UNROLL, seg)
    sub = lax.broadcasted_iota(jnp.int32, (nb, 128), 0)
    lane = lax.broadcasted_iota(jnp.int32, (nb, 128), 1)
    col = sub * 128 + lane
    rowid = lax.broadcasted_iota(jnp.int32, (8, 128), 0)

    for h, s_ref in enumerate((own_ref, partner_ref)):
        def segment(s, carry, h=h, s_ref=s_ref):
            def group(g, carry2):
                for part in range(unroll // 8):
                    acc = jnp.zeros((8, 128), jnp.float32)
                    first = (h * senders + s) * seg + g * unroll + part * 8
                    for u in range(8):
                        j = first + u
                        rk = r_ref[j]
                        r = rk >> KBITS
                        k = rk & ((1 << KBITS) - 1)
                        lower = s_ref[r]
                        upper = s_ref[r + 1]
                        fy = c_ref[0, j]
                        fx = c_ref[1, j]
                        blend = (1.0 - fy) * lower + fy * upper
                        wx = jnp.where(col == k, 1.0 - fx, jnp.where(col == k + 1, fx, 0.0))
                        row = jnp.sum(blend * wx, axis=0, keepdims=True)
                        acc = jnp.where(rowid == u, row, acc)
                    o_ref[pl.ds(pl.multiple_of(first, 8), 8), :] = jnp.sum(acc, axis=1, keepdims=True)
                return carry2

            trips = (n_ref[h * senders + s] + unroll - 1) // unroll
            lax.fori_loop(0, trips, group, 0)
            return carry

        lax.fori_loop(0, senders, segment, 0)


def interpolate_balanced(own, partner, coords, live):
    rows, nb, _ = own.shape
    cols = nb * 128
    _, halves, senders, seg = coords.shape
    flat = coords.reshape(2, halves * senders * seg)
    y = flat[0] * (rows - 1)
    x = flat[1] * (cols - 1)
    r = jnp.clip(jnp.floor(y), 0.0, rows - 2.0)
    k = jnp.clip(jnp.floor(x), 0.0, cols - 2.0)
    rk = (r.astype(jnp.int32) << KBITS) | k.astype(jnp.int32)
    frac = jnp.stack([y - r, x - k])
    spec = pl.BlockSpec((rows, nb, 128), lambda i, n, rr, cc: (0, 0, 0))
    out = pl.pallas_call(
        _balanced_kernel,
        grid_spec=pltpu.PrefetchScalarGridSpec(
            num_scalar_prefetch=3,
            grid=(1,),
            in_specs=[spec, spec],
            out_specs=pl.BlockSpec((halves * senders * seg, 1), lambda i, n, rr, cc: (0, 0)),
        ),
        out_shape=jax.ShapeDtypeStruct((halves * senders * seg, 1), jnp.float32),
    )(live, rk, frac, own, partner)
    return out.reshape(halves, senders, seg)


def _scatter_kernel(n_ref, d_ref, v_ref, o_ref):
    rows = n_ref.shape[0]
    width = d_ref.shape[0] // rows
    half = width // 2
    step = 32 if width % 32 == 0 else 2
    for row in range(rows):
        def body(i, carry, row=row):
            for u in range(step):
                slot = row * width + i * step + u
                parity = u % 2
                source = ((row ^ parity) * 2 + parity) * half + i * (step // 2) + u // 2
                o_ref[d_ref[slot]] = v_ref[source]
            return carry

        lax.fori_loop(0, (n_ref[row] + step - 1) // step, body, 0)


def scatter_kernel(dest, vals, size):
    live = jnp.sum((dest < size - 1).astype(jnp.int32), axis=1)
    return pl.pallas_call(
        _scatter_kernel,
        grid_spec=pltpu.PrefetchScalarGridSpec(
            num_scalar_prefetch=3,
            grid=(1,),
            in_specs=[],
            out_specs=pl.BlockSpec((size,), lambda i, n, d, v: (0,), memory_space=pltpu.SMEM),
        ),
        out_shape=jax.ShapeDtypeStruct((size,), jnp.float32),
    )(live, dest.reshape(-1), vals.reshape(-1))


def make_phasors(station_rows, iono_rows, directions, freq_ratio):
    delays = (
        station_rows[:, 0:1] * directions[0][None, :]
        + station_rows[:, 1:2] * directions[1][None, :]
    )
    delays = delays + station_rows[:, 2:3] * directions[2][None, :]
    angles = (TWO_PI * freq_ratio)[None, :, None] * delays[:, None, :] + iono_rows[
        :, None, :
    ] / freq_ratio[None, :, None]
    return jnp.concatenate([jnp.cos(angles), jnp.sin(angles)], axis=-1).astype(jnp.bfloat16)


def spectrum(source_flux, spectral_index, freq_ratio, count):
    return (
        source_flux[None, :]
        * jnp.exp(spectral_index[None, :] * jnp.log(freq_ratio)[:, None])
        / math.sqrt(count)
    )


def weight_rows(phasors, intensity):
    sources = intensity.shape[1]
    real_part = (phasors[:, :, :sources].astype(jnp.float32) * intensity[None]).astype(jnp.bfloat16)
    imag_part = (phasors[:, :, sources:].astype(jnp.float32) * intensity[None]).astype(jnp.bfloat16)
    upper_rows = jnp.concatenate([real_part, imag_part], axis=-1)
    lower_rows = jnp.concatenate([imag_part, -real_part], axis=-1)
    return jnp.concatenate([upper_rows, lower_rows], axis=0)


def body(
    screen,
    pierce_coords,
    query_dest,
    positions,
    directions,
    freq_ratio,
    source_flux,
    spectral_index,
):
    groups = lax.axis_size("stn")
    tile_cols = screen.shape[2]
    strip_rows = screen.shape[0] * screen.shape[1]
    values = screen.reshape(-1)
    capacity = query_dest.shape[3]
    stations_local = positions.shape[1]
    local_sources = source_flux.shape[0] // lax.axis_size("chan")
    queries = stations_local * local_sources
    half = capacity // 2
    coords = pierce_coords.reshape(2, groups, capacity)
    dead = query_dest.reshape(groups, capacity) >= queries
    coords = jnp.where(dead[None], -1.0, coords).reshape(2, groups, half, 2)
    swap = lambda a: a.reshape(a.shape[0], groups // 2, 2, half)[:, :, ::-1, :].reshape(a.shape[0], groups, half)
    send = jnp.stack([coords[..., 0], swap(coords[..., 1])], axis=2)
    received = lax.all_to_all(send, "stn", split_axis=1, concat_axis=1, tiled=True)
    kin = received.transpose(0, 2, 1, 3)
    live = jnp.sum((kin[0] >= 0.0).astype(jnp.int32), axis=2).reshape(-1)
    own = screen.reshape(strip_rows, tile_cols // 128, 128)
    partner = lax.ppermute(own, "stn", [(i, i ^ 1) for i in range(groups)])
    sampled = interpolate_balanced(own, partner, kin, live).transpose(1, 0, 2)
    back = lax.all_to_all(sampled, "stn", split_axis=0, concat_axis=0, tiled=True)
    buffer = scatter_kernel(query_dest.reshape(groups, capacity), back, queries + 1)
    own_iono = buffer[:queries].reshape(stations_local, local_sources)
    station_rows = positions.T
    total_stations = stations_local * groups
    channels = freq_ratio.shape[0]
    n_chan = lax.axis_size("chan")
    if channels % groups:
        return _rows_path(own_iono, station_rows, directions, freq_ratio, source_flux, spectral_index)
    iono_phase = lax.all_gather(own_iono, "chan", axis=1, tiled=True)
    packed = jnp.concatenate([iono_phase, station_rows], axis=1)
    gathered = lax.all_gather(packed, "stn", axis=0, tiled=True)
    all_iono = gathered[:, : n_chan * local_sources]
    all_rows = gathered[:, n_chan * local_sources :]
    per_dev = channels // groups
    my_freq = lax.dynamic_slice_in_dim(freq_ratio, lax.axis_index("stn") * per_dev, per_dev)
    phasors = make_phasors(all_rows, all_iono, directions, my_freq)
    intensity = spectrum(source_flux, spectral_index, my_freq, source_flux.shape[0])
    weighted = weight_rows(phasors, intensity)
    columns = jnp.einsum("ack,nck->can", weighted, phasors, preferred_element_type=jnp.float32)
    visible = columns.reshape(per_dev, 2, total_stations, total_stations)
    ids = jnp.arange(total_stations, dtype=jnp.int32)
    cross_only = ids[:, None] != ids[None, :]
    visible = jnp.where(cross_only[None, None], visible, jnp.zeros_like(visible))
    moved = lax.all_to_all(visible.astype(jnp.bfloat16), "stn", split_axis=2, concat_axis=0, tiled=True)
    return moved.astype(jnp.float32)


def _rows_path(own_iono, station_rows, directions, freq_ratio, source_flux, spectral_index):
    groups = lax.axis_size("stn")
    stations_local = station_rows.shape[0]
    iono_phase = lax.all_gather(own_iono, "chan", axis=1, tiled=True)
    own_phasors = make_phasors(station_rows, iono_phase, directions, freq_ratio)
    intensity = spectrum(source_flux, spectral_index, freq_ratio, source_flux.shape[0])
    weighted = weight_rows(own_phasors, intensity)
    total_stations = stations_local * groups
    channels = freq_ratio.shape[0]
    columns = jnp.einsum(
        "ack,nck->can",
        weighted,
        make_phasors(
            lax.all_gather(station_rows, "stn", axis=0, tiled=True),
            lax.all_gather(iono_phase, "stn", axis=0, tiled=True),
            directions,
            freq_ratio,
        ),
        preferred_element_type=jnp.float32,
    )
    visible = columns.reshape(channels, 2, stations_local, total_stations)
    first_row = lax.axis_index("stn") * stations_local
    rows_global = first_row + jnp.arange(stations_local, dtype=jnp.int32)
    cross_only = rows_global[:, None] != jnp.arange(total_stations, dtype=jnp.int32)[None, :]
    return jnp.where(cross_only[None, None], visible, jnp.zeros_like(visible))


def solution(mesh):
    in_specs = (
        P("stn", None, None),
        P(None, "stn", "chan", None, None),
        P("stn", "chan", None, None),
        P(None, "stn"),
        P(),
        P("chan"),
        P(),
        P(),
    )
    out_specs = P("chan", None, "stn", None)
    return jax.shard_map(body, mesh=mesh, in_specs=in_specs, out_specs=out_specs, check_vma=False)
```
